32 devices in a mesh: gx: 2 (over x), gy: 2 (over y), gz: 8 (over z, core).
Axes of the slice: x: 2, y: 2, z: 4, core: 2. Of those that a mesh axis runs over, the one named last changes fastest.
Arguments:
- edge_coeffs_x: float32 [4, 4, 16, 5, 1280], P('gx', None, 'gy', None, 'gz'), may hold values from -3 to 3
- edge_coeffs_y: float32 [4, 5, 16, 4, 1280], P('gx', None, 'gy', None, 'gz'), may hold values from -3 to 3
- edge_coeffs_z: float32 [4, 5, 16, 5, 1024], P('gx', None, 'gy', None, 'gz'), may hold values from -3 to 3
- flips: int32 [3, 4, 16, 256], P(None, 'gx', 'gy', 'gz'), may hold values from 0 to 1
- flags: int32 [16, 64, 1024], P('gx', 'gy', 'gz'), may hold values 0 or 1
Outputs:
- field_out: float32 [3, 16, 64, 1024], P(None, 'gx', 'gy', 'gz')
The draws below stay inside these ranges and needn't reach their ends.
Inputs may be any that keep to these rules, and one draw needn't show every extreme that they name: `flips`: 1 marks an element whose reference direction of that component is reversed. `flags`: 1 marks a constrained node, whose assembled value is set to zero.
All inputs are finite; a program needn't handle non-finite values. No bound on the sum of `flags` on one device may be relied on, other than what follows from the above.
Results may differ from the reference program's by a relative error of at most 0.000068.
Values sent between devices are 32-bit elements; how exact they have to be, the bound alone decides.
No kernel may reach another device: no remote copies, remote signals or barrier semaphores. Data moves between devices by JAX's collectives and lax.ppermute only.
A program may use at most 64 MiB of HBM per device.

```python
import math
import jax
import jax.numpy as jnp
import numpy as np
from jax import lax

ELEMENTS_X = 4
ELEMENTS_Y = 16
ELEMENTS_Z = 256
NX = 16
NY = 64
NZ = 1024


def set_ends(result, own_key, low, largest):
    extent = result.shape
    spot = [jax.random.randint(jax.random.fold_in(own_key, axis), (), 0, extent[axis]) for axis in range(len(extent))]
    result = result.at[tuple(spot)].set(low)
    longest = extent.index(max(extent))
    spot[longest] = (spot[longest] + 1) % extent[longest]
    return result.at[tuple(spot)].set(largest)


def block_levels(rng, extent, pieces, low, high):
    level = 1.0
    for dim, blocks in pieces:
        heights = jax.random.uniform(jax.random.fold_in(jax.random.fold_in(rng, 6), dim), (blocks,), jnp.float32, low / len(pieces), high / len(pieces))
        level = level * jnp.repeat(jnp.exp(heights), extent[dim] // blocks).reshape((-1,) + (1,) * (len(extent) - 1 - dim))
    return level


def bell_draw(key, dims, width, most, cuts=(), held_as=jnp.bfloat16):
    entries = jax.random.normal(key, dims, jnp.float32) * width
    if len(cuts) > 0:
        entries = block_levels(key, dims, cuts, -0.22, 0.18) * entries
    return jnp.clip(entries, min=-most, max=most).astype(held_as)


def setup_inputs(seed: int = 0) -> dict:
    key_list = jax.random.split(jax.random.key(seed), 6)
    edge_coeffs_x = bell_draw(key_list[0], (ELEMENTS_X, 4, ELEMENTS_Y, 5, 5 * ELEMENTS_Z), 0.5, 3.0, ((0, 2), (2, 2), (4, 8)), jnp.float32)
    edge_coeffs_y = bell_draw(key_list[1], (ELEMENTS_X, 5, ELEMENTS_Y, 4, 5 * ELEMENTS_Z), 0.5, 3.0, ((0, 2), (2, 2), (4, 8)), jnp.float32)
    edge_coeffs_z = bell_draw(key_list[2], (ELEMENTS_X, 5, ELEMENTS_Y, 5, 4 * ELEMENTS_Z), 0.5, 3.0, ((0, 2), (2, 2), (4, 8)), jnp.float32)
    flips = set_ends(jax.random.randint(key_list[3], (3, ELEMENTS_X, ELEMENTS_Y, ELEMENTS_Z), 0, 2), jax.random.fold_in(key_list[3], 1), 0, 1).astype(jnp.int32)
    flags = set_ends((jax.random.randint(key_list[4], (NX, NY, NZ), 0, 8) < 1).astype(jnp.int32), jax.random.fold_in(key_list[4], 1), 0, 1)
    return dict(edge_coeffs_x=edge_coeffs_x, edge_coeffs_y=edge_coeffs_y, edge_coeffs_z=edge_coeffs_z, flips=flips, flags=flags)


def lagrange_table(points, targets):
    table = np.ones((len(targets), len(points)))
    for row_pos in range(len(targets)):
        for col_pos in range(len(points)):
            for other in range(len(points)):
                if other != col_pos:
                    table[row_pos, col_pos] *= (targets[row_pos] - points[other]) / (points[col_pos] - points[other])
    return table

def basis_tables():
    spread = math.sqrt(3.0 / 7.0)
    targets = [0.0, (1.0 - spread) / 2.0, 0.5, (1.0 + spread) / 2.0, 1.0]
    closed = [0.0, 0.25, 0.5, 0.75, 1.0]
    inner = math.sqrt(3.0 / 7.0 - 2.0 / 7.0 * math.sqrt(6.0 / 5.0))
    outer = math.sqrt(3.0 / 7.0 + 2.0 / 7.0 * math.sqrt(6.0 / 5.0))
    gauss = [(1.0 - outer) / 2.0, (1.0 - inner) / 2.0, (1.0 + inner) / 2.0, (1.0 + outer) / 2.0]
    closed_map = jnp.asarray(lagrange_table(closed, targets), dtype=jnp.float32)
    open_map = jnp.asarray(lagrange_table(gauss, targets), dtype=jnp.float32)
    return (closed_map, open_map)

def interpolate(coef, flip, map_x, map_y, map_z):
    ex_count, size_x, ey_count, size_y, merged = coef.shape
    size_z = map_z.shape[1]
    blocks = coef.reshape(ex_count, size_x, ey_count, size_y, merged // size_z, size_z)
    precise = lax.Precision.HIGHEST
    partial_value = jnp.einsum('ai,xiyjzk->xayjzk', map_x, blocks, precision=precise)
    partial_value = jnp.einsum('bj,xayjzk->xaybzk', map_y, partial_value, precision=precise)
    partial_value = jnp.einsum('ck,xaybzk->xaybzc', map_z, partial_value, precision=precise)
    orient = (1 - 2 * flip).astype(jnp.float32)
    return partial_value * orient[:, None, :, None, :, None]

def merge_pair(array, axis_pos):
    shape_list = array.shape
    return array.reshape(shape_list[:axis_pos] + (shape_list[axis_pos] * shape_list[axis_pos + 1],) + shape_list[axis_pos + 2:])

def assemble_dim(nodal, axis_pos):
    leading = merge_pair(lax.slice_in_dim(nodal, 0, 4, axis=axis_pos + 1), axis_pos)
    upper = lax.slice_in_dim(nodal, 4, 5, axis=axis_pos + 1)
    zero_shape = list(upper.shape)
    zero_shape[axis_pos + 1] = 3
    trailing = merge_pair(jnp.concatenate([jnp.zeros(tuple(zero_shape), nodal.dtype), upper], axis=axis_pos + 1), axis_pos)
    right_pad = [(0, 0)] * leading.ndim
    right_pad[axis_pos] = (0, 1)
    left_pad = [(0, 0)] * leading.ndim
    left_pad[axis_pos] = (1, 0)
    return jnp.pad(leading, right_pad) + jnp.pad(trailing, left_pad)

def assemble_all(nodal, first):
    summed = nodal
    for step_pos in range(3):
        summed = assemble_dim(summed, first + step_pos)
    return summed

def folded_dimension(extended, axis_pos):
    length = extended.shape[axis_pos]
    first_plane = lax.slice_in_dim(extended, 0, 1, axis=axis_pos) + lax.slice_in_dim(extended, length - 1, length, axis=axis_pos)
    return jnp.concatenate([first_plane, lax.slice_in_dim(extended, 1, length - 1, axis=axis_pos)], axis=axis_pos)

def stencil_roll(masked):
    total = 8.0 * masked
    for axis_pos in range(3):
        near = jnp.roll(masked, 1, axis_pos) + jnp.roll(masked, -1, axis_pos)
        far = jnp.roll(masked, 2, axis_pos) + jnp.roll(masked, -2, axis_pos)
        total = total - 4.0 / 3.0 * near + 1.0 / 12.0 * far
    return 0.25 * total

def reference(edge_coeffs_x, edge_coeffs_y, edge_coeffs_z, flips, flags):
    closed_map, open_map = basis_tables()
    keep = (1 - flags).astype(jnp.float32)
    nodal_x = interpolate(edge_coeffs_x, flips[0], open_map, closed_map, closed_map)
    nodal_y = interpolate(edge_coeffs_y, flips[1], closed_map, open_map, closed_map)
    nodal_z = interpolate(edge_coeffs_z, flips[2], closed_map, closed_map, open_map)
    results = []
    for nodal in (nodal_x, nodal_y, nodal_z):
        summed = assemble_all(nodal, 0)
        for axis_pos in range(3):
            summed = folded_dimension(summed, axis_pos)
        results.append(stencil_roll(summed * keep))
    return jnp.stack(results)
```

```python
import math

import jax
import jax.numpy as jnp
import numpy as np
from jax import lax
from jax.sharding import PartitionSpec as P


def lagrange_table(points, targets):
    table = np.ones((len(targets), len(points)))
    for row_pos in range(len(targets)):
        for col_pos in range(len(points)):
            for other in range(len(points)):
                if other != col_pos:
                    table[row_pos, col_pos] *= (targets[row_pos] - points[other]) / (
                        points[col_pos] - points[other]
                    )
    return table


def basis_tables():
    spread = math.sqrt(3.0 / 7.0)
    targets = [0.0, (1.0 - spread) / 2.0, 0.5, (1.0 + spread) / 2.0, 1.0]
    closed = [0.0, 0.25, 0.5, 0.75, 1.0]
    inner = math.sqrt(3.0 / 7.0 - 2.0 / 7.0 * math.sqrt(6.0 / 5.0))
    outer = math.sqrt(3.0 / 7.0 + 2.0 / 7.0 * math.sqrt(6.0 / 5.0))
    gauss = [(1.0 - outer) / 2.0, (1.0 - inner) / 2.0, (1.0 + inner) / 2.0, (1.0 + outer) / 2.0]
    closed_map = np.asarray(lagrange_table(closed, targets), dtype=np.float32).astype(np.float64)
    open_map = np.asarray(lagrange_table(gauss, targets), dtype=np.float32).astype(np.float64)
    return closed_map, open_map


def assembly_matrix(table, count):
    size = table.shape[1]
    matrix = np.zeros((4 * count + 1, count * size))
    for elem_pos in range(count):
        matrix[4 * elem_pos : 4 * elem_pos + 5, size * elem_pos : size * elem_pos + size] += table
    return matrix


def interpolate(coef, flip, table_x, table_y, table_z):
    ex_count, size_x, ey_count, size_y, merged = coef.shape
    size_z = table_z.shape[1]
    ez_count = merged // size_z
    precise = lax.Precision.HIGHEST
    orient = jnp.repeat((1 - 2 * flip).astype(jnp.float32), size_z, axis=2)
    signed = (coef * orient[:, None, :, None, :]).reshape(ex_count * size_x * ey_count * size_y, merged)
    plane_map = np.kron(assembly_matrix(table_x, ex_count), assembly_matrix(table_y, ey_count))
    depth_map = assembly_matrix(table_z, ez_count)
    deep = jnp.dot(signed, jnp.asarray(depth_map.T, jnp.float32), precision=precise)
    nodal = jnp.dot(jnp.asarray(plane_map, jnp.float32), deep, precision=precise)
    return nodal.reshape(4 * ex_count + 1, 4 * ey_count + 1, 4 * ez_count + 1)


def from_neighbours(up, down, axis, dim):
    count = lax.axis_size(axis)
    if count == 1:
        return up, down
    if count == 2:
        both = lax.ppermute(jnp.concatenate([up, down], axis=dim), axis, [(0, 1), (1, 0)])
        rows = up.shape[dim]
        return (
            lax.slice_in_dim(both, 0, rows, axis=dim),
            lax.slice_in_dim(both, rows, both.shape[dim], axis=dim),
        )
    from_prev = lax.ppermute(up, axis, [(i, (i + 1) % count) for i in range(count)])
    from_next = lax.ppermute(down, axis, [(i, (i - 1) % count) for i in range(count)])
    return from_prev, from_next


def fold_and_halo(partial, axis, dim):
    n = partial.shape[dim] - 1
    up = lax.slice_in_dim(partial, n - 2, n + 1, axis=dim)
    down = lax.slice_in_dim(partial, 0, 2, axis=dim)
    from_prev, from_next = from_neighbours(up, down, axis, dim)
    return jnp.concatenate(
        [
            lax.slice_in_dim(from_prev, 0, 2, axis=dim),
            lax.slice_in_dim(partial, 0, 1, axis=dim) + lax.slice_in_dim(from_prev, 2, 3, axis=dim),
            lax.slice_in_dim(partial, 1, n, axis=dim),
            lax.slice_in_dim(partial, n, n + 1, axis=dim) + lax.slice_in_dim(from_next, 0, 1, axis=dim),
            lax.slice_in_dim(from_next, 1, 2, axis=dim),
        ],
        axis=dim,
    )


def halo(cells, axis, dim):
    n = cells.shape[dim]
    up = lax.slice_in_dim(cells, n - 2, n, axis=dim)
    down = lax.slice_in_dim(cells, 0, 2, axis=dim)
    from_prev, from_next = from_neighbours(up, down, axis, dim)
    return jnp.concatenate([from_prev, cells, from_next], axis=dim)


def window(padded_array, axis_pos, offset):
    starts = [0, 2, 2, 2]
    limits = [
        padded_array.shape[0],
        padded_array.shape[1] - 2,
        padded_array.shape[2] - 2,
        padded_array.shape[3] - 2,
    ]
    starts[axis_pos] = offset
    limits[axis_pos] = offset + padded_array.shape[axis_pos] - 4
    return lax.slice(padded_array, tuple(starts), tuple(limits))


def stencil_apply(padded_array):
    total = 8.0 * window(padded_array, 1, 2)
    for axis_pos in (1, 2, 3):
        near = window(padded_array, axis_pos, 1) + window(padded_array, axis_pos, 3)
        far = window(padded_array, axis_pos, 0) + window(padded_array, axis_pos, 4)
        total = total - 4.0 / 3.0 * near + 1.0 / 12.0 * far
    return 0.25 * total


def body(edge_coeffs_x, edge_coeffs_y, edge_coeffs_z, flips, flags):
    closed_map, open_map = basis_tables()
    keep = (1 - flags).astype(jnp.float32)
    for axis, dim in (("gz", 2), ("gy", 1), ("gx", 0)):
        keep = halo(keep, axis, dim)
    nodal_x = interpolate(edge_coeffs_x, flips[0], open_map, closed_map, closed_map)
    nodal_y = interpolate(edge_coeffs_y, flips[1], closed_map, open_map, closed_map)
    nodal_z = interpolate(edge_coeffs_z, flips[2], closed_map, closed_map, open_map)
    extended = jnp.stack([nodal_x, nodal_y, nodal_z])
    for axis, dim in (("gz", 3), ("gy", 2), ("gx", 1)):
        extended = fold_and_halo(extended, axis, dim)
    return stencil_apply(extended * keep[None])


def solution(mesh):
    in_specs = (
        P("gx", None, "gy", None, "gz"),
        P("gx", None, "gy", None, "gz"),
        P("gx", None, "gy", None, "gz"),
        P(None, "gx", "gy", "gz"),
        P("gx", "gy", "gz"),
    )
    out_specs = P(None, "gx", "gy", "gz")
    return jax.shard_map(body, mesh=mesh, in_specs=in_specs, out_specs=out_specs, check_vma=False)
```

```python
import math

import jax
import jax.numpy as jnp
import numpy as np
from jax import lax
from jax.sharding import PartitionSpec as P


def lagrange_table(points, targets):
    table = np.ones((len(targets), len(points)))
    for row_pos in range(len(targets)):
        for col_pos in range(len(points)):
            for other in range(len(points)):
                if other != col_pos:
                    table[row_pos, col_pos] *= (targets[row_pos] - points[other]) / (
                        points[col_pos] - points[other]
                    )
    return table


def basis_tables():
    spread = math.sqrt(3.0 / 7.0)
    targets = [0.0, (1.0 - spread) / 2.0, 0.5, (1.0 + spread) / 2.0, 1.0]
    closed = [0.0, 0.25, 0.5, 0.75, 1.0]
    inner = math.sqrt(3.0 / 7.0 - 2.0 / 7.0 * math.sqrt(6.0 / 5.0))
    outer = math.sqrt(3.0 / 7.0 + 2.0 / 7.0 * math.sqrt(6.0 / 5.0))
    gauss = [(1.0 - outer) / 2.0, (1.0 - inner) / 2.0, (1.0 + inner) / 2.0, (1.0 + outer) / 2.0]
    closed_map = np.asarray(lagrange_table(closed, targets), dtype=np.float32).astype(np.float64)
    open_map = np.asarray(lagrange_table(gauss, targets), dtype=np.float32).astype(np.float64)
    return closed_map, open_map


def assembly_matrix(table, count):
    size = table.shape[1]
    matrix = np.zeros((4 * count + 1, count * size))
    for elem_pos in range(count):
        matrix[4 * elem_pos : 4 * elem_pos + 5, size * elem_pos : size * elem_pos + size] += table
    return matrix


def interpolate(coef, flip, table_x, table_y, table_z):
    ex_count, size_x, ey_count, size_y, merged = coef.shape
    size_z = table_z.shape[1]
    ez_count = merged // size_z
    nx, ny, nz = 4 * ex_count, 4 * ey_count, 4 * ez_count
    precise = lax.Precision.HIGHEST
    orient = jnp.repeat((1 - 2 * flip).astype(jnp.float32), size_z, axis=2)
    signed = (coef * orient[:, None, :, None, :]).reshape(ex_count * size_x * ey_count * size_y, merged)
    plane_map = np.kron(assembly_matrix(table_x, ex_count), assembly_matrix(table_y, ey_count))
    plane_map = plane_map.reshape(nx + 1, ny + 1, -1)
    plane_map = np.concatenate(
        [
            plane_map[:nx, :ny].reshape(nx * ny, -1),
            plane_map[nx, :ny],
            plane_map[:nx, ny],
            plane_map[nx, ny][None],
        ]
    )
    depth_map = assembly_matrix(table_z, ez_count)
    planar = jnp.dot(jnp.asarray(plane_map, jnp.float32), signed, precision=precise)
    body_part = jnp.dot(planar, jnp.asarray(depth_map[:nz].T, jnp.float32), precision=precise)
    top_part = jnp.dot(planar, jnp.asarray(depth_map[nz], jnp.float32), precision=precise)
    return body_part, top_part


def shifted(block, axes, step=1):
    sizes = [lax.axis_size(axis) for axis in axes]
    pairs = []
    for source in np.ndindex(*sizes):
        target = tuple((c + step) % s for c, s in zip(source, sizes))
        pairs.append((int(np.ravel_multi_index(source, sizes)), int(np.ravel_multi_index(target, sizes))))
    if all(a == b for a, b in pairs):
        return block
    return lax.ppermute(block, tuple(axes) if len(axes) > 1 else axes[0], pairs)


def both_ways(up, down, axis):
    count = lax.axis_size(axis)
    if count <= 2:
        both = shifted(jnp.stack([up, down]), [axis])
        return both[0], both[1]
    return shifted(up, [axis]), shifted(down, [axis], -1)


def body(edge_coeffs_x, edge_coeffs_y, edge_coeffs_z, flips, flags):
    closed_map, open_map = basis_tables()
    nx, ny, nz = flags.shape
    parts = [
        interpolate(edge_coeffs_x, flips[0], open_map, closed_map, closed_map),
        interpolate(edge_coeffs_y, flips[1], closed_map, open_map, closed_map),
        interpolate(edge_coeffs_z, flips[2], closed_map, closed_map, open_map),
    ]
    rows = jnp.stack([part[0] for part in parts])
    tops = jnp.stack([part[1] for part in parts])
    own = nx * ny
    main = rows[:, :own].reshape(3, nx, ny, nz)
    x_top = rows[:, own : own + ny]
    y_top = rows[:, own + ny : own + ny + nx]
    xy_top = rows[:, own + ny + nx]
    z_top = tops[:, :own].reshape(3, nx, ny)
    xz_top = tops[:, own : own + ny]
    yz_top = tops[:, own + ny : own + ny + nx]
    xyz_top = tops[:, own + ny + nx]

    x_in = shifted(x_top, ["gx"])
    y_in = shifted(y_top, ["gy"])
    z_in = shifted(z_top, ["gz"])
    xy_in = shifted(xy_top, ["gx", "gy"])
    xz_in = shifted(xz_top, ["gx", "gz"])
    yz_in = shifted(yz_top, ["gy", "gz"])
    xyz_in = shifted(xyz_top, ["gx", "gy", "gz"])

    main = main.at[:, 0].add(x_in)
    main = main.at[:, :, 0].add(y_in)
    main = main.at[:, :, :, 0].add(z_in)
    main = main.at[:, 0, 0].add(xy_in)
    main = main.at[:, 0, :, 0].add(xz_in)
    main = main.at[:, :, 0, 0].add(yz_in)
    main = main.at[:, 0, 0, 0].add(xyz_in)

    masked = main * (1 - flags).astype(jnp.float32)[None]

    lo_x, hi_x = both_ways(masked[:, nx - 2 :], masked[:, :2], "gx")
    up_y = jnp.swapaxes(masked[:, :, ny - 2 :], 1, 2)
    down_y = jnp.swapaxes(masked[:, :, :2], 1, 2)
    lo_y, hi_y = both_ways(up_y, down_y, "gy")
    lo_y, hi_y = jnp.swapaxes(lo_y, 1, 2), jnp.swapaxes(hi_y, 1, 2)
    up_z = jnp.moveaxis(masked[..., nz - 2 :], 3, 1).reshape(3, 2, nx * ny)
    down_z = jnp.moveaxis(masked[..., :2], 3, 1).reshape(3, 2, nx * ny)
    lo_z, hi_z = both_ways(up_z, down_z, "gz")
    lo_z = jnp.moveaxis(lo_z.reshape(3, 2, nx, ny), 1, 3)
    hi_z = jnp.moveaxis(hi_z.reshape(3, 2, nx, ny), 1, 3)

    total = 8.0 * masked
    for lo, hi, dim in ((lo_x, hi_x, 1), (lo_y, hi_y, 2), (lo_z, hi_z, 3)):
        padded = jnp.concatenate([lo, masked, hi], axis=dim)
        length = masked.shape[dim]
        near = lax.slice_in_dim(padded, 1, 1 + length, axis=dim) + lax.slice_in_dim(
            padded, 3, 3 + length, axis=dim
        )
        far = lax.slice_in_dim(padded, 0, length, axis=dim) + lax.slice_in_dim(
            padded, 4, 4 + length, axis=dim
        )
        total = total - 4.0 / 3.0 * near + 1.0 / 12.0 * far
    return 0.25 * total


def solution(mesh):
    in_specs = (
        P("gx", None, "gy", None, "gz"),
        P("gx", None, "gy", None, "gz"),
        P("gx", None, "gy", None, "gz"),
        P(None, "gx", "gy", "gz"),
        P("gx", "gy", "gz"),
    )
    out_specs = P(None, "gx", "gy", "gz")
    return jax.shard_map(body, mesh=mesh, in_specs=in_specs, out_specs=out_specs, check_vma=False)
```

```python
import math

import jax
import jax.numpy as jnp
import numpy as np
from jax import lax
from jax.sharding import PartitionSpec as P


def lagrange_table(points, targets):
    table = np.ones((len(targets), len(points)))
    for row_pos in range(len(targets)):
        for col_pos in range(len(points)):
            for other in range(len(points)):
                if other != col_pos:
                    table[row_pos, col_pos] *= (targets[row_pos] - points[other]) / (
                        points[col_pos] - points[other]
                    )
    return table


def basis_tables():
    spread = math.sqrt(3.0 / 7.0)
    targets = [0.0, (1.0 - spread) / 2.0, 0.5, (1.0 + spread) / 2.0, 1.0]
    closed = [0.0, 0.25, 0.5, 0.75, 1.0]
    inner = math.sqrt(3.0 / 7.0 - 2.0 / 7.0 * math.sqrt(6.0 / 5.0))
    outer = math.sqrt(3.0 / 7.0 + 2.0 / 7.0 * math.sqrt(6.0 / 5.0))
    gauss = [(1.0 - outer) / 2.0, (1.0 - inner) / 2.0, (1.0 + inner) / 2.0, (1.0 + outer) / 2.0]
    closed_map = np.asarray(lagrange_table(closed, targets), dtype=np.float32).astype(np.float64)
    open_map = np.asarray(lagrange_table(gauss, targets), dtype=np.float32).astype(np.float64)
    return closed_map, open_map


def assembly_matrix(table, count):
    size = table.shape[1]
    matrix = np.zeros((4 * count + 1, count * size))
    for elem_pos in range(count):
        matrix[4 * elem_pos : 4 * elem_pos + 5, size * elem_pos : size * elem_pos + size] += table
    return matrix


def interpolate(coef, flip, table_x, table_y, table_z):
    ex_count, size_x, ey_count, size_y, merged = coef.shape
    size_z = table_z.shape[1]
    ez_count = merged // size_z
    precise = lax.Precision.HIGHEST
    orient = jnp.repeat((1 - 2 * flip).astype(jnp.float32), size_z, axis=2)
    signed = (coef * orient[:, None, :, None, :]).reshape(ex_count * size_x * ey_count * size_y, merged)
    plane_map = np.kron(assembly_matrix(table_x, ex_count), assembly_matrix(table_y, ey_count))
    depth_map = assembly_matrix(table_z, ez_count)
    deep = jnp.dot(signed, jnp.asarray(depth_map.T, jnp.float32), precision=precise)
    nodal = jnp.dot(jnp.asarray(plane_map, jnp.float32), deep, precision=precise)
    return nodal.reshape(4 * ex_count + 1, 4 * ey_count + 1, 4 * ez_count + 1)


def shifted(block, axis, step=1):
    count = lax.axis_size(axis)
    if count == 1:
        return block
    return lax.ppermute(block, axis, [(i, (i + step) % count) for i in range(count)])


def both_ways(up, down, axis):
    if lax.axis_size(axis) <= 2:
        both = shifted(jnp.concatenate([up, down]), axis)
        return both[: up.shape[0]], both[up.shape[0] :]
    return shifted(up, axis), shifted(down, axis, -1)


def to_wire(slab, dim):
    layers = jnp.moveaxis(slab, dim, 0)
    return layers.reshape(layers.shape[0] * layers.shape[1], -1), layers.shape


def from_wire(rows, shape, dim):
    return jnp.moveaxis(rows.reshape(shape), 0, dim)


def fold_and_halo(partial, axis, dim):
    n = partial.shape[dim] - 1
    up, up_shape = to_wire(lax.slice_in_dim(partial, n - 2, n + 1, axis=dim), dim)
    down, down_shape = to_wire(lax.slice_in_dim(partial, 0, 2, axis=dim), dim)
    from_prev, from_next = both_ways(up, down, axis)
    from_prev = from_wire(from_prev, up_shape, dim)
    from_next = from_wire(from_next, down_shape, dim)
    return jnp.concatenate(
        [
            lax.slice_in_dim(from_prev, 0, 2, axis=dim),
            lax.slice_in_dim(partial, 0, 1, axis=dim) + lax.slice_in_dim(from_prev, 2, 3, axis=dim),
            lax.slice_in_dim(partial, 1, n, axis=dim),
            lax.slice_in_dim(partial, n, n + 1, axis=dim) + lax.slice_in_dim(from_next, 0, 1, axis=dim),
            lax.slice_in_dim(from_next, 1, 2, axis=dim),
        ],
        axis=dim,
    )


def cross_rows(plane, ny, nz):
    own = plane[:, 2 : ny + 2, 2 : nz + 2]
    strips_y = jnp.concatenate([plane[:, 0:2, 2 : nz + 2], plane[:, ny + 2 :, 2 : nz + 2]], axis=1)
    strips_z = jnp.concatenate([plane[:, 2 : ny + 2, 0:2], plane[:, 2 : ny + 2, nz + 2 :]], axis=2)
    strips_z = jnp.swapaxes(strips_z, 1, 2).reshape(-1)
    strips_z = jnp.pad(strips_z, (0, -strips_z.shape[0] % nz))
    return [own.reshape(-1, nz), strips_y.reshape(-1, nz), strips_z.reshape(-1, nz)]


def cross_plane(own, strips_y, strips_z):
    middle = jnp.concatenate([strips_z[..., 0:2], own, strips_z[..., 2:4]], axis=2)
    widths = ((0, 0), (0, 0), (2, 2))
    return jnp.concatenate(
        [jnp.pad(strips_y[:, 0:2], widths), middle, jnp.pad(strips_y[:, 2:4], widths)], axis=1
    )


def fold_and_halo_last(extended, axis, ny, nz):
    n = extended.shape[1] - 1
    comps = extended.shape[0] - 1
    data = extended[:comps]
    keep = extended[comps]

    def own(block):
        return block[..., 2 : ny + 2, 2 : nz + 2]

    halo_up = own(data[:, n - 2 : n] * keep[n - 2 : n])
    halo_down = own(data[:, 1] * keep[1])
    up_parts = [halo_up.reshape(-1, nz)] + cross_rows(data[:, n], ny, nz)
    down_parts = [own(data[:, 0]).reshape(-1, nz), own(keep[0]), halo_down.reshape(-1, nz)]
    up = jnp.concatenate(up_parts)
    down = jnp.concatenate(down_parts)
    from_prev, from_next = both_ways(up, down, axis)

    sizes = [part.shape[0] for part in up_parts]
    marks = np.cumsum([0] + sizes)
    prev_halo = from_prev[marks[0] : marks[1]].reshape(comps, 2, ny, nz)
    prev_own = from_prev[marks[1] : marks[2]].reshape(comps, ny, nz)
    prev_strips_y = from_prev[marks[2] : marks[3]].reshape(comps, 4, nz)
    prev_strips_z = from_prev[marks[3] : marks[4]].reshape(-1)[: comps * 4 * ny]
    prev_strips_z = jnp.swapaxes(prev_strips_z.reshape(comps, 4, ny), 1, 2)
    fold_in = cross_plane(prev_own, prev_strips_y, prev_strips_z)

    plane_rows = comps * ny
    next_fold = from_next[:plane_rows].reshape(comps, ny, nz)
    next_keep = from_next[plane_rows : plane_rows + ny]
    next_halo = from_next[plane_rows + ny :].reshape(comps, ny, nz)

    widths = ((0, 0), (0, 0), (2, 2), (2, 2))
    first = (data[:, 0] + fold_in) * keep[0]
    last = (own(data[:, n]) + next_fold) * next_keep
    return jnp.concatenate(
        [
            jnp.pad(prev_halo, widths),
            first[:, None],
            data[:, 1:n] * keep[1:n],
            jnp.pad(last[:, None], widths),
            jnp.pad(next_halo[:, None], widths),
        ],
        axis=1,
    )


def window(padded_array, axis_pos, offset):
    starts = [0, 2, 2, 2]
    limits = [
        padded_array.shape[0],
        padded_array.shape[1] - 2,
        padded_array.shape[2] - 2,
        padded_array.shape[3] - 2,
    ]
    starts[axis_pos] = offset
    limits[axis_pos] = offset + padded_array.shape[axis_pos] - 4
    return lax.slice(padded_array, tuple(starts), tuple(limits))


def stencil_apply(padded_array):
    total = 8.0 * window(padded_array, 1, 2)
    for axis_pos in (1, 2, 3):
        near = window(padded_array, axis_pos, 1) + window(padded_array, axis_pos, 3)
        far = window(padded_array, axis_pos, 0) + window(padded_array, axis_pos, 4)
        total = total - 4.0 / 3.0 * near + 1.0 / 12.0 * far
    return 0.25 * total


def body(edge_coeffs_x, edge_coeffs_y, edge_coeffs_z, flips, flags):
    closed_map, open_map = basis_tables()
    nx, ny, nz = flags.shape
    nodal_x = interpolate(edge_coeffs_x, flips[0], open_map, closed_map, closed_map)
    nodal_y = interpolate(edge_coeffs_y, flips[1], closed_map, open_map, closed_map)
    nodal_z = interpolate(edge_coeffs_z, flips[2], closed_map, closed_map, open_map)
    keep = jnp.pad((1 - flags).astype(jnp.float32), ((0, 1), (0, 1), (0, 1)))
    extended = jnp.stack([nodal_x, nodal_y, nodal_z, keep])
    extended = fold_and_halo(extended, "gz", 3)
    extended = fold_and_halo(extended, "gy", 2)
    masked = fold_and_halo_last(extended, "gx", ny, nz)
    return stencil_apply(masked)


def solution(mesh):
    in_specs = (
        P("gx", None, "gy", None, "gz"),
        P("gx", None, "gy", None, "gz"),
        P("gx", None, "gy", None, "gz"),
        P(None, "gx", "gy", "gz"),
        P("gx", "gy", "gz"),
    )
    out_specs = P(None, "gx", "gy", "gz")
    return jax.shard_map(body, mesh=mesh, in_specs=in_specs, out_specs=out_specs, check_vma=False)
```

```python
import math

import jax
import jax.numpy as jnp
import numpy as np
from jax import lax
from jax.sharding import PartitionSpec as P


def lagrange_table(points, targets):
    table = np.ones((len(targets), len(points)))
    for row_pos in range(len(targets)):
        for col_pos in range(len(points)):
            for other in range(len(points)):
                if other != col_pos:
                    table[row_pos, col_pos] *= (targets[row_pos] - points[other]) / (
                        points[col_pos] - points[other]
                    )
    return table


def basis_tables():
    spread = math.sqrt(3.0 / 7.0)
    targets = [0.0, (1.0 - spread) / 2.0, 0.5, (1.0 + spread) / 2.0, 1.0]
    closed = [0.0, 0.25, 0.5, 0.75, 1.0]
    inner = math.sqrt(3.0 / 7.0 - 2.0 / 7.0 * math.sqrt(6.0 / 5.0))
    outer = math.sqrt(3.0 / 7.0 + 2.0 / 7.0 * math.sqrt(6.0 / 5.0))
    gauss = [(1.0 - outer) / 2.0, (1.0 - inner) / 2.0, (1.0 + inner) / 2.0, (1.0 + outer) / 2.0]
    closed_map = np.asarray(lagrange_table(closed, targets), dtype=np.float32).astype(np.float64)
    open_map = np.asarray(lagrange_table(gauss, targets), dtype=np.float32).astype(np.float64)
    return closed_map, open_map


def assembly_matrix(table, count):
    size = table.shape[1]
    matrix = np.zeros((4 * count + 1, count * size))
    for elem_pos in range(count):
        matrix[4 * elem_pos : 4 * elem_pos + 5, size * elem_pos : size * elem_pos + size] += table
    return matrix


def interpolate(coef, flip, table_x, table_y, table_z):
    ex_count, size_x, ey_count, size_y, merged = coef.shape
    size_z = table_z.shape[1]
    ez_count = merged // size_z
    precise = lax.Precision.HIGHEST
    orient = jnp.repeat((1 - 2 * flip).astype(jnp.float32), size_z, axis=2)
    signed = (coef * orient[:, None, :, None, :]).reshape(ex_count * size_x * ey_count * size_y, merged)
    rows_y = np.pad(assembly_matrix(table_y, ey_count), ((2, 1), (0, 0)))
    plane_map = np.kron(assembly_matrix(table_x, ex_count), rows_y)
    depth_map = np.pad(assembly_matrix(table_z, ez_count), ((2, 1), (0, 0)))
    deep = jnp.dot(signed, jnp.asarray(depth_map.T, jnp.float32), precision=precise)
    nodal = jnp.dot(jnp.asarray(plane_map, jnp.float32), deep, precision=precise)
    return nodal.reshape(4 * ex_count + 1, 4 * ey_count + 4, 4 * ez_count + 4)


def shifted(block, axis, step=1):
    count = lax.axis_size(axis)
    if count == 1:
        return block
    return lax.ppermute(block, axis, [(i, (i + step) % count) for i in range(count)])


def both_ways(up, down, axis):
    if lax.axis_size(axis) <= 2:
        both = shifted(jnp.concatenate([up, down]), axis)
        return both[: up.shape[0]], both[up.shape[0] :]
    return shifted(up, axis), shifted(down, axis, -1)


def to_wire(slab, dim):
    layers = jnp.moveaxis(slab, dim, 0)
    return layers.reshape(layers.shape[0] * layers.shape[1], -1), layers.shape


def from_wire(rows, shape, dim):
    return jnp.moveaxis(rows.reshape(shape), 0, dim)


def fold_and_halo(extended, axis, dim):
    length = extended.shape[dim]
    n = length - 4
    up, up_shape = to_wire(lax.slice_in_dim(extended, n, n + 3, axis=dim), dim)
    down, down_shape = to_wire(lax.slice_in_dim(extended, 2, 4, axis=dim), dim)
    from_prev, from_next = both_ways(up, down, axis)
    widths_prev = [(0, 0)] * extended.ndim
    widths_prev[dim] = (0, length - 3)
    widths_next = [(0, 0)] * extended.ndim
    widths_next[dim] = (n + 2, 0)
    return (
        extended
        + jnp.pad(from_wire(from_prev, up_shape, dim), widths_prev)
        + jnp.pad(from_wire(from_next, down_shape, dim), widths_next)
    )


def pack(parts, width):
    flat = jnp.concatenate([part.reshape(-1) for part in parts])
    flat = jnp.pad(flat, (0, -flat.shape[0] % width))
    return flat.reshape(-1, width)


def unpack(rows, shapes):
    flat = rows.reshape(-1)
    parts = []
    start = 0
    for shape in shapes:
        size = int(np.prod(shape))
        parts.append(flat[start : start + size].reshape(shape))
        start += size
    return parts


def patch(block, row, col):
    at_row = lax.broadcasted_iota(jnp.int32, block.shape, block.ndim - 2) == 0
    at_col = lax.broadcasted_iota(jnp.int32, block.shape, block.ndim - 1) == 0
    return jnp.where(at_col, col[..., None], jnp.where(at_row, row[..., None, :], block))


def cross_plane(own, strips_y, strips_z):
    middle = jnp.concatenate([strips_z[..., 0:2], own, strips_z[..., 2:4]], axis=2)
    widths = ((0, 0), (0, 0), (2, 2))
    return jnp.concatenate(
        [jnp.pad(strips_y[:, 0:2], widths), middle, jnp.pad(strips_y[:, 2:4], widths)], axis=1
    )


def window(padded_array, axis_pos, offset):
    starts = [0, 2, 2, 2]
    limits = [
        padded_array.shape[0],
        padded_array.shape[1] - 2,
        padded_array.shape[2] - 2,
        padded_array.shape[3] - 2,
    ]
    starts[axis_pos] = offset
    limits[axis_pos] = offset + padded_array.shape[axis_pos] - 4
    return lax.slice(padded_array, tuple(starts), tuple(limits))


def stencil_apply(padded_array):
    total = 8.0 * window(padded_array, 1, 2)
    for axis_pos in (1, 2, 3):
        near = window(padded_array, axis_pos, 1) + window(padded_array, axis_pos, 3)
        far = window(padded_array, axis_pos, 0) + window(padded_array, axis_pos, 4)
        total = total - 4.0 / 3.0 * near + 1.0 / 12.0 * far
    return 0.25 * total


def body(edge_coeffs_x, edge_coeffs_y, edge_coeffs_z, flips, flags):
    closed_map, open_map = basis_tables()
    nx, ny, nz = flags.shape
    comps = 3
    nodal_x = interpolate(edge_coeffs_x, flips[0], open_map, closed_map, closed_map)
    nodal_y = interpolate(edge_coeffs_y, flips[1], closed_map, open_map, closed_map)
    nodal_z = interpolate(edge_coeffs_z, flips[2], closed_map, closed_map, open_map)
    keep = jnp.pad((1 - flags).astype(jnp.float32), ((0, 1), (2, 2), (2, 2)))
    extended = jnp.stack([nodal_x, nodal_y, nodal_z, keep])

    def own(block):
        return block[..., 2 : ny + 2, 2 : nz + 2]

    data = extended[:comps]
    up = [
        own(data[:, nx - 2 : nx] * keep[nx - 2 : nx]).reshape(-1, nz),
        own(data[:, nx]).reshape(-1, nz),
    ]
    down = [
        own(data[:, 0]).reshape(-1, nz),
        own(keep[0]),
        own(data[:, 1] * keep[1]).reshape(-1, nz),
    ]
    early_prev, early_next = both_ways(jnp.concatenate(up), jnp.concatenate(down), "gx")

    extended = fold_and_halo(extended, "gz", 3)
    extended = fold_and_halo(extended, "gy", 2)
    data = extended[:comps]
    keep = extended[comps]

    def edges(block):
        return [block[..., 2, 2 : nz + 2], block[..., 2 : ny + 2, 2]]

    top = data[:, nx]
    strips_y = jnp.concatenate([top[:, 0:2, 2 : nz + 2], top[:, ny + 2 :, 2 : nz + 2]], axis=1)
    strips_z = jnp.concatenate([top[:, 2 : ny + 2, 0:2], top[:, 2 : ny + 2, nz + 2 :]], axis=2)
    late_up = edges(data[:, nx - 2 : nx] * keep[nx - 2 : nx]) + edges(top) + [strips_y, strips_z]
    late_down = edges(data[:, 0]) + edges(data[:, 1] * keep[1])
    late_prev, late_next = both_ways(pack(late_up, nz), pack(late_down, nz), "gx")
    halo_row, halo_col, top_row, top_col, in_strips_y, in_strips_z = unpack(
        late_prev,
        [(comps, 2, nz), (comps, 2, ny), (comps, nz), (comps, ny), (comps, 4, nz), (comps, ny, 4)],
    )
    bottom_row, bottom_col, next_row, next_col = unpack(
        late_next, [(comps, nz), (comps, ny), (comps, nz), (comps, ny)]
    )

    plane = comps * ny
    prev_halo = patch(early_prev[: 2 * plane].reshape(comps, 2, ny, nz), halo_row, halo_col)
    prev_top = patch(early_prev[2 * plane :].reshape(comps, ny, nz), top_row, top_col)
    next_bottom = patch(early_next[:plane].reshape(comps, ny, nz), bottom_row, bottom_col)
    next_keep = early_next[plane : plane + ny]
    next_halo = patch(early_next[plane + ny :].reshape(comps, ny, nz), next_row, next_col)

    fold_in = cross_plane(prev_top, in_strips_y, in_strips_z)
    first = (data[:, 0] + fold_in) * keep[0]
    last = (own(data[:, nx]) + next_bottom) * next_keep
    widths = ((0, 0), (0, 0), (2, 2), (2, 2))
    masked = jnp.concatenate(
        [
            jnp.pad(prev_halo, widths),
            first[:, None],
            data[:, 1:nx] * keep[1:nx],
            jnp.pad(last[:, None], widths),
            jnp.pad(next_halo[:, None], widths),
        ],
        axis=1,
    )
    return stencil_apply(masked)


def solution(mesh):
    in_specs = (
        P("gx", None, "gy", None, "gz"),
        P("gx", None, "gy", None, "gz"),
        P("gx", None, "gy", None, "gz"),
        P(None, "gx", "gy", "gz"),
        P("gx", "gy", "gz"),
    )
    out_specs = P(None, "gx", "gy", "gz")
    return jax.shard_map(body, mesh=mesh, in_specs=in_specs, out_specs=out_specs, check_vma=False)
```

```python
import math

import jax
import jax.numpy as jnp
import numpy as np
from jax import lax
from jax.sharding import PartitionSpec as P


def lagrange_table(points, targets):
    table = np.ones((len(targets), len(points)))
    for row_pos in range(len(targets)):
        for col_pos in range(len(points)):
            for other in range(len(points)):
                if other != col_pos:
                    table[row_pos, col_pos] *= (targets[row_pos] - points[other]) / (
                        points[col_pos] - points[other]
                    )
    return table


def basis_tables():
    spread = math.sqrt(3.0 / 7.0)
    targets = [0.0, (1.0 - spread) / 2.0, 0.5, (1.0 + spread) / 2.0, 1.0]
    closed = [0.0, 0.25, 0.5, 0.75, 1.0]
    inner = math.sqrt(3.0 / 7.0 - 2.0 / 7.0 * math.sqrt(6.0 / 5.0))
    outer = math.sqrt(3.0 / 7.0 + 2.0 / 7.0 * math.sqrt(6.0 / 5.0))
    gauss = [(1.0 - outer) / 2.0, (1.0 - inner) / 2.0, (1.0 + inner) / 2.0, (1.0 + outer) / 2.0]
    closed_map = np.asarray(lagrange_table(closed, targets), dtype=np.float32).astype(np.float64)
    open_map = np.asarray(lagrange_table(gauss, targets), dtype=np.float32).astype(np.float64)
    return closed_map, open_map


def assembly_matrix(table, count):
    size = table.shape[1]
    matrix = np.zeros((4 * count + 1, count * size))
    for elem_pos in range(count):
        matrix[4 * elem_pos : 4 * elem_pos + 5, size * elem_pos : size * elem_pos + size] += table
    return matrix


def interpolate(coef, flip, table_x, table_y, table_z):
    ex_count, size_x, ey_count, size_y, merged = coef.shape
    size_z = table_z.shape[1]
    ez_count = merged // size_z
    precise = lax.Precision.HIGHEST
    orient = jnp.repeat((1 - 2 * flip).astype(jnp.float32), size_z, axis=2)
    signed = (coef * orient[:, None, :, None, :]).reshape(ex_count * size_x * ey_count * size_y, merged)
    rows_y = np.pad(assembly_matrix(table_y, ey_count), ((2, 1), (0, 0)))
    plane_map = np.kron(assembly_matrix(table_x, ex_count), rows_y)
    depth_map = np.pad(assembly_matrix(table_z, ez_count), ((2, 1), (0, 0)))
    deep = jnp.dot(signed, jnp.asarray(depth_map.T, jnp.float32), precision=precise)
    nodal = jnp.dot(jnp.asarray(plane_map, jnp.float32), deep, precision=precise)
    return nodal.reshape(4 * ex_count + 1, 4 * ey_count + 4, 4 * ez_count + 4)


def shifted(block, axis, step=1):
    count = lax.axis_size(axis)
    if count == 1:
        return block
    return lax.ppermute(block, axis, [(i, (i + step) % count) for i in range(count)])


def both_ways(up, down, axis):
    if lax.axis_size(axis) <= 2:
        both = shifted(jnp.concatenate([up, down]), axis)
        return both[: up.shape[0]], both[up.shape[0] :]
    return shifted(up, axis), shifted(down, axis, -1)


def to_wire(slab, dim):
    layers = jnp.moveaxis(slab, dim, 0)
    return layers.reshape(layers.shape[0] * layers.shape[1], -1), layers.shape


def from_wire(rows, shape, dim):
    return jnp.moveaxis(rows.reshape(shape), 0, dim)


def fold_and_halo(extended, axis, dim):
    length = extended.shape[dim]
    n = length - 4
    up, up_shape = to_wire(lax.slice_in_dim(extended, n, n + 3, axis=dim), dim)
    down, down_shape = to_wire(lax.slice_in_dim(extended, 2, 4, axis=dim), dim)
    from_prev, from_next = both_ways(up, down, axis)
    widths_prev = [(0, 0)] * extended.ndim
    widths_prev[dim] = (0, length - 3)
    widths_next = [(0, 0)] * extended.ndim
    widths_next[dim] = (n + 2, 0)
    return (
        extended
        + jnp.pad(from_wire(from_prev, up_shape, dim), widths_prev)
        + jnp.pad(from_wire(from_next, down_shape, dim), widths_next)
    )


def cross_rows(plane, ny, nz):
    own = plane[:, 2 : ny + 2, 2 : nz + 2]
    strips_y = jnp.concatenate([plane[:, 0:2, 2 : nz + 2], plane[:, ny + 2 :, 2 : nz + 2]], axis=1)
    strips_z = jnp.concatenate([plane[:, 2 : ny + 2, 0:2], plane[:, 2 : ny + 2, nz + 2 :]], axis=2)
    strips_z = jnp.swapaxes(strips_z, 1, 2).reshape(-1)
    strips_z = jnp.pad(strips_z, (0, -strips_z.shape[0] % nz))
    return [own.reshape(-1, nz), strips_y.reshape(-1, nz), strips_z.reshape(-1, nz)]


def cross_plane(own, strips_y, strips_z):
    middle = jnp.concatenate([strips_z[..., 0:2], own, strips_z[..., 2:4]], axis=2)
    widths = ((0, 0), (0, 0), (2, 2))
    return jnp.concatenate(
        [jnp.pad(strips_y[:, 0:2], widths), middle, jnp.pad(strips_y[:, 2:4], widths)], axis=1
    )


def fold_and_halo_last(extended, axis, ny, nz):
    n = extended.shape[1] - 1
    comps = extended.shape[0] - 1
    data = extended[:comps]
    keep = extended[comps]

    def own(block):
        return block[..., 2 : ny + 2, 2 : nz + 2]

    halo_up = own(data[:, n - 2 : n] * keep[n - 2 : n])
    halo_down = own(data[:, 1] * keep[1])
    up_parts = [halo_up.reshape(-1, nz)] + cross_rows(data[:, n], ny, nz)
    down_parts = [own(data[:, 0]).reshape(-1, nz), own(keep[0]), halo_down.reshape(-1, nz)]
    up = jnp.concatenate(up_parts)
    down = jnp.concatenate(down_parts)
    from_prev, from_next = both_ways(up, down, axis)

    sizes = [part.shape[0] for part in up_parts]
    marks = np.cumsum([0] + sizes)
    prev_halo = from_prev[marks[0] : marks[1]].reshape(comps, 2, ny, nz)
    prev_own = from_prev[marks[1] : marks[2]].reshape(comps, ny, nz)
    prev_strips_y = from_prev[marks[2] : marks[3]].reshape(comps, 4, nz)
    prev_strips_z = from_prev[marks[3] : marks[4]].reshape(-1)[: comps * 4 * ny]
    prev_strips_z = jnp.swapaxes(prev_strips_z.reshape(comps, 4, ny), 1, 2)
    fold_in = cross_plane(prev_own, prev_strips_y, prev_strips_z)

    plane_rows = comps * ny
    next_fold = from_next[:plane_rows].reshape(comps, ny, nz)
    next_keep = from_next[plane_rows : plane_rows + ny]
    next_halo = from_next[plane_rows + ny :].reshape(comps, ny, nz)

    widths = ((0, 0), (0, 0), (2, 2), (2, 2))
    first = (data[:, 0] + fold_in) * keep[0]
    last = (own(data[:, n]) + next_fold) * next_keep
    return jnp.concatenate(
        [
            jnp.pad(prev_halo, widths),
            first[:, None],
            data[:, 1:n] * keep[1:n],
            jnp.pad(last[:, None], widths),
            jnp.pad(next_halo[:, None], widths),
        ],
        axis=1,
    )


def window(padded_array, axis_pos, offset):
    starts = [0, 2, 2, 2]
    limits = [
        padded_array.shape[0],
        padded_array.shape[1] - 2,
        padded_array.shape[2] - 2,
        padded_array.shape[3] - 2,
    ]
    starts[axis_pos] = offset
    limits[axis_pos] = offset + padded_array.shape[axis_pos] - 4
    return lax.slice(padded_array, tuple(starts), tuple(limits))


def stencil_apply(padded_array):
    total = 8.0 * window(padded_array, 1, 2)
    for axis_pos in (1, 2, 3):
        near = window(padded_array, axis_pos, 1) + window(padded_array, axis_pos, 3)
        far = window(padded_array, axis_pos, 0) + window(padded_array, axis_pos, 4)
        total = total - 4.0 / 3.0 * near + 1.0 / 12.0 * far
    return 0.25 * total


def body(edge_coeffs_x, edge_coeffs_y, edge_coeffs_z, flips, flags):
    closed_map, open_map = basis_tables()
    nx, ny, nz = flags.shape
    nodal_x = interpolate(edge_coeffs_x, flips[0], open_map, closed_map, closed_map)
    nodal_y = interpolate(edge_coeffs_y, flips[1], closed_map, open_map, closed_map)
    nodal_z = interpolate(edge_coeffs_z, flips[2], closed_map, closed_map, open_map)
    keep = jnp.pad((1 - flags).astype(jnp.float32), ((0, 1), (2, 2), (2, 2)))
    extended = jnp.stack([nodal_x, nodal_y, nodal_z, keep])
    extended = fold_and_halo(extended, "gz", 3)
    extended = fold_and_halo(extended, "gy", 2)
    masked = fold_and_halo_last(extended, "gx", ny, nz)
    return stencil_apply(masked)


def solution(mesh):
    in_specs = (
        P("gx", None, "gy", None, "gz"),
        P("gx", None, "gy", None, "gz"),
        P("gx", None, "gy", None, "gz"),
        P(None, "gx", "gy", "gz"),
        P("gx", "gy", "gz"),
    )
    out_specs = P(None, "gx", "gy", "gz")
    return jax.shard_map(body, mesh=mesh, in_specs=in_specs, out_specs=out_specs, check_vma=False)
```

```python
import math

import jax
import jax.numpy as jnp
import numpy as np
from jax import lax
from jax.sharding import PartitionSpec as P


def lagrange_table(points, targets):
    table = np.ones((len(targets), len(points)))
    for row_pos in range(len(targets)):
        for col_pos in range(len(points)):
            for other in range(len(points)):
                if other != col_pos:
                    table[row_pos, col_pos] *= (targets[row_pos] - points[other]) / (
                        points[col_pos] - points[other]
                    )
    return table


def basis_tables():
    spread = math.sqrt(3.0 / 7.0)
    targets = [0.0, (1.0 - spread) / 2.0, 0.5, (1.0 + spread) / 2.0, 1.0]
    closed = [0.0, 0.25, 0.5, 0.75, 1.0]
    inner = math.sqrt(3.0 / 7.0 - 2.0 / 7.0 * math.sqrt(6.0 / 5.0))
    outer = math.sqrt(3.0 / 7.0 + 2.0 / 7.0 * math.sqrt(6.0 / 5.0))
    gauss = [(1.0 - outer) / 2.0, (1.0 - inner) / 2.0, (1.0 + inner) / 2.0, (1.0 + outer) / 2.0]
    closed_map = np.asarray(lagrange_table(closed, targets), dtype=np.float32).astype(np.float64)
    open_map = np.asarray(lagrange_table(gauss, targets), dtype=np.float32).astype(np.float64)
    return closed_map, open_map


def assembly_matrix(table, count):
    size = table.shape[1]
    matrix = np.zeros((4 * count + 1, count * size))
    for elem_pos in range(count):
        matrix[4 * elem_pos : 4 * elem_pos + 5, size * elem_pos : size * elem_pos + size] += table
    return matrix


def planar_part(coef, flip, table_x, table_y, size_z):
    ex_count, size_x, ey_count, size_y, merged = coef.shape
    orient = jnp.repeat((1 - 2 * flip).astype(jnp.float32), size_z, axis=2)
    signed = (coef * orient[:, None, :, None, :]).reshape(ex_count * size_x * ey_count * size_y, merged)
    rows_y = np.pad(assembly_matrix(table_y, ey_count), ((2, 1), (0, 0)))
    plane_map = np.kron(assembly_matrix(table_x, ex_count), rows_y)
    return jnp.dot(jnp.asarray(plane_map, jnp.float32), signed, precision=lax.Precision.HIGHEST)


def depth_map_of(table_z, merged):
    return np.pad(assembly_matrix(table_z, merged // table_z.shape[1]), ((2, 1), (0, 0)))


def shifted(block, axis, step=1):
    count = lax.axis_size(axis)
    if count == 1:
        return block
    return lax.ppermute(block, axis, [(i, (i + step) % count) for i in range(count)])


def both_ways(up, down, axis):
    if lax.axis_size(axis) <= 2:
        both = shifted(jnp.concatenate([up, down]), axis)
        return both[: up.shape[0]], both[up.shape[0] :]
    return shifted(up, axis), shifted(down, axis, -1)


def to_wire(slab, dim):
    layers = jnp.moveaxis(slab, dim, 0)
    return layers.reshape(layers.shape[0] * layers.shape[1], -1), layers.shape


def from_wire(rows, shape, dim):
    return jnp.moveaxis(rows.reshape(shape), 0, dim)


def fold_and_halo(extended, axis, dim):
    length = extended.shape[dim]
    n = length - 4
    up, up_shape = to_wire(lax.slice_in_dim(extended, n, n + 3, axis=dim), dim)
    down, down_shape = to_wire(lax.slice_in_dim(extended, 2, 4, axis=dim), dim)
    from_prev, from_next = both_ways(up, down, axis)
    widths_prev = [(0, 0)] * extended.ndim
    widths_prev[dim] = (0, length - 3)
    widths_next = [(0, 0)] * extended.ndim
    widths_next[dim] = (n + 2, 0)
    return (
        extended
        + jnp.pad(from_wire(from_prev, up_shape, dim), widths_prev)
        + jnp.pad(from_wire(from_next, down_shape, dim), widths_next)
    )


def cross_rows(plane, ny, nz):
    own = plane[:, 2 : ny + 2, 2 : nz + 2]
    strips_y = jnp.concatenate([plane[:, 0:2, 2 : nz + 2], plane[:, ny + 2 :, 2 : nz + 2]], axis=1)
    strips_z = jnp.concatenate([plane[:, 2 : ny + 2, 0:2], plane[:, 2 : ny + 2, nz + 2 :]], axis=2)
    strips_z = jnp.swapaxes(strips_z, 1, 2).reshape(-1)
    strips_z = jnp.pad(strips_z, (0, -strips_z.shape[0] % nz))
    return [own.reshape(-1, nz), strips_y.reshape(-1, nz), strips_z.reshape(-1, nz)]


def cross_plane(own, strips_y, strips_z):
    middle = jnp.concatenate([strips_z[..., 0:2], own, strips_z[..., 2:4]], axis=2)
    widths = ((0, 0), (0, 0), (2, 2))
    return jnp.concatenate(
        [jnp.pad(strips_y[:, 0:2], widths), middle, jnp.pad(strips_y[:, 2:4], widths)], axis=1
    )


def fold_and_halo_last(extended, axis, ny, nz):
    n = extended.shape[1] - 1
    comps = extended.shape[0] - 1
    data = extended[:comps]
    keep = extended[comps]

    def own(block):
        return block[..., 2 : ny + 2, 2 : nz + 2]

    halo_up = own(data[:, n - 2 : n] * keep[n - 2 : n])
    halo_down = own(data[:, 1] * keep[1])
    up_parts = [halo_up.reshape(-1, nz)] + cross_rows(data[:, n], ny, nz)
    down_parts = [own(data[:, 0]).reshape(-1, nz), own(keep[0]), halo_down.reshape(-1, nz)]
    up = jnp.concatenate(up_parts)
    down = jnp.concatenate(down_parts)
    from_prev, from_next = both_ways(up, down, axis)

    sizes = [part.shape[0] for part in up_parts]
    marks = np.cumsum([0] + sizes)
    prev_halo = from_prev[marks[0] : marks[1]].reshape(comps, 2, ny, nz)
    prev_own = from_prev[marks[1] : marks[2]].reshape(comps, ny, nz)
    prev_strips_y = from_prev[marks[2] : marks[3]].reshape(comps, 4, nz)
    prev_strips_z = from_prev[marks[3] : marks[4]].reshape(-1)[: comps * 4 * ny]
    prev_strips_z = jnp.swapaxes(prev_strips_z.reshape(comps, 4, ny), 1, 2)
    fold_in = cross_plane(prev_own, prev_strips_y, prev_strips_z)

    plane_rows = comps * ny
    next_fold = from_next[:plane_rows].reshape(comps, ny, nz)
    next_keep = from_next[plane_rows : plane_rows + ny]
    next_halo = from_next[plane_rows + ny :].reshape(comps, ny, nz)

    widths = ((0, 0), (0, 0), (2, 2), (2, 2))
    first = (data[:, 0] + fold_in) * keep[0]
    last = (own(data[:, n]) + next_fold) * next_keep
    return jnp.concatenate(
        [
            jnp.pad(prev_halo, widths),
            first[:, None],
            data[:, 1:n] * keep[1:n],
            jnp.pad(last[:, None], widths),
            jnp.pad(next_halo[:, None], widths),
        ],
        axis=1,
    )


def window(padded_array, axis_pos, offset):
    starts = [0, 2, 2, 2]
    limits = [
        padded_array.shape[0],
        padded_array.shape[1] - 2,
        padded_array.shape[2] - 2,
        padded_array.shape[3] - 2,
    ]
    starts[axis_pos] = offset
    limits[axis_pos] = offset + padded_array.shape[axis_pos] - 4
    return lax.slice(padded_array, tuple(starts), tuple(limits))


def stencil_apply(padded_array):
    total = 8.0 * window(padded_array, 1, 2)
    for axis_pos in (1, 2, 3):
        near = window(padded_array, axis_pos, 1) + window(padded_array, axis_pos, 3)
        far = window(padded_array, axis_pos, 0) + window(padded_array, axis_pos, 4)
        total = total - 4.0 / 3.0 * near + 1.0 / 12.0 * far
    return 0.25 * total


def body(edge_coeffs_x, edge_coeffs_y, edge_coeffs_z, flips, flags):
    closed_map, open_map = basis_tables()
    nx, ny, nz = flags.shape
    precise = lax.Precision.HIGHEST
    inputs = [
        (edge_coeffs_x, flips[0], open_map, closed_map, closed_map),
        (edge_coeffs_y, flips[1], closed_map, open_map, closed_map),
        (edge_coeffs_z, flips[2], closed_map, closed_map, open_map),
    ]
    length = nz + 4
    up_places = [nz, nz + 1, nz + 2]
    down_places = [2, 3]
    planars = []
    depths = []
    slabs = []
    for coef, flip, table_x, table_y, table_z in inputs:
        planar = planar_part(coef, flip, table_x, table_y, table_z.shape[1])
        depth_map = depth_map_of(table_z, coef.shape[4])
        edge_map = jnp.asarray(depth_map[up_places + down_places], jnp.float32)
        planars.append(planar)
        depths.append(depth_map)
        slabs.append(lax.dot_general(edge_map, planar, (((1,), (1,)), ((), ())), precision=precise))
    keep = jnp.pad((1 - flags).astype(jnp.float32), ((0, 1), (2, 2), (2, 2)))
    slabs.append(jnp.moveaxis(keep[..., up_places + down_places], 2, 0).reshape(5, -1))
    slabs = jnp.stack(slabs)
    up = slabs[:, :3].reshape(-1, slabs.shape[2])
    down = slabs[:, 3:].reshape(-1, slabs.shape[2])
    from_prev, from_next = both_ways(up, down, "gz")
    arrived = jnp.concatenate(
        [from_prev.reshape(4, 3, -1), from_next.reshape(4, 2, -1)], axis=1
    )
    place = np.zeros((5, length))
    for row, col in enumerate([0, 1, 2, nz + 2, nz + 3]):
        place[row, col] = 1.0
    place = jnp.asarray(place, jnp.float32)
    nodal = []
    for comp in range(3):
        own_part = jnp.dot(planars[comp], jnp.asarray(depths[comp].T, jnp.float32), precision=precise)
        folded = lax.dot_general(arrived[comp], place, (((0,), (0,)), ((), ())), precision=precise)
        nodal.append((own_part + folded).reshape(nx + 1, ny + 4, length))
    keep_in = jnp.moveaxis(arrived[3].reshape(5, nx + 1, ny + 4), 0, 2)
    keep = keep + jnp.pad(keep_in[..., :3], ((0, 0), (0, 0), (0, length - 3))) + jnp.pad(
        keep_in[..., 3:], ((0, 0), (0, 0), (nz + 2, 0))
    )
    extended = jnp.stack(nodal + [keep])
    extended = fold_and_halo(extended, "gy", 2)
    masked = fold_and_halo_last(extended, "gx", ny, nz)
    return stencil_apply(masked)


def solution(mesh):
    in_specs = (
        P("gx", None, "gy", None, "gz"),
        P("gx", None, "gy", None, "gz"),
        P("gx", None, "gy", None, "gz"),
        P(None, "gx", "gy", "gz"),
        P("gx", "gy", "gz"),
    )
    out_specs = P(None, "gx", "gy", "gz")
    return jax.shard_map(body, mesh=mesh, in_specs=in_specs, out_specs=out_specs, check_vma=False)
```

```python
import math

import jax
import jax.numpy as jnp
import numpy as np
from jax import lax
from jax.sharding import PartitionSpec as P


def lagrange_table(points, targets):
    table = np.ones((len(targets), len(points)))
    for row_pos in range(len(targets)):
        for col_pos in range(len(points)):
            for other in range(len(points)):
                if other != col_pos:
                    table[row_pos, col_pos] *= (targets[row_pos] - points[other]) / (
                        points[col_pos] - points[other]
                    )
    return table


def basis_tables():
    spread = math.sqrt(3.0 / 7.0)
    targets = [0.0, (1.0 - spread) / 2.0, 0.5, (1.0 + spread) / 2.0, 1.0]
    closed = [0.0, 0.25, 0.5, 0.75, 1.0]
    inner = math.sqrt(3.0 / 7.0 - 2.0 / 7.0 * math.sqrt(6.0 / 5.0))
    outer = math.sqrt(3.0 / 7.0 + 2.0 / 7.0 * math.sqrt(6.0 / 5.0))
    gauss = [(1.0 - outer) / 2.0, (1.0 - inner) / 2.0, (1.0 + inner) / 2.0, (1.0 + outer) / 2.0]
    closed_map = np.asarray(lagrange_table(closed, targets), dtype=np.float32).astype(np.float64)
    open_map = np.asarray(lagrange_table(gauss, targets), dtype=np.float32).astype(np.float64)
    return closed_map, open_map


def assembly_matrix(table, count):
    size = table.shape[1]
    matrix = np.zeros((4 * count + 1, count * size))
    for elem_pos in range(count):
        matrix[4 * elem_pos : 4 * elem_pos + 5, size * elem_pos : size * elem_pos + size] += table
    return matrix


def planar_part(coef, flip, table_x, table_y, size_z):
    ex_count, size_x, ey_count, size_y, merged = coef.shape
    orient = jnp.repeat((1 - 2 * flip).astype(jnp.float32), size_z, axis=2)
    signed = (coef * orient[:, None, :, None, :]).reshape(ex_count * size_x * ey_count * size_y, merged)
    rows_y = np.pad(assembly_matrix(table_y, ey_count), ((2, 1), (0, 0)))
    plane_map = np.kron(assembly_matrix(table_x, ex_count), rows_y)
    return jnp.dot(jnp.asarray(plane_map, jnp.float32), signed, precision=lax.Precision.HIGH)


def depth_map_of(table_z, merged):
    return np.pad(assembly_matrix(table_z, merged // table_z.shape[1]), ((2, 1), (0, 0)))


def shifted(block, axis, step=1):
    count = lax.axis_size(axis)
    if count == 1:
        return block
    return lax.ppermute(block, axis, [(i, (i + step) % count) for i in range(count)])


def both_ways(up, down, axis):
    if lax.axis_size(axis) <= 2:
        both = shifted(jnp.concatenate([up, down]), axis)
        return both[: up.shape[0]], both[up.shape[0] :]
    return shifted(up, axis), shifted(down, axis, -1)


def to_wire(slab, dim):
    layers = jnp.moveaxis(slab, dim, 0)
    return layers.reshape(layers.shape[0] * layers.shape[1], -1), layers.shape


def from_wire(rows, shape, dim):
    return jnp.moveaxis(rows.reshape(shape), 0, dim)


def fold_and_halo(extended, axis, dim):
    length = extended.shape[dim]
    n = length - 4
    up, up_shape = to_wire(lax.slice_in_dim(extended, n, n + 3, axis=dim), dim)
    down, down_shape = to_wire(lax.slice_in_dim(extended, 2, 4, axis=dim), dim)
    from_prev, from_next = both_ways(up, down, axis)
    widths_prev = [(0, 0)] * extended.ndim
    widths_prev[dim] = (0, length - 3)
    widths_next = [(0, 0)] * extended.ndim
    widths_next[dim] = (n + 2, 0)
    return (
        extended
        + jnp.pad(from_wire(from_prev, up_shape, dim), widths_prev)
        + jnp.pad(from_wire(from_next, down_shape, dim), widths_next)
    )


def cross_rows(plane, ny, nz):
    own = plane[:, 2 : ny + 2, 2 : nz + 2]
    strips_y = jnp.concatenate([plane[:, 0:2, 2 : nz + 2], plane[:, ny + 2 :, 2 : nz + 2]], axis=1)
    strips_z = jnp.concatenate([plane[:, 2 : ny + 2, 0:2], plane[:, 2 : ny + 2, nz + 2 :]], axis=2)
    strips_z = jnp.swapaxes(strips_z, 1, 2).reshape(-1)
    strips_z = jnp.pad(strips_z, (0, -strips_z.shape[0] % nz))
    return [own.reshape(-1, nz), strips_y.reshape(-1, nz), strips_z.reshape(-1, nz)]


def cross_plane(own, strips_y, strips_z):
    middle = jnp.concatenate([strips_z[..., 0:2], own, strips_z[..., 2:4]], axis=2)
    widths = ((0, 0), (0, 0), (2, 2))
    return jnp.concatenate(
        [jnp.pad(strips_y[:, 0:2], widths), middle, jnp.pad(strips_y[:, 2:4], widths)], axis=1
    )


def fold_and_halo_last(extended, axis, ny, nz):
    n = extended.shape[1] - 1
    comps = extended.shape[0] - 1
    data = extended[:comps]
    keep = extended[comps]

    def own(block):
        return block[..., 2 : ny + 2, 2 : nz + 2]

    halo_up = own(data[:, n - 2 : n] * keep[n - 2 : n])
    halo_down = own(data[:, 1] * keep[1])
    up_parts = [halo_up.reshape(-1, nz)] + cross_rows(data[:, n], ny, nz)
    down_parts = [own(data[:, 0]).reshape(-1, nz), own(keep[0]), halo_down.reshape(-1, nz)]
    up = jnp.concatenate(up_parts)
    down = jnp.concatenate(down_parts)
    from_prev, from_next = both_ways(up, down, axis)

    sizes = [part.shape[0] for part in up_parts]
    marks = np.cumsum([0] + sizes)
    prev_halo = from_prev[marks[0] : marks[1]].reshape(comps, 2, ny, nz)
    prev_own = from_prev[marks[1] : marks[2]].reshape(comps, ny, nz)
    prev_strips_y = from_prev[marks[2] : marks[3]].reshape(comps, 4, nz)
    prev_strips_z = from_prev[marks[3] : marks[4]].reshape(-1)[: comps * 4 * ny]
    prev_strips_z = jnp.swapaxes(prev_strips_z.reshape(comps, 4, ny), 1, 2)
    fold_in = cross_plane(prev_own, prev_strips_y, prev_strips_z)

    plane_rows = comps * ny
    next_fold = from_next[:plane_rows].reshape(comps, ny, nz)
    next_keep = from_next[plane_rows : plane_rows + ny]
    next_halo = from_next[plane_rows + ny :].reshape(comps, ny, nz)

    widths = ((0, 0), (0, 0), (2, 2), (2, 2))
    first = (data[:, 0] + fold_in) * keep[0]
    last = (own(data[:, n]) + next_fold) * next_keep
    return jnp.concatenate(
        [
            jnp.pad(prev_halo, widths),
            first[:, None],
            data[:, 1:n] * keep[1:n],
            jnp.pad(last[:, None], widths),
            jnp.pad(next_halo[:, None], widths),
        ],
        axis=1,
    )


def window(padded_array, axis_pos, offset):
    starts = [0, 2, 2, 2]
    limits = [
        padded_array.shape[0],
        padded_array.shape[1] - 2,
        padded_array.shape[2] - 2,
        padded_array.shape[3] - 2,
    ]
    starts[axis_pos] = offset
    limits[axis_pos] = offset + padded_array.shape[axis_pos] - 4
    return lax.slice(padded_array, tuple(starts), tuple(limits))


def stencil_apply(padded_array):
    total = 8.0 * window(padded_array, 1, 2)
    for axis_pos in (1, 2, 3):
        near = window(padded_array, axis_pos, 1) + window(padded_array, axis_pos, 3)
        far = window(padded_array, axis_pos, 0) + window(padded_array, axis_pos, 4)
        total = total - 4.0 / 3.0 * near + 1.0 / 12.0 * far
    return 0.25 * total


def body(edge_coeffs_x, edge_coeffs_y, edge_coeffs_z, flips, flags):
    closed_map, open_map = basis_tables()
    nx, ny, nz = flags.shape
    precise = lax.Precision.HIGHEST
    inputs = [
        (edge_coeffs_x, flips[0], open_map, closed_map, closed_map),
        (edge_coeffs_y, flips[1], closed_map, open_map, closed_map),
        (edge_coeffs_z, flips[2], closed_map, closed_map, open_map),
    ]
    length = nz + 4
    up_places = [nz, nz + 1, nz + 2]
    down_places = [2, 3]
    planars = []
    depths = []
    slabs = []
    for coef, flip, table_x, table_y, table_z in inputs:
        planar = planar_part(coef, flip, table_x, table_y, table_z.shape[1])
        depth_map = depth_map_of(table_z, coef.shape[4])
        edge_map = jnp.asarray(depth_map[up_places + down_places], jnp.float32)
        planars.append(planar)
        depths.append(depth_map)
        slabs.append(
            lax.dot_general(edge_map, planar, (((1,), (1,)), ((), ())), precision=lax.Precision.HIGH)
        )
    keep = jnp.pad((1 - flags).astype(jnp.float32), ((0, 1), (2, 2), (2, 2)))
    slabs.append(jnp.moveaxis(keep[..., up_places + down_places], 2, 0).reshape(5, -1))
    slabs = jnp.stack(slabs)
    up = slabs[:, :3].reshape(-1, slabs.shape[2])
    down = slabs[:, 3:].reshape(-1, slabs.shape[2])
    from_prev, from_next = both_ways(up, down, "gz")
    arrived = jnp.concatenate(
        [from_prev.reshape(4, 3, -1), from_next.reshape(4, 2, -1)], axis=1
    )
    place = np.zeros((5, length))
    for row, col in enumerate([0, 1, 2, nz + 2, nz + 3]):
        place[row, col] = 1.0
    place = jnp.asarray(place, jnp.float32)
    nodal = []
    for comp in range(3):
        own_part = jnp.dot(
            planars[comp], jnp.asarray(depths[comp].T, jnp.float32), precision=lax.Precision.HIGH
        )
        folded = lax.dot_general(arrived[comp], place, (((0,), (0,)), ((), ())), precision=precise)
        nodal.append((own_part + folded).reshape(nx + 1, ny + 4, length))
    keep_in = jnp.moveaxis(arrived[3].reshape(5, nx + 1, ny + 4), 0, 2)
    keep = keep + jnp.pad(keep_in[..., :3], ((0, 0), (0, 0), (0, length - 3))) + jnp.pad(
        keep_in[..., 3:], ((0, 0), (0, 0), (nz + 2, 0))
    )
    extended = jnp.stack(nodal + [keep])
    extended = fold_and_halo(extended, "gy", 2)
    masked = fold_and_halo_last(extended, "gx", ny, nz)
    return stencil_apply(masked)


def solution(mesh):
    in_specs = (
        P("gx", None, "gy", None, "gz"),
        P("gx", None, "gy", None, "gz"),
        P("gx", None, "gy", None, "gz"),
        P(None, "gx", "gy", "gz"),
        P("gx", "gy", "gz"),
    )
    out_specs = P(None, "gx", "gy", "gz")
    return jax.shard_map(body, mesh=mesh, in_specs=in_specs, out_specs=out_specs, check_vma=False)
```

```python
import math

import jax
import jax.numpy as jnp
import numpy as np
from jax import lax
from jax.sharding import PartitionSpec as P


def lagrange_table(points, targets):
    table = np.ones((len(targets), len(points)))
    for row_pos in range(len(targets)):
        for col_pos in range(len(points)):
            for other in range(len(points)):
                if other != col_pos:
                    table[row_pos, col_pos] *= (targets[row_pos] - points[other]) / (
                        points[col_pos] - points[other]
                    )
    return table


def basis_tables():
    spread = math.sqrt(3.0 / 7.0)
    targets = [0.0, (1.0 - spread) / 2.0, 0.5, (1.0 + spread) / 2.0, 1.0]
    closed = [0.0, 0.25, 0.5, 0.75, 1.0]
    inner = math.sqrt(3.0 / 7.0 - 2.0 / 7.0 * math.sqrt(6.0 / 5.0))
    outer = math.sqrt(3.0 / 7.0 + 2.0 / 7.0 * math.sqrt(6.0 / 5.0))
    gauss = [(1.0 - outer) / 2.0, (1.0 - inner) / 2.0, (1.0 + inner) / 2.0, (1.0 + outer) / 2.0]
    closed_map = np.asarray(lagrange_table(closed, targets), dtype=np.float32).astype(np.float64)
    open_map = np.asarray(lagrange_table(gauss, targets), dtype=np.float32).astype(np.float64)
    return closed_map, open_map


def assembly_matrix(table, count):
    size = table.shape[1]
    matrix = np.zeros((4 * count + 1, count * size))
    for elem_pos in range(count):
        matrix[4 * elem_pos : 4 * elem_pos + 5, size * elem_pos : size * elem_pos + size] += table
    return matrix


def planar_part(coef, flip, table_x, table_y, size_z):
    ex_count, size_x, ey_count, size_y, merged = coef.shape
    orient = jnp.repeat((1 - 2 * flip).astype(jnp.float32), size_z, axis=2)
    signed = (coef * orient[:, None, :, None, :]).reshape(ex_count * size_x * ey_count * size_y, merged)
    rows_y = np.pad(assembly_matrix(table_y, ey_count), ((2, 1), (0, 0)))
    plane_map = np.kron(assembly_matrix(table_x, ex_count), rows_y)
    return jnp.dot(jnp.asarray(plane_map, jnp.float32), signed, precision=lax.Precision.HIGH)


def depth_map_of(table_z, merged):
    return np.pad(assembly_matrix(table_z, merged // table_z.shape[1]), ((2, 1), (0, 0)))


def shifted(block, axis, step=1):
    count = lax.axis_size(axis)
    if count == 1:
        return block
    return lax.ppermute(block, axis, [(i, (i + step) % count) for i in range(count)])


def both_ways(up, down, axis):
    if lax.axis_size(axis) <= 2:
        both = shifted(jnp.concatenate([up, down]), axis)
        return both[: up.shape[0]], both[up.shape[0] :]
    return shifted(up, axis), shifted(down, axis, -1)


def to_wire(slab, dim):
    layers = jnp.moveaxis(slab, dim, 0)
    return layers.reshape(layers.shape[0] * layers.shape[1], -1), layers.shape


def from_wire(rows, shape, dim):
    return jnp.moveaxis(rows.reshape(shape), 0, dim)


def fold_and_halo(extended, axis, dim):
    length = extended.shape[dim]
    n = length - 4
    up, up_shape = to_wire(lax.slice_in_dim(extended, n, n + 3, axis=dim), dim)
    down, down_shape = to_wire(lax.slice_in_dim(extended, 2, 4, axis=dim), dim)
    from_prev, from_next = both_ways(up, down, axis)
    widths_prev = [(0, 0)] * extended.ndim
    widths_prev[dim] = (0, length - 3)
    widths_next = [(0, 0)] * extended.ndim
    widths_next[dim] = (n + 2, 0)
    return (
        extended
        + jnp.pad(from_wire(from_prev, up_shape, dim), widths_prev)
        + jnp.pad(from_wire(from_next, down_shape, dim), widths_next)
    )


def cross_rows(plane, ny, nz):
    own = plane[:, 2 : ny + 2, 2 : nz + 2]
    strips_y = jnp.concatenate([plane[:, 0:2, 2 : nz + 2], plane[:, ny + 2 :, 2 : nz + 2]], axis=1)
    strips_z = jnp.concatenate([plane[:, 2 : ny + 2, 0:2], plane[:, 2 : ny + 2, nz + 2 :]], axis=2)
    strips_z = jnp.swapaxes(strips_z, 1, 2).reshape(-1)
    strips_z = jnp.pad(strips_z, (0, -strips_z.shape[0] % nz))
    return [own.reshape(-1, nz), strips_y.reshape(-1, nz), strips_z.reshape(-1, nz)]


def cross_plane(own, strips_y, strips_z):
    middle = jnp.concatenate([strips_z[..., 0:2], own, strips_z[..., 2:4]], axis=2)
    widths = ((0, 0), (0, 0), (2, 2))
    return jnp.concatenate(
        [jnp.pad(strips_y[:, 0:2], widths), middle, jnp.pad(strips_y[:, 2:4], widths)], axis=1
    )


def fold_and_halo_last(extended, axis, ny, nz):
    n = extended.shape[1] - 1
    comps = extended.shape[0] - 1
    data = extended[:comps]
    keep = extended[comps]

    def own(block):
        return block[..., 2 : ny + 2, 2 : nz + 2]

    halo_up = own(data[:, n - 2 : n] * keep[n - 2 : n])
    halo_down = own(data[:, 1] * keep[1])
    up_parts = [halo_up.reshape(-1, nz)] + cross_rows(data[:, n], ny, nz)
    down_parts = [own(data[:, 0]).reshape(-1, nz), own(keep[0]), halo_down.reshape(-1, nz)]
    up = jnp.concatenate(up_parts)
    down = jnp.concatenate(down_parts)
    from_prev, from_next = both_ways(up, down, axis)

    sizes = [part.shape[0] for part in up_parts]
    marks = np.cumsum([0] + sizes)
    prev_halo = from_prev[marks[0] : marks[1]].reshape(comps, 2, ny, nz)
    prev_own = from_prev[marks[1] : marks[2]].reshape(comps, ny, nz)
    prev_strips_y = from_prev[marks[2] : marks[3]].reshape(comps, 4, nz)
    prev_strips_z = from_prev[marks[3] : marks[4]].reshape(-1)[: comps * 4 * ny]
    prev_strips_z = jnp.swapaxes(prev_strips_z.reshape(comps, 4, ny), 1, 2)
    fold_in = cross_plane(prev_own, prev_strips_y, prev_strips_z)

    plane_rows = comps * ny
    next_fold = from_next[:plane_rows].reshape(comps, ny, nz)
    next_keep = from_next[plane_rows : plane_rows + ny]
    next_halo = from_next[plane_rows + ny :].reshape(comps, ny, nz)

    widths = ((0, 0), (0, 0), (2, 2), (2, 2))
    first = (data[:, 0] + fold_in) * keep[0]
    last = (own(data[:, n]) + next_fold) * next_keep
    return jnp.concatenate(
        [
            jnp.pad(prev_halo, widths),
            first[:, None],
            data[:, 1:n] * keep[1:n],
            jnp.pad(last[:, None], widths),
            jnp.pad(next_halo[:, None], widths),
        ],
        axis=1,
    )


def window(padded_array, axis_pos, offset):
    starts = [0, 2, 2, 2]
    limits = [
        padded_array.shape[0],
        padded_array.shape[1] - 2,
        padded_array.shape[2] - 2,
        padded_array.shape[3] - 2,
    ]
    starts[axis_pos] = offset
    limits[axis_pos] = offset + padded_array.shape[axis_pos] - 4
    return lax.slice(padded_array, tuple(starts), tuple(limits))


def stencil_apply(padded_array):
    total = 8.0 * window(padded_array, 1, 2)
    for axis_pos in (1, 2, 3):
        near = window(padded_array, axis_pos, 1) + window(padded_array, axis_pos, 3)
        far = window(padded_array, axis_pos, 0) + window(padded_array, axis_pos, 4)
        total = total - 4.0 / 3.0 * near + 1.0 / 12.0 * far
    return 0.25 * total


def body(edge_coeffs_x, edge_coeffs_y, edge_coeffs_z, flips, flags):
    closed_map, open_map = basis_tables()
    nx, ny, nz = flags.shape
    precise = lax.Precision.HIGHEST
    inputs = [
        (edge_coeffs_x, flips[0], open_map, closed_map, closed_map),
        (edge_coeffs_y, flips[1], closed_map, open_map, closed_map),
        (edge_coeffs_z, flips[2], closed_map, closed_map, open_map),
    ]
    length = nz + 4
    up_places = [nz, nz + 1, nz + 2]
    down_places = [2, 3]
    planars = []
    depths = []
    slabs = []
    for coef, flip, table_x, table_y, table_z in inputs:
        planar = planar_part(coef, flip, table_x, table_y, table_z.shape[1])
        depth_map = depth_map_of(table_z, coef.shape[4])
        edge_map = jnp.asarray(depth_map[up_places + down_places], jnp.float32)
        planars.append(planar)
        depths.append(depth_map)
        slabs.append(
            lax.dot_general(edge_map, planar, (((1,), (1,)), ((), ())), precision=lax.Precision.HIGH)
        )
    keep_own = (1 - flags).astype(jnp.float32)
    keep = jnp.pad(keep_own, ((0, 1), (2, 2), (2, 2)))
    keep_layers = [
        lax.slice_in_dim(keep_own, nz - 2, nz, axis=2),
        jnp.zeros_like(lax.slice_in_dim(keep_own, 0, 1, axis=2)),
        lax.slice_in_dim(keep_own, 0, 2, axis=2),
    ]
    keep_layers = jnp.moveaxis(jnp.concatenate(keep_layers, axis=2), 2, 0)
    slabs.append(jnp.pad(keep_layers, ((0, 0), (0, 1), (2, 2))).reshape(5, -1))
    slabs = jnp.stack(slabs)
    up = slabs[:, :3].reshape(-1, slabs.shape[2])
    down = slabs[:, 3:].reshape(-1, slabs.shape[2])
    from_prev, from_next = both_ways(up, down, "gz")
    arrived = jnp.concatenate(
        [from_prev.reshape(4, 3, -1), from_next.reshape(4, 2, -1)], axis=1
    )
    place = np.zeros((5, length))
    for row, col in enumerate([0, 1, 2, nz + 2, nz + 3]):
        place[row, col] = 1.0
    place = jnp.asarray(place, jnp.float32)
    nodal = []
    for comp in range(3):
        own_part = jnp.dot(
            planars[comp], jnp.asarray(depths[comp].T, jnp.float32), precision=lax.Precision.HIGH
        )
        folded = lax.dot_general(arrived[comp], place, (((0,), (0,)), ((), ())), precision=precise)
        nodal.append((own_part + folded).reshape(nx + 1, ny + 4, length))
    keep_in = jnp.moveaxis(arrived[3].reshape(5, nx + 1, ny + 4), 0, 2)
    keep = keep + jnp.pad(keep_in[..., :3], ((0, 0), (0, 0), (0, length - 3))) + jnp.pad(
        keep_in[..., 3:], ((0, 0), (0, 0), (nz + 2, 0))
    )
    extended = jnp.stack(nodal + [keep])
    extended = fold_and_halo(extended, "gy", 2)
    masked = fold_and_halo_last(extended, "gx", ny, nz)
    return stencil_apply(masked)


def solution(mesh):
    in_specs = (
        P("gx", None, "gy", None, "gz"),
        P("gx", None, "gy", None, "gz"),
        P("gx", None, "gy", None, "gz"),
        P(None, "gx", "gy", "gz"),
        P("gx", "gy", "gz"),
    )
    out_specs = P(None, "gx", "gy", "gz")
    return jax.shard_map(body, mesh=mesh, in_specs=in_specs, out_specs=out_specs, check_vma=False)
```

```python
import math

import jax
import jax.numpy as jnp
import numpy as np
from jax import lax
from jax.sharding import PartitionSpec as P


def lagrange_table(points, targets):
    table = np.ones((len(targets), len(points)))
    for row_pos in range(len(targets)):
        for col_pos in range(len(points)):
            for other in range(len(points)):
                if other != col_pos:
                    table[row_pos, col_pos] *= (targets[row_pos] - points[other]) / (
                        points[col_pos] - points[other]
                    )
    return table


def basis_tables():
    spread = math.sqrt(3.0 / 7.0)
    targets = [0.0, (1.0 - spread) / 2.0, 0.5, (1.0 + spread) / 2.0, 1.0]
    closed = [0.0, 0.25, 0.5, 0.75, 1.0]
    inner = math.sqrt(3.0 / 7.0 - 2.0 / 7.0 * math.sqrt(6.0 / 5.0))
    outer = math.sqrt(3.0 / 7.0 + 2.0 / 7.0 * math.sqrt(6.0 / 5.0))
    gauss = [(1.0 - outer) / 2.0, (1.0 - inner) / 2.0, (1.0 + inner) / 2.0, (1.0 + outer) / 2.0]
    closed_map = np.asarray(lagrange_table(closed, targets), dtype=np.float32).astype(np.float64)
    open_map = np.asarray(lagrange_table(gauss, targets), dtype=np.float32).astype(np.float64)
    return closed_map, open_map


def assembly_matrix(table, count):
    size = table.shape[1]
    matrix = np.zeros((4 * count + 1, count * size))
    for elem_pos in range(count):
        matrix[4 * elem_pos : 4 * elem_pos + 5, size * elem_pos : size * elem_pos + size] += table
    return matrix


def signed_coefficients(coef, flip, size_z):
    ex_count, size_x, ey_count, size_y, merged = coef.shape
    orient = jnp.repeat((1 - 2 * flip).astype(jnp.float32), size_z, axis=2)
    return (coef * orient[:, None, :, None, :]).reshape(ex_count * size_x * ey_count * size_y, merged)


def plane_map_of(table_x, table_y, ex_count, ey_count):
    rows_y = np.pad(assembly_matrix(table_y, ey_count), ((2, 1), (0, 0)))
    return np.kron(assembly_matrix(table_x, ex_count), rows_y)


def depth_map_of(table_z, merged):
    return np.pad(assembly_matrix(table_z, merged // table_z.shape[1]), ((2, 1), (0, 0)))


def shifted(block, axis, step=1):
    count = lax.axis_size(axis)
    if count == 1:
        return block
    return lax.ppermute(block, axis, [(i, (i + step) % count) for i in range(count)])


def both_ways(up, down, axis):
    if lax.axis_size(axis) <= 2:
        both = shifted(jnp.concatenate([up, down]), axis)
        return both[: up.shape[0]], both[up.shape[0] :]
    return shifted(up, axis), shifted(down, axis, -1)


def to_wire(slab, dim):
    layers = jnp.moveaxis(slab, dim, 0)
    return layers.reshape(layers.shape[0] * layers.shape[1], -1), layers.shape


def from_wire(rows, shape, dim):
    return jnp.moveaxis(rows.reshape(shape), 0, dim)


def fold_and_halo(extended, axis, dim):
    length = extended.shape[dim]
    n = length - 4
    up, up_shape = to_wire(lax.slice_in_dim(extended, n, n + 3, axis=dim), dim)
    down, down_shape = to_wire(lax.slice_in_dim(extended, 2, 4, axis=dim), dim)
    from_prev, from_next = both_ways(up, down, axis)
    widths_prev = [(0, 0)] * extended.ndim
    widths_prev[dim] = (0, length - 3)
    widths_next = [(0, 0)] * extended.ndim
    widths_next[dim] = (n + 2, 0)
    return (
        extended
        + jnp.pad(from_wire(from_prev, up_shape, dim), widths_prev)
        + jnp.pad(from_wire(from_next, down_shape, dim), widths_next)
    )


def cross_rows(plane, ny, nz):
    own = plane[:, 2 : ny + 2, 2 : nz + 2]
    strips_y = jnp.concatenate([plane[:, 0:2, 2 : nz + 2], plane[:, ny + 2 :, 2 : nz + 2]], axis=1)
    strips_z = jnp.concatenate([plane[:, 2 : ny + 2, 0:2], plane[:, 2 : ny + 2, nz + 2 :]], axis=2)
    strips_z = jnp.swapaxes(strips_z, 1, 2).reshape(-1)
    strips_z = jnp.pad(strips_z, (0, -strips_z.shape[0] % nz))
    return [own.reshape(-1, nz), strips_y.reshape(-1, nz), strips_z.reshape(-1, nz)]


def cross_plane(own, strips_y, strips_z):
    middle = jnp.concatenate([strips_z[..., 0:2], own, strips_z[..., 2:4]], axis=2)
    widths = ((0, 0), (0, 0), (2, 2))
    return jnp.concatenate(
        [jnp.pad(strips_y[:, 0:2], widths), middle, jnp.pad(strips_y[:, 2:4], widths)], axis=1
    )


def fold_and_halo_last(extended, axis, ny, nz):
    n = extended.shape[1] - 1
    comps = extended.shape[0] - 1
    data = extended[:comps]
    keep = extended[comps]

    def own(block):
        return block[..., 2 : ny + 2, 2 : nz + 2]

    halo_up = own(data[:, n - 2 : n] * keep[n - 2 : n])
    halo_down = own(data[:, 1] * keep[1])
    up_parts = [halo_up.reshape(-1, nz)] + cross_rows(data[:, n], ny, nz)
    down_parts = [own(data[:, 0]).reshape(-1, nz), own(keep[0]), halo_down.reshape(-1, nz)]
    up = jnp.concatenate(up_parts)
    down = jnp.concatenate(down_parts)
    from_prev, from_next = both_ways(up, down, axis)

    sizes = [part.shape[0] for part in up_parts]
    marks = np.cumsum([0] + sizes)
    prev_halo = from_prev[marks[0] : marks[1]].reshape(comps, 2, ny, nz)
    prev_own = from_prev[marks[1] : marks[2]].reshape(comps, ny, nz)
    prev_strips_y = from_prev[marks[2] : marks[3]].reshape(comps, 4, nz)
    prev_strips_z = from_prev[marks[3] : marks[4]].reshape(-1)[: comps * 4 * ny]
    prev_strips_z = jnp.swapaxes(prev_strips_z.reshape(comps, 4, ny), 1, 2)
    fold_in = cross_plane(prev_own, prev_strips_y, prev_strips_z)

    plane_rows = comps * ny
    next_fold = from_next[:plane_rows].reshape(comps, ny, nz)
    next_keep = from_next[plane_rows : plane_rows + ny]
    next_halo = from_next[plane_rows + ny :].reshape(comps, ny, nz)

    widths = ((0, 0), (0, 0), (2, 2), (2, 2))
    first = (data[:, 0] + fold_in) * keep[0]
    last = (own(data[:, n]) + next_fold) * next_keep
    return jnp.concatenate(
        [
            jnp.pad(prev_halo, widths),
            first[:, None],
            data[:, 1:n] * keep[1:n],
            jnp.pad(last[:, None], widths),
            jnp.pad(next_halo[:, None], widths),
        ],
        axis=1,
    )


def window(padded_array, axis_pos, offset):
    starts = [0, 2, 2, 2]
    limits = [
        padded_array.shape[0],
        padded_array.shape[1] - 2,
        padded_array.shape[2] - 2,
        padded_array.shape[3] - 2,
    ]
    starts[axis_pos] = offset
    limits[axis_pos] = offset + padded_array.shape[axis_pos] - 4
    return lax.slice(padded_array, tuple(starts), tuple(limits))


def stencil_apply(padded_array):
    total = 8.0 * window(padded_array, 1, 2)
    for axis_pos in (1, 2, 3):
        near = window(padded_array, axis_pos, 1) + window(padded_array, axis_pos, 3)
        far = window(padded_array, axis_pos, 0) + window(padded_array, axis_pos, 4)
        total = total - 4.0 / 3.0 * near + 1.0 / 12.0 * far
    return 0.25 * total


def body(edge_coeffs_x, edge_coeffs_y, edge_coeffs_z, flips, flags):
    closed_map, open_map = basis_tables()
    nx, ny, nz = flags.shape
    precise = lax.Precision.HIGH
    inputs = [
        (edge_coeffs_x, flips[0], open_map, closed_map, closed_map),
        (edge_coeffs_y, flips[1], closed_map, open_map, closed_map),
        (edge_coeffs_z, flips[2], closed_map, closed_map, open_map),
    ]
    keep = jnp.pad((1 - flags).astype(jnp.float32), ((0, 1), (2, 2), (2, 2)))
    boundary = [nx - 2, nx - 1, nx, 0, 1]
    slabs = []
    nodal = []
    for coef, flip, table_x, table_y, table_z in inputs:
        signed = signed_coefficients(coef, flip, table_z.shape[1])
        plane_map = plane_map_of(table_x, table_y, coef.shape[0], coef.shape[2])
        depth_map = jnp.asarray(depth_map_of(table_z, coef.shape[4]).T, jnp.float32)
        rows = plane_map.reshape(nx + 1, ny + 4, -1)[boundary].reshape(-1, plane_map.shape[1])
        edge = jnp.dot(jnp.asarray(rows, jnp.float32), signed, precision=precise)
        slabs.append(jnp.dot(edge, depth_map, precision=precise).reshape(5, ny + 4, nz + 4))
        planar = jnp.dot(jnp.asarray(plane_map, jnp.float32), signed, precision=precise)
        nodal.append(jnp.dot(planar, depth_map, precision=precise).reshape(nx + 1, ny + 4, nz + 4))
    slabs.append(keep[np.array(boundary)])
    slabs = jnp.stack(slabs)
    channels = slabs.shape[0]
    up = slabs[:, :3].reshape(channels * 3, -1)
    down = slabs[:, 3:].reshape(channels * 2, -1)
    from_prev, from_next = both_ways(up, down, "gx")
    from_prev = from_prev.reshape(channels, 3, ny + 4, nz + 4)
    from_next = from_next.reshape(channels, 2, ny + 4, nz + 4)
    partial = jnp.stack(nodal + [keep])
    extended = jnp.concatenate(
        [
            from_prev[:, 0:2],
            partial[:, 0:1] + from_prev[:, 2:3],
            partial[:, 1:nx],
            partial[:, nx : nx + 1] + from_next[:, 0:1],
            from_next[:, 1:2],
        ],
        axis=1,
    )
    extended = fold_and_halo(extended, "gz", 3)
    extended = fold_and_halo(extended, "gy", 2)
    return stencil_apply(extended[:3] * extended[3])


def solution(mesh):
    in_specs = (
        P("gx", None, "gy", None, "gz"),
        P("gx", None, "gy", None, "gz"),
        P("gx", None, "gy", None, "gz"),
        P(None, "gx", "gy", "gz"),
        P("gx", "gy", "gz"),
    )
    out_specs = P(None, "gx", "gy", "gz")
    return jax.shard_map(body, mesh=mesh, in_specs=in_specs, out_specs=out_specs, check_vma=False)
```

```python
import math

import jax
import jax.numpy as jnp
import numpy as np
from jax import lax
from jax.sharding import PartitionSpec as P


def lagrange_table(points, targets):
    table = np.ones((len(targets), len(points)))
    for row_pos in range(len(targets)):
        for col_pos in range(len(points)):
            for other in range(len(points)):
                if other != col_pos:
                    table[row_pos, col_pos] *= (targets[row_pos] - points[other]) / (
                        points[col_pos] - points[other]
                    )
    return table


def basis_tables():
    spread = math.sqrt(3.0 / 7.0)
    targets = [0.0, (1.0 - spread) / 2.0, 0.5, (1.0 + spread) / 2.0, 1.0]
    closed = [0.0, 0.25, 0.5, 0.75, 1.0]
    inner = math.sqrt(3.0 / 7.0 - 2.0 / 7.0 * math.sqrt(6.0 / 5.0))
    outer = math.sqrt(3.0 / 7.0 + 2.0 / 7.0 * math.sqrt(6.0 / 5.0))
    gauss = [(1.0 - outer) / 2.0, (1.0 - inner) / 2.0, (1.0 + inner) / 2.0, (1.0 + outer) / 2.0]
    closed_map = np.asarray(lagrange_table(closed, targets), dtype=np.float32).astype(np.float64)
    open_map = np.asarray(lagrange_table(gauss, targets), dtype=np.float32).astype(np.float64)
    return closed_map, open_map


def assembly_matrix(table, count):
    size = table.shape[1]
    matrix = np.zeros((4 * count + 1, count * size))
    for elem_pos in range(count):
        matrix[4 * elem_pos : 4 * elem_pos + 5, size * elem_pos : size * elem_pos + size] += table
    return matrix


def planar_part(coef, flip, table_x, table_y, size_z):
    ex_count, size_x, ey_count, size_y, merged = coef.shape
    orient = jnp.repeat((1 - 2 * flip).astype(jnp.float32), size_z, axis=2)
    signed = (coef * orient[:, None, :, None, :]).reshape(ex_count * size_x * ey_count * size_y, merged)
    rows_y = np.pad(assembly_matrix(table_y, ey_count), ((2, 1), (0, 0)))
    plane_map = np.kron(assembly_matrix(table_x, ex_count), rows_y)
    return jnp.dot(jnp.asarray(plane_map, jnp.float32), signed, precision=lax.Precision.HIGH)


def depth_map_of(table_z, merged):
    return np.pad(assembly_matrix(table_z, merged // table_z.shape[1]), ((2, 1), (0, 0)))


def shifted(block, axis, step=1):
    count = lax.axis_size(axis)
    if count == 1:
        return block
    return lax.ppermute(block, axis, [(i, (i + step) % count) for i in range(count)])


def both_ways(up, down, axis):
    if lax.axis_size(axis) <= 2:
        both = shifted(jnp.concatenate([up, down]), axis)
        return both[: up.shape[0]], both[up.shape[0] :]
    return shifted(up, axis), shifted(down, axis, -1)


def to_wire(slab, dim):
    layers = jnp.moveaxis(slab, dim, 0)
    return layers.reshape(layers.shape[0] * layers.shape[1], -1), layers.shape


def from_wire(rows, shape, dim):
    return jnp.moveaxis(rows.reshape(shape), 0, dim)


def fold_and_halo(extended, axis, dim):
    length = extended.shape[dim]
    n = length - 4
    up, up_shape = to_wire(lax.slice_in_dim(extended, n, n + 3, axis=dim), dim)
    down, down_shape = to_wire(lax.slice_in_dim(extended, 2, 4, axis=dim), dim)
    from_prev, from_next = both_ways(up, down, axis)
    widths_prev = [(0, 0)] * extended.ndim
    widths_prev[dim] = (0, length - 3)
    widths_next = [(0, 0)] * extended.ndim
    widths_next[dim] = (n + 2, 0)
    return (
        extended
        + jnp.pad(from_wire(from_prev, up_shape, dim), widths_prev)
        + jnp.pad(from_wire(from_next, down_shape, dim), widths_next)
    )


def cross_rows(plane, ny, nz):
    own = plane[:, 2 : ny + 2, 2 : nz + 2]
    strips_y = jnp.concatenate([plane[:, 0:2, 2 : nz + 2], plane[:, ny + 2 :, 2 : nz + 2]], axis=1)
    strips_z = jnp.concatenate([plane[:, 2 : ny + 2, 0:2], plane[:, 2 : ny + 2, nz + 2 :]], axis=2)
    strips_z = jnp.swapaxes(strips_z, 1, 2).reshape(-1)
    strips_z = jnp.pad(strips_z, (0, -strips_z.shape[0] % nz))
    return [own.reshape(-1, nz), strips_y.reshape(-1, nz), strips_z.reshape(-1, nz)]


def cross_plane(own, strips_y, strips_z):
    middle = jnp.concatenate([strips_z[..., 0:2], own, strips_z[..., 2:4]], axis=2)
    widths = ((0, 0), (0, 0), (2, 2))
    return jnp.concatenate(
        [jnp.pad(strips_y[:, 0:2], widths), middle, jnp.pad(strips_y[:, 2:4], widths)], axis=1
    )


def last_round_and_stencil(extended, axis, ny, nz):
    n = extended.shape[1] - 1
    comps = extended.shape[0] - 1
    data = extended[:comps]
    keep = extended[comps]

    def own(block):
        return block[..., 2 : ny + 2, 2 : nz + 2]

    halo_up = own(data[:, n - 2 : n] * keep[n - 2 : n])
    halo_down = own(data[:, 1] * keep[1])
    up_parts = [halo_up.reshape(-1, nz)] + cross_rows(data[:, n], ny, nz)
    down_parts = [own(data[:, 0]).reshape(-1, nz), own(keep[0]), halo_down.reshape(-1, nz)]
    up = jnp.concatenate(up_parts)
    down = jnp.concatenate(down_parts)
    from_prev, from_next = both_ways(up, down, axis)

    sizes = [part.shape[0] for part in up_parts]
    marks = np.cumsum([0] + sizes)
    prev_halo = from_prev[marks[0] : marks[1]].reshape(comps, 2, ny, nz)
    prev_own = from_prev[marks[1] : marks[2]].reshape(comps, ny, nz)
    prev_strips_y = from_prev[marks[2] : marks[3]].reshape(comps, 4, nz)
    prev_strips_z = from_prev[marks[3] : marks[4]].reshape(-1)[: comps * 4 * ny]
    prev_strips_z = jnp.swapaxes(prev_strips_z.reshape(comps, 4, ny), 1, 2)
    fold_in = cross_plane(prev_own, prev_strips_y, prev_strips_z)

    plane_rows = comps * ny
    next_fold = from_next[:plane_rows].reshape(comps, ny, nz)
    next_keep = from_next[plane_rows : plane_rows + ny]
    next_halo = from_next[plane_rows + ny :].reshape(comps, ny, nz)

    inner = data[:, 1:n] * keep[1:n]
    first = (data[:, 0] + fold_in) * keep[0]
    last = (own(data[:, n]) + next_fold) * next_keep
    across = jnp.concatenate([yz_terms(first[:, None], ny, nz), yz_terms(inner, ny, nz)], axis=1)
    column = jnp.concatenate(
        [prev_halo, own(first)[:, None], own(inner), last[:, None], next_halo[:, None]], axis=1
    )
    near = column[:, 1 : n + 1] + column[:, 3 : n + 3]
    far = column[:, 0:n] + column[:, 4 : n + 4]
    return 0.25 * (across - 4.0 / 3.0 * near + 1.0 / 12.0 * far)


def yz_terms(block, ny, nz):
    def part(dy, dz):
        return block[..., 2 + dy : ny + 2 + dy, 2 + dz : nz + 2 + dz]

    near = part(-1, 0) + part(1, 0) + part(0, -1) + part(0, 1)
    far = part(-2, 0) + part(2, 0) + part(0, -2) + part(0, 2)
    return 8.0 * part(0, 0) - 4.0 / 3.0 * near + 1.0 / 12.0 * far


def body(edge_coeffs_x, edge_coeffs_y, edge_coeffs_z, flips, flags):
    closed_map, open_map = basis_tables()
    nx, ny, nz = flags.shape
    precise = lax.Precision.HIGHEST
    inputs = [
        (edge_coeffs_x, flips[0], open_map, closed_map, closed_map),
        (edge_coeffs_y, flips[1], closed_map, open_map, closed_map),
        (edge_coeffs_z, flips[2], closed_map, closed_map, open_map),
    ]
    length = nz + 4
    up_places = [nz, nz + 1, nz + 2]
    down_places = [2, 3]
    planars = []
    depths = []
    slabs = []
    for coef, flip, table_x, table_y, table_z in inputs:
        planar = planar_part(coef, flip, table_x, table_y, table_z.shape[1])
        depth_map = depth_map_of(table_z, coef.shape[4])
        edge_map = jnp.asarray(depth_map[up_places + down_places], jnp.float32)
        planars.append(planar)
        depths.append(depth_map)
        slabs.append(
            lax.dot_general(edge_map, planar, (((1,), (1,)), ((), ())), precision=lax.Precision.HIGH)
        )
    keep_own = (1 - flags).astype(jnp.float32)
    keep = jnp.pad(keep_own, ((0, 1), (2, 2), (2, 2)))
    keep_layers = [
        lax.slice_in_dim(keep_own, nz - 2, nz, axis=2),
        jnp.zeros_like(lax.slice_in_dim(keep_own, 0, 1, axis=2)),
        lax.slice_in_dim(keep_own, 0, 2, axis=2),
    ]
    keep_layers = jnp.moveaxis(jnp.concatenate(keep_layers, axis=2), 2, 0)
    slabs.append(jnp.pad(keep_layers, ((0, 0), (0, 1), (2, 2))).reshape(5, -1))
    slabs = jnp.stack(slabs)
    up = slabs[:, :3].reshape(-1, slabs.shape[2])
    down = slabs[:, 3:].reshape(-1, slabs.shape[2])
    from_prev, from_next = both_ways(up, down, "gz")
    arrived = jnp.concatenate(
        [from_prev.reshape(4, 3, -1), from_next.reshape(4, 2, -1)], axis=1
    )
    place = np.zeros((5, length))
    for row, col in enumerate([0, 1, 2, nz + 2, nz + 3]):
        place[row, col] = 1.0
    place = jnp.asarray(place, jnp.float32)
    nodal = []
    for comp in range(3):
        own_part = jnp.dot(
            planars[comp], jnp.asarray(depths[comp].T, jnp.float32), precision=lax.Precision.HIGH
        )
        folded = lax.dot_general(arrived[comp], place, (((0,), (0,)), ((), ())), precision=precise)
        nodal.append((own_part + folded).reshape(nx + 1, ny + 4, length))
    keep_in = jnp.moveaxis(arrived[3].reshape(5, nx + 1, ny + 4), 0, 2)
    keep = keep + jnp.pad(keep_in[..., :3], ((0, 0), (0, 0), (0, length - 3))) + jnp.pad(
        keep_in[..., 3:], ((0, 0), (0, 0), (nz + 2, 0))
    )
    extended = jnp.stack(nodal + [keep])
    extended = fold_and_halo(extended, "gy", 2)
    return last_round_and_stencil(extended, "gx", ny, nz)


def solution(mesh):
    in_specs = (
        P("gx", None, "gy", None, "gz"),
        P("gx", None, "gy", None, "gz"),
        P("gx", None, "gy", None, "gz"),
        P(None, "gx", "gy", "gz"),
        P("gx", "gy", "gz"),
    )
    out_specs = P(None, "gx", "gy", "gz")
    return jax.shard_map(body, mesh=mesh, in_specs=in_specs, out_specs=out_specs, check_vma=False)
```

```python
import math

import jax
import jax.numpy as jnp
import numpy as np
from jax import lax
from jax.sharding import PartitionSpec as P


def lagrange_table(points, targets):
    table = np.ones((len(targets), len(points)))
    for row_pos in range(len(targets)):
        for col_pos in range(len(points)):
            for other in range(len(points)):
                if other != col_pos:
                    table[row_pos, col_pos] *= (targets[row_pos] - points[other]) / (
                        points[col_pos] - points[other]
                    )
    return table


def basis_tables():
    spread = math.sqrt(3.0 / 7.0)
    targets = [0.0, (1.0 - spread) / 2.0, 0.5, (1.0 + spread) / 2.0, 1.0]
    closed = [0.0, 0.25, 0.5, 0.75, 1.0]
    inner = math.sqrt(3.0 / 7.0 - 2.0 / 7.0 * math.sqrt(6.0 / 5.0))
    outer = math.sqrt(3.0 / 7.0 + 2.0 / 7.0 * math.sqrt(6.0 / 5.0))
    gauss = [(1.0 - outer) / 2.0, (1.0 - inner) / 2.0, (1.0 + inner) / 2.0, (1.0 + outer) / 2.0]
    closed_map = np.asarray(lagrange_table(closed, targets), dtype=np.float32).astype(np.float64)
    open_map = np.asarray(lagrange_table(gauss, targets), dtype=np.float32).astype(np.float64)
    return closed_map, open_map


def assembly_matrix(table, count):
    size = table.shape[1]
    matrix = np.zeros((4 * count + 1, count * size))
    for elem_pos in range(count):
        matrix[4 * elem_pos : 4 * elem_pos + 5, size * elem_pos : size * elem_pos + size] += table
    return matrix


def planar_part(coef, flip, table_x, table_y, size_z):
    ex_count, size_x, ey_count, size_y, merged = coef.shape
    orient = jnp.repeat((1 - 2 * flip).astype(jnp.float32), size_z, axis=2)
    signed = (coef * orient[:, None, :, None, :]).reshape(ex_count * size_x * ey_count * size_y, merged)
    rows_y = np.pad(assembly_matrix(table_y, ey_count), ((2, 1), (0, 0)))
    plane_map = np.kron(assembly_matrix(table_x, ex_count), rows_y)
    return jnp.dot(jnp.asarray(plane_map, jnp.float32), signed, precision=lax.Precision.HIGH)


def depth_map_of(table_z, merged):
    return np.pad(assembly_matrix(table_z, merged // table_z.shape[1]), ((2, 1), (0, 0)))


def shifted(block, axis, step=1):
    count = lax.axis_size(axis)
    if count == 1:
        return block
    return lax.ppermute(block, axis, [(i, (i + step) % count) for i in range(count)])


def both_ways(up, down, axis):
    if lax.axis_size(axis) <= 2:
        both = shifted(jnp.concatenate([up, down]), axis)
        return both[: up.shape[0]], both[up.shape[0] :]
    return shifted(up, axis), shifted(down, axis, -1)


def to_wire(slab, dim):
    layers = jnp.moveaxis(slab, dim, 0)
    return layers.reshape(layers.shape[0] * layers.shape[1], -1), layers.shape


def from_wire(rows, shape, dim):
    return jnp.moveaxis(rows.reshape(shape), 0, dim)


def fold_and_halo(extended, axis, dim):
    length = extended.shape[dim]
    n = length - 4
    up, up_shape = to_wire(lax.slice_in_dim(extended, n, n + 3, axis=dim), dim)
    down, down_shape = to_wire(lax.slice_in_dim(extended, 2, 4, axis=dim), dim)
    from_prev, from_next = both_ways(up, down, axis)
    widths_prev = [(0, 0)] * extended.ndim
    widths_prev[dim] = (0, length - 3)
    widths_next = [(0, 0)] * extended.ndim
    widths_next[dim] = (n + 2, 0)
    return (
        extended
        + jnp.pad(from_wire(from_prev, up_shape, dim), widths_prev)
        + jnp.pad(from_wire(from_next, down_shape, dim), widths_next)
    )


def cross_rows(plane, ny, nz):
    own = plane[:, 2 : ny + 2, 2 : nz + 2]
    strips_y = jnp.concatenate([plane[:, 0:2, 2 : nz + 2], plane[:, ny + 2 :, 2 : nz + 2]], axis=1)
    strips_z = jnp.concatenate([plane[:, 2 : ny + 2, 0:2], plane[:, 2 : ny + 2, nz + 2 :]], axis=2)
    strips_z = jnp.swapaxes(strips_z, 1, 2).reshape(-1)
    strips_z = jnp.pad(strips_z, (0, -strips_z.shape[0] % nz))
    return [own.reshape(-1, nz), strips_y.reshape(-1, nz), strips_z.reshape(-1, nz)]


def cross_plane(own, strips_y, strips_z):
    middle = jnp.concatenate([strips_z[..., 0:2], own, strips_z[..., 2:4]], axis=2)
    widths = ((0, 0), (0, 0), (2, 2))
    return jnp.concatenate(
        [jnp.pad(strips_y[:, 0:2], widths), middle, jnp.pad(strips_y[:, 2:4], widths)], axis=1
    )


def last_round_and_stencil(extended, axis, ny, nz):
    n = extended.shape[1] - 1
    comps = extended.shape[0] - 1
    data = extended[:comps]
    keep = extended[comps]

    def own(block):
        return block[..., 2 : ny + 2, 2 : nz + 2]

    halo_up = own(data[:, n - 2 : n] * keep[n - 2 : n])
    halo_down = own(data[:, 1] * keep[1])
    up_parts = [halo_up.reshape(-1, nz)] + cross_rows(data[:, n], ny, nz)
    down_parts = [own(data[:, 0]).reshape(-1, nz), own(keep[0]), halo_down.reshape(-1, nz)]
    up = jnp.concatenate(up_parts)
    down = jnp.concatenate(down_parts)
    from_prev, from_next = both_ways(up, down, axis)

    sizes = [part.shape[0] for part in up_parts]
    marks = np.cumsum([0] + sizes)
    prev_halo = from_prev[marks[0] : marks[1]].reshape(comps, 2, ny, nz)
    prev_own = from_prev[marks[1] : marks[2]].reshape(comps, ny, nz)
    prev_strips_y = from_prev[marks[2] : marks[3]].reshape(comps, 4, nz)
    prev_strips_z = from_prev[marks[3] : marks[4]].reshape(-1)[: comps * 4 * ny]
    prev_strips_z = jnp.swapaxes(prev_strips_z.reshape(comps, 4, ny), 1, 2)
    fold_in = cross_plane(prev_own, prev_strips_y, prev_strips_z)

    plane_rows = comps * ny
    next_fold = from_next[:plane_rows].reshape(comps, ny, nz)
    next_keep = from_next[plane_rows : plane_rows + ny]
    next_halo = from_next[plane_rows + ny :].reshape(comps, ny, nz)

    inner = data[:, 1:n] * keep[1:n]
    first = (data[:, 0] + fold_in) * keep[0]
    last = (own(data[:, n]) + next_fold) * next_keep
    across = jnp.concatenate([yz_terms(first[:, None], ny, nz), yz_terms(inner, ny, nz)], axis=1)
    column = jnp.concatenate(
        [prev_halo, own(first)[:, None], own(inner), last[:, None], next_halo[:, None]], axis=1
    )
    near = column[:, 1 : n + 1] + column[:, 3 : n + 3]
    far = column[:, 0:n] + column[:, 4 : n + 4]
    return 0.25 * (across - 4.0 / 3.0 * near + 1.0 / 12.0 * far)


def yz_terms(block, ny, nz):
    def part(dy, dz):
        return block[..., 2 + dy : ny + 2 + dy, 2 + dz : nz + 2 + dz]

    near = part(-1, 0) + part(1, 0) + part(0, -1) + part(0, 1)
    far = part(-2, 0) + part(2, 0) + part(0, -2) + part(0, 2)
    return 8.0 * part(0, 0) - 4.0 / 3.0 * near + 1.0 / 12.0 * far


def body(edge_coeffs_x, edge_coeffs_y, edge_coeffs_z, flips, flags):
    closed_map, open_map = basis_tables()
    nx, ny, nz = flags.shape
    precise = lax.Precision.HIGHEST
    inputs = [
        (edge_coeffs_x, flips[0], open_map, closed_map, closed_map),
        (edge_coeffs_y, flips[1], closed_map, open_map, closed_map),
        (edge_coeffs_z, flips[2], closed_map, closed_map, open_map),
    ]
    length = nz + 4
    up_places = [nz, nz + 1, nz + 2]
    down_places = [2, 3]
    planars = []
    depths = []
    slabs = []
    for coef, flip, table_x, table_y, table_z in inputs:
        planar = planar_part(coef, flip, table_x, table_y, table_z.shape[1])
        depth_map = depth_map_of(table_z, coef.shape[4])
        edge_map = jnp.asarray(depth_map[up_places + down_places], jnp.float32)
        planars.append(planar)
        depths.append(depth_map)
        slabs.append(
            lax.dot_general(edge_map, planar, (((1,), (1,)), ((), ())), precision=lax.Precision.HIGH)
        )
    keep_own = (1 - flags).astype(jnp.float32)
    keep = jnp.pad(keep_own, ((0, 1), (2, 2), (2, 2)))
    keep_layers = [
        lax.slice_in_dim(keep_own, nz - 2, nz, axis=2),
        jnp.zeros_like(lax.slice_in_dim(keep_own, 0, 1, axis=2)),
        lax.slice_in_dim(keep_own, 0, 2, axis=2),
    ]
    keep_layers = jnp.moveaxis(jnp.concatenate(keep_layers, axis=2), 2, 0)
    slabs.append(jnp.pad(keep_layers, ((0, 0), (0, 1), (2, 2))).reshape(5, -1))
    slabs = jnp.stack(slabs)
    up = slabs[:, :3].reshape(-1, slabs.shape[2])
    down = slabs[:, 3:].reshape(-1, slabs.shape[2])
    from_prev, from_next = both_ways(up, down, "gz")
    own_parts = lax.optimization_barrier(
        [
            jnp.dot(planar, jnp.asarray(depth.T, jnp.float32), precision=lax.Precision.HIGH)
            for planar, depth in zip(planars, depths)
        ]
    )
    arrived = jnp.concatenate(
        [from_prev.reshape(4, 3, -1), from_next.reshape(4, 2, -1)], axis=1
    )
    place = np.zeros((5, length))
    for row, col in enumerate([0, 1, 2, nz + 2, nz + 3]):
        place[row, col] = 1.0
    place = jnp.asarray(place, jnp.float32)
    nodal = []
    for comp in range(3):
        folded = lax.dot_general(arrived[comp], place, (((0,), (0,)), ((), ())), precision=precise)
        nodal.append((own_parts[comp] + folded).reshape(nx + 1, ny + 4, length))
    keep_in = jnp.moveaxis(arrived[3].reshape(5, nx + 1, ny + 4), 0, 2)
    keep = keep + jnp.pad(keep_in[..., :3], ((0, 0), (0, 0), (0, length - 3))) + jnp.pad(
        keep_in[..., 3:], ((0, 0), (0, 0), (nz + 2, 0))
    )
    extended = jnp.stack(nodal + [keep])
    extended = fold_and_halo(extended, "gy", 2)
    return last_round_and_stencil(extended, "gx", ny, nz)


def solution(mesh):
    in_specs = (
        P("gx", None, "gy", None, "gz"),
        P("gx", None, "gy", None, "gz"),
        P("gx", None, "gy", None, "gz"),
        P(None, "gx", "gy", "gz"),
        P("gx", "gy", "gz"),
    )
    out_specs = P(None, "gx", "gy", "gz")
    return jax.shard_map(body, mesh=mesh, in_specs=in_specs, out_specs=out_specs, check_vma=False)
```

```python
import math

import jax
import jax.numpy as jnp
import numpy as np
from jax import lax
from jax.sharding import PartitionSpec as P


def lagrange_table(points, targets):
    table = np.ones((len(targets), len(points)))
    for row_pos in range(len(targets)):
        for col_pos in range(len(points)):
            for other in range(len(points)):
                if other != col_pos:
                    table[row_pos, col_pos] *= (targets[row_pos] - points[other]) / (
                        points[col_pos] - points[other]
                    )
    return table


def basis_tables():
    spread = math.sqrt(3.0 / 7.0)
    targets = [0.0, (1.0 - spread) / 2.0, 0.5, (1.0 + spread) / 2.0, 1.0]
    closed = [0.0, 0.25, 0.5, 0.75, 1.0]
    inner = math.sqrt(3.0 / 7.0 - 2.0 / 7.0 * math.sqrt(6.0 / 5.0))
    outer = math.sqrt(3.0 / 7.0 + 2.0 / 7.0 * math.sqrt(6.0 / 5.0))
    gauss = [(1.0 - outer) / 2.0, (1.0 - inner) / 2.0, (1.0 + inner) / 2.0, (1.0 + outer) / 2.0]
    closed_map = np.asarray(lagrange_table(closed, targets), dtype=np.float32).astype(np.float64)
    open_map = np.asarray(lagrange_table(gauss, targets), dtype=np.float32).astype(np.float64)
    return closed_map, open_map


def assembly_matrix(table, count):
    size = table.shape[1]
    matrix = np.zeros((4 * count + 1, count * size))
    for elem_pos in range(count):
        matrix[4 * elem_pos : 4 * elem_pos + 5, size * elem_pos : size * elem_pos + size] += table
    return matrix


def planar_part(coef, flip, table_x, table_y, size_z):
    ex_count, size_x, ey_count, size_y, merged = coef.shape
    orient = jnp.repeat((1 - 2 * flip).astype(jnp.float32), size_z, axis=2)
    signed = (coef * orient[:, None, :, None, :]).reshape(ex_count * size_x * ey_count * size_y, merged)
    rows_y = np.pad(assembly_matrix(table_y, ey_count), ((2, 1), (0, 0)))
    plane_map = np.kron(assembly_matrix(table_x, ex_count), rows_y)
    return jnp.dot(jnp.asarray(plane_map, jnp.float32), signed, precision=lax.Precision.HIGH)


def depth_map_of(table_z, merged):
    return np.pad(assembly_matrix(table_z, merged // table_z.shape[1]), ((2, 1), (0, 0)))


def shifted(block, axis, step=1):
    count = lax.axis_size(axis)
    if count == 1:
        return block
    return lax.ppermute(block, axis, [(i, (i + step) % count) for i in range(count)])


def both_ways(up, down, axis):
    if lax.axis_size(axis) <= 2:
        both = shifted(jnp.concatenate([up, down]), axis)
        return both[: up.shape[0]], both[up.shape[0] :]
    return shifted(up, axis), shifted(down, axis, -1)


def to_wire(slab, dim):
    layers = jnp.moveaxis(slab, dim, 0)
    return layers.reshape(layers.shape[0] * layers.shape[1], -1), layers.shape


def from_wire(rows, shape, dim):
    return jnp.moveaxis(rows.reshape(shape), 0, dim)


def fold_and_halo(extended, axis, dim):
    length = extended.shape[dim]
    n = length - 4
    up, up_shape = to_wire(lax.slice_in_dim(extended, n, n + 3, axis=dim), dim)
    down, down_shape = to_wire(lax.slice_in_dim(extended, 2, 4, axis=dim), dim)
    from_prev, from_next = both_ways(up, down, axis)
    widths_prev = [(0, 0)] * extended.ndim
    widths_prev[dim] = (0, length - 3)
    widths_next = [(0, 0)] * extended.ndim
    widths_next[dim] = (n + 2, 0)
    return (
        extended
        + jnp.pad(from_wire(from_prev, up_shape, dim), widths_prev)
        + jnp.pad(from_wire(from_next, down_shape, dim), widths_next)
    )


def cross_rows(plane, ny, nz):
    own = plane[:, 2 : ny + 2, 2 : nz + 2]
    strips_y = jnp.concatenate([plane[:, 0:2, 2 : nz + 2], plane[:, ny + 2 :, 2 : nz + 2]], axis=1)
    strips_z = jnp.concatenate([plane[:, 2 : ny + 2, 0:2], plane[:, 2 : ny + 2, nz + 2 :]], axis=2)
    strips_z = jnp.swapaxes(strips_z, 1, 2).reshape(-1)
    strips_z = jnp.pad(strips_z, (0, -strips_z.shape[0] % nz))
    return [own.reshape(-1, nz), strips_y.reshape(-1, nz), strips_z.reshape(-1, nz)]


def cross_plane(own, strips_y, strips_z):
    middle = jnp.concatenate([strips_z[..., 0:2], own, strips_z[..., 2:4]], axis=2)
    widths = ((0, 0), (0, 0), (2, 2))
    return jnp.concatenate(
        [jnp.pad(strips_y[:, 0:2], widths), middle, jnp.pad(strips_y[:, 2:4], widths)], axis=1
    )


def last_round_and_stencil(extended, axis, ny, nz):
    n = extended.shape[1] - 1
    comps = extended.shape[0] - 1
    data = extended[:comps]
    keep = extended[comps]

    def own(block):
        return block[..., 2 : ny + 2, 2 : nz + 2]

    halo_up = own(data[:, n - 2 : n] * keep[n - 2 : n])
    halo_down = own(data[:, 1] * keep[1])
    up_parts = [halo_up.reshape(-1, nz)] + cross_rows(data[:, n], ny, nz)
    down_parts = [own(data[:, 0]).reshape(-1, nz), own(keep[0]), halo_down.reshape(-1, nz)]
    up = jnp.concatenate(up_parts)
    down = jnp.concatenate(down_parts)
    from_prev, from_next = both_ways(up, down, axis)

    sizes = [part.shape[0] for part in up_parts]
    marks = np.cumsum([0] + sizes)
    prev_halo = from_prev[marks[0] : marks[1]].reshape(comps, 2, ny, nz)
    prev_own = from_prev[marks[1] : marks[2]].reshape(comps, ny, nz)
    prev_strips_y = from_prev[marks[2] : marks[3]].reshape(comps, 4, nz)
    prev_strips_z = from_prev[marks[3] : marks[4]].reshape(-1)[: comps * 4 * ny]
    prev_strips_z = jnp.swapaxes(prev_strips_z.reshape(comps, 4, ny), 1, 2)
    fold_in = cross_plane(prev_own, prev_strips_y, prev_strips_z)

    plane_rows = comps * ny
    next_fold = from_next[:plane_rows].reshape(comps, ny, nz)
    next_keep = from_next[plane_rows : plane_rows + ny]
    next_halo = from_next[plane_rows + ny :].reshape(comps, ny, nz)

    inner = data[:, 1:n] * keep[1:n]
    first = (data[:, 0] + fold_in) * keep[0]
    last = (own(data[:, n]) + next_fold) * next_keep
    across = jnp.concatenate([yz_terms(first[:, None], ny, nz), yz_terms(inner, ny, nz)], axis=1)
    column = jnp.concatenate(
        [prev_halo, own(first)[:, None], own(inner), last[:, None], next_halo[:, None]], axis=1
    )
    near = column[:, 1 : n + 1] + column[:, 3 : n + 3]
    far = column[:, 0:n] + column[:, 4 : n + 4]
    return 0.25 * (across - 4.0 / 3.0 * near + 1.0 / 12.0 * far)


def yz_terms(block, ny, nz):
    def part(dy, dz):
        return block[..., 2 + dy : ny + 2 + dy, 2 + dz : nz + 2 + dz]

    near = part(-1, 0) + part(1, 0) + part(0, -1) + part(0, 1)
    far = part(-2, 0) + part(2, 0) + part(0, -2) + part(0, 2)
    return 8.0 * part(0, 0) - 4.0 / 3.0 * near + 1.0 / 12.0 * far


def window(padded_array, axis_pos, offset):
    starts = [0, 2, 2, 2]
    limits = [
        padded_array.shape[0],
        padded_array.shape[1] - 2,
        padded_array.shape[2] - 2,
        padded_array.shape[3] - 2,
    ]
    starts[axis_pos] = offset
    limits[axis_pos] = offset + padded_array.shape[axis_pos] - 4
    return lax.slice(padded_array, tuple(starts), tuple(limits))


def stencil_apply(padded_array):
    total = 8.0 * window(padded_array, 1, 2)
    for axis_pos in (1, 2, 3):
        near = window(padded_array, axis_pos, 1) + window(padded_array, axis_pos, 3)
        far = window(padded_array, axis_pos, 0) + window(padded_array, axis_pos, 4)
        total = total - 4.0 / 3.0 * near + 1.0 / 12.0 * far
    return 0.25 * total


def exchange(payloads, axes):
    sizes = [lax.axis_size(axis) for axis in axes]
    groups = {}
    for offset in payloads:
        key = tuple(o % s for o, s in zip(offset, sizes))
        groups.setdefault(key, []).append(offset)
    arrived = {}
    for key, offsets in groups.items():
        flat = jnp.concatenate([payloads[offset].reshape(-1) for offset in offsets])
        length = flat.shape[0]
        rows = jnp.pad(flat, (0, -length % 128)).reshape(-1, 128)
        if any(key):
            pairs = []
            for source in np.ndindex(*sizes):
                target = tuple((c + k) % s for c, k, s in zip(source, key, sizes))
                pairs.append((int(np.ravel_multi_index(source, sizes)), int(np.ravel_multi_index(target, sizes))))
            rows = lax.ppermute(rows, tuple(axes), pairs)
        flat = rows.reshape(-1)
        start = 0
        for offset in offsets:
            shape = payloads[offset].shape
            size = int(np.prod(shape))
            arrived[offset] = flat[start : start + size].reshape(shape)
            start += size
    return arrived


def placed(block, starts, shape):
    return jnp.pad(block, [(b, s - b - d) for b, d, s in zip(starts, block.shape, shape)])


def plane_round_and_stencil(extended, nx, ny):
    e = extended
    payloads = {
        (1, 0): e[:, nx - 2 : nx + 1, 2 : ny + 3],
        (-1, 0): e[:, 0:2, 2 : ny + 2],
        (0, 1): e[:, :, ny : ny + 3],
        (0, -1): e[:, 0:nx, 2:4],
        (1, 1): jnp.concatenate([e[:, nx - 2 : nx + 1, ny + 2], e[:, nx, ny : ny + 2]], axis=1),
        (-1, 1): e[:, 0:2, ny + 2],
        (1, -1): e[:, nx, 2:4],
    }
    got = exchange(payloads, ("gx", "gy"))
    channels, _, _, depth = e.shape
    shape = (channels, nx + 4, ny + 4, depth)

    def at(block, layer, row):
        return placed(block, (0, layer, row, 0), shape)

    corner = got[(1, 1)]
    total = (
        at(e, 2, 0)
        + at(got[(1, 0)], 0, 2)
        + at(got[(-1, 0)], nx + 2, 2)
        + at(got[(0, 1)], 2, 0)
        + at(got[(0, -1)], 2, ny + 2)
        + at(corner[:, 0:3, None], 0, 2)
        + at(corner[:, 3:5, :][:, None], 2, 0)
        + at(got[(-1, 1)][:, :, None], nx + 2, 2)
        + at(got[(1, -1)][:, None], 2, ny + 2)
    )
    return stencil_apply(total[:-1] * total[-1])


def body(edge_coeffs_x, edge_coeffs_y, edge_coeffs_z, flips, flags):
    closed_map, open_map = basis_tables()
    nx, ny, nz = flags.shape
    precise = lax.Precision.HIGHEST
    inputs = [
        (edge_coeffs_x, flips[0], open_map, closed_map, closed_map),
        (edge_coeffs_y, flips[1], closed_map, open_map, closed_map),
        (edge_coeffs_z, flips[2], closed_map, closed_map, open_map),
    ]
    length = nz + 4
    up_places = [nz, nz + 1, nz + 2]
    down_places = [2, 3]
    planars = []
    depths = []
    slabs = []
    for coef, flip, table_x, table_y, table_z in inputs:
        planar = planar_part(coef, flip, table_x, table_y, table_z.shape[1])
        depth_map = depth_map_of(table_z, coef.shape[4])
        edge_map = jnp.asarray(depth_map[up_places + down_places], jnp.float32)
        planars.append(planar)
        depths.append(depth_map)
        slabs.append(
            lax.dot_general(edge_map, planar, (((1,), (1,)), ((), ())), precision=lax.Precision.HIGH)
        )
    keep_own = (1 - flags).astype(jnp.float32)
    keep = jnp.pad(keep_own, ((0, 1), (2, 2), (2, 2)))
    keep_layers = [
        lax.slice_in_dim(keep_own, nz - 2, nz, axis=2),
        jnp.zeros_like(lax.slice_in_dim(keep_own, 0, 1, axis=2)),
        lax.slice_in_dim(keep_own, 0, 2, axis=2),
    ]
    keep_layers = jnp.moveaxis(jnp.concatenate(keep_layers, axis=2), 2, 0)
    slabs.append(jnp.pad(keep_layers, ((0, 0), (0, 1), (2, 2))).reshape(5, -1))
    slabs = jnp.stack(slabs)
    up = slabs[:, :3].reshape(-1, slabs.shape[2])
    down = slabs[:, 3:].reshape(-1, slabs.shape[2])
    from_prev, from_next = both_ways(up, down, "gz")
    own_parts = lax.optimization_barrier(
        [
            jnp.dot(planar, jnp.asarray(depth.T, jnp.float32), precision=lax.Precision.HIGH)
            for planar, depth in zip(planars, depths)
        ]
    )
    arrived = jnp.concatenate(
        [from_prev.reshape(4, 3, -1), from_next.reshape(4, 2, -1)], axis=1
    )
    place = np.zeros((5, length))
    for row, col in enumerate([0, 1, 2, nz + 2, nz + 3]):
        place[row, col] = 1.0
    place = jnp.asarray(place, jnp.float32)
    nodal = []
    for comp in range(3):
        folded = lax.dot_general(arrived[comp], place, (((0,), (0,)), ((), ())), precision=precise)
        nodal.append((own_parts[comp] + folded).reshape(nx + 1, ny + 4, length))
    keep_in = jnp.moveaxis(arrived[3].reshape(5, nx + 1, ny + 4), 0, 2)
    keep = keep + jnp.pad(keep_in[..., :3], ((0, 0), (0, 0), (0, length - 3))) + jnp.pad(
        keep_in[..., 3:], ((0, 0), (0, 0), (nz + 2, 0))
    )
    extended = jnp.stack(nodal + [keep])
    return plane_round_and_stencil(extended, nx, ny)


def solution(mesh):
    in_specs = (
        P("gx", None, "gy", None, "gz"),
        P("gx", None, "gy", None, "gz"),
        P("gx", None, "gy", None, "gz"),
        P(None, "gx", "gy", "gz"),
        P("gx", "gy", "gz"),
    )
    out_specs = P(None, "gx", "gy", "gz")
    return jax.shard_map(body, mesh=mesh, in_specs=in_specs, out_specs=out_specs, check_vma=False)
```

```python
import math

import jax
import jax.numpy as jnp
import numpy as np
from jax import lax
from jax.sharding import PartitionSpec as P


def lagrange_table(points, targets):
    table = np.ones((len(targets), len(points)))
    for row_pos in range(len(targets)):
        for col_pos in range(len(points)):
            for other in range(len(points)):
                if other != col_pos:
                    table[row_pos, col_pos] *= (targets[row_pos] - points[other]) / (
                        points[col_pos] - points[other]
                    )
    return table


def basis_tables():
    spread = math.sqrt(3.0 / 7.0)
    targets = [0.0, (1.0 - spread) / 2.0, 0.5, (1.0 + spread) / 2.0, 1.0]
    closed = [0.0, 0.25, 0.5, 0.75, 1.0]
    inner = math.sqrt(3.0 / 7.0 - 2.0 / 7.0 * math.sqrt(6.0 / 5.0))
    outer = math.sqrt(3.0 / 7.0 + 2.0 / 7.0 * math.sqrt(6.0 / 5.0))
    gauss = [(1.0 - outer) / 2.0, (1.0 - inner) / 2.0, (1.0 + inner) / 2.0, (1.0 + outer) / 2.0]
    closed_map = np.asarray(lagrange_table(closed, targets), dtype=np.float32).astype(np.float64)
    open_map = np.asarray(lagrange_table(gauss, targets), dtype=np.float32).astype(np.float64)
    return closed_map, open_map


def assembly_matrix(table, count):
    size = table.shape[1]
    matrix = np.zeros((4 * count + 1, count * size))
    for elem_pos in range(count):
        matrix[4 * elem_pos : 4 * elem_pos + 5, size * elem_pos : size * elem_pos + size] += table
    return matrix


def planar_part(coef, flip, table_x, table_y, size_z):
    ex_count, size_x, ey_count, size_y, merged = coef.shape
    orient = jnp.repeat((1 - 2 * flip).astype(jnp.float32), size_z, axis=2)
    signed = (coef * orient[:, None, :, None, :]).reshape(ex_count * size_x * ey_count * size_y, merged)
    rows_y = np.pad(assembly_matrix(table_y, ey_count), ((2, 1), (0, 0)))
    plane_map = np.kron(assembly_matrix(table_x, ex_count), rows_y)
    return jnp.dot(jnp.asarray(plane_map, jnp.float32), signed, precision=lax.Precision.HIGH)


def depth_map_of(table_z, merged):
    return np.pad(assembly_matrix(table_z, merged // table_z.shape[1]), ((2, 1), (0, 0)))


def shifted(block, axis, step=1):
    count = lax.axis_size(axis)
    if count == 1:
        return block
    return lax.ppermute(block, axis, [(i, (i + step) % count) for i in range(count)])


def both_ways(up, down, axis):
    if lax.axis_size(axis) <= 2:
        both = shifted(jnp.concatenate([up, down]), axis)
        return both[: up.shape[0]], both[up.shape[0] :]
    return shifted(up, axis), shifted(down, axis, -1)


def to_wire(slab, dim):
    layers = jnp.moveaxis(slab, dim, 0)
    return layers.reshape(layers.shape[0] * layers.shape[1], -1), layers.shape


def from_wire(rows, shape, dim):
    return jnp.moveaxis(rows.reshape(shape), 0, dim)


def fold_and_halo(extended, axis, dim):
    length = extended.shape[dim]
    n = length - 4
    up, up_shape = to_wire(lax.slice_in_dim(extended, n, n + 3, axis=dim), dim)
    down, down_shape = to_wire(lax.slice_in_dim(extended, 2, 4, axis=dim), dim)
    from_prev, from_next = both_ways(up, down, axis)
    widths_prev = [(0, 0)] * extended.ndim
    widths_prev[dim] = (0, length - 3)
    widths_next = [(0, 0)] * extended.ndim
    widths_next[dim] = (n + 2, 0)
    return (
        extended
        + jnp.pad(from_wire(from_prev, up_shape, dim), widths_prev)
        + jnp.pad(from_wire(from_next, down_shape, dim), widths_next)
    )


def cross_rows(plane, ny, nz):
    own = plane[:, 2 : ny + 2, 2 : nz + 2]
    strips_y = jnp.concatenate([plane[:, 0:2, 2 : nz + 2], plane[:, ny + 2 :, 2 : nz + 2]], axis=1)
    strips_z = jnp.concatenate([plane[:, 2 : ny + 2, 0:2], plane[:, 2 : ny + 2, nz + 2 :]], axis=2)
    strips_z = jnp.swapaxes(strips_z, 1, 2).reshape(-1)
    strips_z = jnp.pad(strips_z, (0, -strips_z.shape[0] % nz))
    return [own.reshape(-1, nz), strips_y.reshape(-1, nz), strips_z.reshape(-1, nz)]


def cross_plane(own, strips_y, strips_z):
    middle = jnp.concatenate([strips_z[..., 0:2], own, strips_z[..., 2:4]], axis=2)
    widths = ((0, 0), (0, 0), (2, 2))
    return jnp.concatenate(
        [jnp.pad(strips_y[:, 0:2], widths), middle, jnp.pad(strips_y[:, 2:4], widths)], axis=1
    )


def last_round_and_stencil(extended, axis, ny, nz):
    n = extended.shape[1] - 1
    comps = extended.shape[0] - 1
    data = extended[:comps]
    keep = extended[comps]

    def own(block):
        return block[..., 2 : ny + 2, 2 : nz + 2]

    halo_up = own(data[:, n - 2 : n] * keep[n - 2 : n])
    halo_down = own(data[:, 1] * keep[1])
    up_parts = [halo_up.reshape(-1, nz)] + cross_rows(data[:, n], ny, nz)
    down_parts = [own(data[:, 0]).reshape(-1, nz), own(keep[0]), halo_down.reshape(-1, nz)]
    up = jnp.concatenate(up_parts)
    down = jnp.concatenate(down_parts)
    from_prev, from_next = both_ways(up, down, axis)

    sizes = [part.shape[0] for part in up_parts]
    marks = np.cumsum([0] + sizes)
    prev_halo = from_prev[marks[0] : marks[1]].reshape(comps, 2, ny, nz)
    prev_own = from_prev[marks[1] : marks[2]].reshape(comps, ny, nz)
    prev_strips_y = from_prev[marks[2] : marks[3]].reshape(comps, 4, nz)
    prev_strips_z = from_prev[marks[3] : marks[4]].reshape(-1)[: comps * 4 * ny]
    prev_strips_z = jnp.swapaxes(prev_strips_z.reshape(comps, 4, ny), 1, 2)
    fold_in = cross_plane(prev_own, prev_strips_y, prev_strips_z)

    plane_rows = comps * ny
    next_fold = from_next[:plane_rows].reshape(comps, ny, nz)
    next_keep = from_next[plane_rows : plane_rows + ny]
    next_halo = from_next[plane_rows + ny :].reshape(comps, ny, nz)

    inner = data[:, 1:n] * keep[1:n]
    first = (data[:, 0] + fold_in) * keep[0]
    last = (own(data[:, n]) + next_fold) * next_keep
    across = jnp.concatenate([yz_terms(first[:, None], ny, nz), yz_terms(inner, ny, nz)], axis=1)
    column = jnp.concatenate(
        [prev_halo, own(first)[:, None], own(inner), last[:, None], next_halo[:, None]], axis=1
    )
    near = column[:, 1 : n + 1] + column[:, 3 : n + 3]
    far = column[:, 0:n] + column[:, 4 : n + 4]
    return 0.25 * (across - 4.0 / 3.0 * near + 1.0 / 12.0 * far)


def yz_terms(block, ny, nz):
    def part(dy, dz):
        return block[..., 2 + dy : ny + 2 + dy, 2 + dz : nz + 2 + dz]

    near = part(-1, 0) + part(1, 0) + part(0, -1) + part(0, 1)
    far = part(-2, 0) + part(2, 0) + part(0, -2) + part(0, 2)
    return 8.0 * part(0, 0) - 4.0 / 3.0 * near + 1.0 / 12.0 * far


def window(padded_array, axis_pos, offset):
    starts = [0, 2, 2, 2]
    limits = [
        padded_array.shape[0],
        padded_array.shape[1] - 2,
        padded_array.shape[2] - 2,
        padded_array.shape[3] - 2,
    ]
    starts[axis_pos] = offset
    limits[axis_pos] = offset + padded_array.shape[axis_pos] - 4
    return lax.slice(padded_array, tuple(starts), tuple(limits))


def stencil_apply(padded_array):
    total = 8.0 * window(padded_array, 1, 2)
    for axis_pos in (1, 2, 3):
        near = window(padded_array, axis_pos, 1) + window(padded_array, axis_pos, 3)
        far = window(padded_array, axis_pos, 0) + window(padded_array, axis_pos, 4)
        total = total - 4.0 / 3.0 * near + 1.0 / 12.0 * far
    return 0.25 * total


def exchange(payloads, axes):
    sizes = [lax.axis_size(axis) for axis in axes]
    groups = {}
    for offset in payloads:
        key = tuple(o % s for o, s in zip(offset, sizes))
        groups.setdefault(key, []).append(offset)
    arrived = {}
    for key, offsets in groups.items():
        flat = jnp.concatenate([part.reshape(-1) for offset in offsets for part in payloads[offset]])
        length = flat.shape[0]
        rows = jnp.pad(flat, (0, -length % 128)).reshape(-1, 128)
        if any(key):
            pairs = []
            for source in np.ndindex(*sizes):
                target = tuple((c + k) % s for c, k, s in zip(source, key, sizes))
                pairs.append((int(np.ravel_multi_index(source, sizes)), int(np.ravel_multi_index(target, sizes))))
            rows = lax.ppermute(rows, tuple(axes), pairs)
        flat = rows.reshape(-1)
        start = 0
        for offset in offsets:
            parts = []
            for part in payloads[offset]:
                size = int(np.prod(part.shape))
                parts.append(flat[start : start + size].reshape(part.shape))
                start += size
            arrived[offset] = parts
    return arrived


def placed(block, starts, shape):
    return jnp.pad(block, [(b, s - b - d) for b, d, s in zip(starts, block.shape, shape)])


def plane_round_and_stencil(extended, nx, ny):
    e = extended
    payloads = {
        (1, 0): (e[:, nx - 2 : nx, 2 : ny + 2, 2:-2], e[:-1, nx : nx + 1, 2 : ny + 3]),
        (-1, 0): (e[:, 0:2, 2 : ny + 2, 2:-2],),
        (0, 1): (e[:, :, ny : ny + 3],),
        (0, -1): (e[:, 0:nx, 2:4],),
        (1, 1): (e[:, nx - 2 : nx + 1, ny + 2], e[:, nx, ny : ny + 2]),
        (-1, 1): (e[:, 0:2, ny + 2],),
        (1, -1): (e[:, nx, 2:4],),
    }
    got = exchange(payloads, ("gx", "gy"))
    channels, _, _, depth = e.shape
    shape = (channels, nx + 4, ny + 4, depth)

    def at(block, layer, row, col=0):
        return placed(block, (0, layer, row, col), shape)

    halo_x, fold_x = got[(1, 0)]
    corner_x, corner_y = got[(1, 1)]
    total = (
        at(e, 2, 0)
        + at(halo_x, 0, 2, 2)
        + at(fold_x, 2, 2)
        + at(got[(-1, 0)][0], nx + 2, 2, 2)
        + at(got[(0, 1)][0], 2, 0)
        + at(got[(0, -1)][0], 2, ny + 2)
        + at(corner_x[:, :, None], 0, 2)
        + at(corner_y[:, None], 2, 0)
        + at(got[(-1, 1)][0][:, :, None], nx + 2, 2)
        + at(got[(1, -1)][0][:, None], 2, ny + 2)
    )
    return stencil_apply(total[:-1] * total[-1])


def body(edge_coeffs_x, edge_coeffs_y, edge_coeffs_z, flips, flags):
    closed_map, open_map = basis_tables()
    nx, ny, nz = flags.shape
    precise = lax.Precision.HIGHEST
    inputs = [
        (edge_coeffs_x, flips[0], open_map, closed_map, closed_map),
        (edge_coeffs_y, flips[1], closed_map, open_map, closed_map),
        (edge_coeffs_z, flips[2], closed_map, closed_map, open_map),
    ]
    length = nz + 4
    up_places = [nz, nz + 1, nz + 2]
    down_places = [2, 3]
    planars = []
    depths = []
    slabs = []
    for coef, flip, table_x, table_y, table_z in inputs:
        planar = planar_part(coef, flip, table_x, table_y, table_z.shape[1])
        depth_map = depth_map_of(table_z, coef.shape[4])
        edge_map = jnp.asarray(depth_map[up_places + down_places], jnp.float32)
        planars.append(planar)
        depths.append(depth_map)
        slabs.append(
            lax.dot_general(edge_map, planar, (((1,), (1,)), ((), ())), precision=lax.Precision.HIGH)
        )
    keep_own = (1 - flags).astype(jnp.float32)
    keep = jnp.pad(keep_own, ((0, 1), (2, 2), (2, 2)))
    keep_layers = [
        lax.slice_in_dim(keep_own, nz - 2, nz, axis=2),
        jnp.zeros_like(lax.slice_in_dim(keep_own, 0, 1, axis=2)),
        lax.slice_in_dim(keep_own, 0, 2, axis=2),
    ]
    keep_layers = jnp.moveaxis(jnp.concatenate(keep_layers, axis=2), 2, 0)
    slabs.append(jnp.pad(keep_layers, ((0, 0), (0, 1), (2, 2))).reshape(5, -1))
    slabs = jnp.stack(slabs)
    up = slabs[:, :3].reshape(-1, slabs.shape[2])
    down = slabs[:, 3:].reshape(-1, slabs.shape[2])
    from_prev, from_next = both_ways(up, down, "gz")
    own_parts = lax.optimization_barrier(
        [
            jnp.dot(planar, jnp.asarray(depth.T, jnp.float32), precision=lax.Precision.HIGH)
            for planar, depth in zip(planars, depths)
        ]
    )
    arrived = jnp.concatenate(
        [from_prev.reshape(4, 3, -1), from_next.reshape(4, 2, -1)], axis=1
    )
    place = np.zeros((5, length))
    for row, col in enumerate([0, 1, 2, nz + 2, nz + 3]):
        place[row, col] = 1.0
    place = jnp.asarray(place, jnp.float32)
    nodal = []
    for comp in range(3):
        folded = lax.dot_general(arrived[comp], place, (((0,), (0,)), ((), ())), precision=precise)
        nodal.append((own_parts[comp] + folded).reshape(nx + 1, ny + 4, length))
    keep_in = jnp.moveaxis(arrived[3].reshape(5, nx + 1, ny + 4), 0, 2)
    keep = keep + jnp.pad(keep_in[..., :3], ((0, 0), (0, 0), (0, length - 3))) + jnp.pad(
        keep_in[..., 3:], ((0, 0), (0, 0), (nz + 2, 0))
    )
    extended = jnp.stack(nodal + [keep])
    return plane_round_and_stencil(extended, nx, ny)


def solution(mesh):
    in_specs = (
        P("gx", None, "gy", None, "gz"),
        P("gx", None, "gy", None, "gz"),
        P("gx", None, "gy", None, "gz"),
        P(None, "gx", "gy", "gz"),
        P("gx", "gy", "gz"),
    )
    out_specs = P(None, "gx", "gy", "gz")
    return jax.shard_map(body, mesh=mesh, in_specs=in_specs, out_specs=out_specs, check_vma=False)
```

```python
import math

import jax
import jax.numpy as jnp
import numpy as np
from jax import lax
from jax.sharding import PartitionSpec as P


def lagrange_table(points, targets):
    table = np.ones((len(targets), len(points)))
    for row_pos in range(len(targets)):
        for col_pos in range(len(points)):
            for other in range(len(points)):
                if other != col_pos:
                    table[row_pos, col_pos] *= (targets[row_pos] - points[other]) / (
                        points[col_pos] - points[other]
                    )
    return table


def basis_tables():
    spread = math.sqrt(3.0 / 7.0)
    targets = [0.0, (1.0 - spread) / 2.0, 0.5, (1.0 + spread) / 2.0, 1.0]
    closed = [0.0, 0.25, 0.5, 0.75, 1.0]
    inner = math.sqrt(3.0 / 7.0 - 2.0 / 7.0 * math.sqrt(6.0 / 5.0))
    outer = math.sqrt(3.0 / 7.0 + 2.0 / 7.0 * math.sqrt(6.0 / 5.0))
    gauss = [(1.0 - outer) / 2.0, (1.0 - inner) / 2.0, (1.0 + inner) / 2.0, (1.0 + outer) / 2.0]
    closed_map = np.asarray(lagrange_table(closed, targets), dtype=np.float32).astype(np.float64)
    open_map = np.asarray(lagrange_table(gauss, targets), dtype=np.float32).astype(np.float64)
    return closed_map, open_map


def assembly_matrix(table, count):
    size = table.shape[1]
    matrix = np.zeros((4 * count + 1, count * size))
    for elem_pos in range(count):
        matrix[4 * elem_pos : 4 * elem_pos + 5, size * elem_pos : size * elem_pos + size] += table
    return matrix


def planar_part(coef, flip, table_x, table_y, size_z):
    ex_count, size_x, ey_count, size_y, merged = coef.shape
    orient = jnp.repeat((1 - 2 * flip).astype(jnp.float32), size_z, axis=2)
    signed = (coef * orient[:, None, :, None, :]).reshape(ex_count * size_x * ey_count * size_y, merged)
    rows_y = np.pad(assembly_matrix(table_y, ey_count), ((2, 1), (0, 0)))
    plane_map = np.kron(assembly_matrix(table_x, ex_count), rows_y)
    return jnp.dot(jnp.asarray(plane_map, jnp.float32), signed, precision=lax.Precision.HIGH)


def depth_map_of(table_z, merged):
    return np.pad(assembly_matrix(table_z, merged // table_z.shape[1]), ((2, 1), (0, 0)))


def shifted(block, axis, step=1):
    count = lax.axis_size(axis)
    if count == 1:
        return block
    return lax.ppermute(block, axis, [(i, (i + step) % count) for i in range(count)])


def both_ways(up, down, axis):
    if lax.axis_size(axis) <= 2:
        both = shifted(jnp.concatenate([up, down]), axis)
        return both[: up.shape[0]], both[up.shape[0] :]
    return shifted(up, axis), shifted(down, axis, -1)


def to_wire(slab, dim):
    layers = jnp.moveaxis(slab, dim, 0)
    return layers.reshape(layers.shape[0] * layers.shape[1], -1), layers.shape


def from_wire(rows, shape, dim):
    return jnp.moveaxis(rows.reshape(shape), 0, dim)


def fold_and_halo(extended, axis, dim):
    length = extended.shape[dim]
    n = length - 4
    up, up_shape = to_wire(lax.slice_in_dim(extended, n, n + 3, axis=dim), dim)
    down, down_shape = to_wire(lax.slice_in_dim(extended, 2, 4, axis=dim), dim)
    from_prev, from_next = both_ways(up, down, axis)
    widths_prev = [(0, 0)] * extended.ndim
    widths_prev[dim] = (0, length - 3)
    widths_next = [(0, 0)] * extended.ndim
    widths_next[dim] = (n + 2, 0)
    return (
        extended
        + jnp.pad(from_wire(from_prev, up_shape, dim), widths_prev)
        + jnp.pad(from_wire(from_next, down_shape, dim), widths_next)
    )


def cross_rows(plane, ny, nz):
    own = plane[:, 2 : ny + 2, 2 : nz + 2]
    strips_y = jnp.concatenate([plane[:, 0:2, 2 : nz + 2], plane[:, ny + 2 :, 2 : nz + 2]], axis=1)
    strips_z = jnp.concatenate([plane[:, 2 : ny + 2, 0:2], plane[:, 2 : ny + 2, nz + 2 :]], axis=2)
    strips_z = jnp.swapaxes(strips_z, 1, 2).reshape(-1)
    strips_z = jnp.pad(strips_z, (0, -strips_z.shape[0] % nz))
    return [own.reshape(-1, nz), strips_y.reshape(-1, nz), strips_z.reshape(-1, nz)]


def cross_plane(own, strips_y, strips_z):
    middle = jnp.concatenate([strips_z[..., 0:2], own, strips_z[..., 2:4]], axis=2)
    widths = ((0, 0), (0, 0), (2, 2))
    return jnp.concatenate(
        [jnp.pad(strips_y[:, 0:2], widths), middle, jnp.pad(strips_y[:, 2:4], widths)], axis=1
    )


def last_round_and_stencil(extended, axis, ny, nz):
    n = extended.shape[1] - 1
    comps = extended.shape[0] - 1
    data = extended[:comps]
    keep = extended[comps]

    def own(block):
        return block[..., 2 : ny + 2, 2 : nz + 2]

    halo_up = own(data[:, n - 2 : n] * keep[n - 2 : n])
    halo_down = own(data[:, 1] * keep[1])
    up_parts = [halo_up.reshape(-1, nz)] + cross_rows(data[:, n], ny, nz)
    down_parts = [own(data[:, 0]).reshape(-1, nz), own(keep[0]), halo_down.reshape(-1, nz)]
    up = jnp.concatenate(up_parts)
    down = jnp.concatenate(down_parts)
    from_prev, from_next = both_ways(up, down, axis)

    sizes = [part.shape[0] for part in up_parts]
    marks = np.cumsum([0] + sizes)
    prev_halo = from_prev[marks[0] : marks[1]].reshape(comps, 2, ny, nz)
    prev_own = from_prev[marks[1] : marks[2]].reshape(comps, ny, nz)
    prev_strips_y = from_prev[marks[2] : marks[3]].reshape(comps, 4, nz)
    prev_strips_z = from_prev[marks[3] : marks[4]].reshape(-1)[: comps * 4 * ny]
    prev_strips_z = jnp.swapaxes(prev_strips_z.reshape(comps, 4, ny), 1, 2)
    fold_in = cross_plane(prev_own, prev_strips_y, prev_strips_z)

    plane_rows = comps * ny
    next_fold = from_next[:plane_rows].reshape(comps, ny, nz)
    next_keep = from_next[plane_rows : plane_rows + ny]
    next_halo = from_next[plane_rows + ny :].reshape(comps, ny, nz)

    inner = data[:, 1:n] * keep[1:n]
    first = (data[:, 0] + fold_in) * keep[0]
    last = (own(data[:, n]) + next_fold) * next_keep
    across = jnp.concatenate([yz_terms(first[:, None], ny, nz), yz_terms(inner, ny, nz)], axis=1)
    column = jnp.concatenate(
        [prev_halo, own(first)[:, None], own(inner), last[:, None], next_halo[:, None]], axis=1
    )
    near = column[:, 1 : n + 1] + column[:, 3 : n + 3]
    far = column[:, 0:n] + column[:, 4 : n + 4]
    return 0.25 * (across - 4.0 / 3.0 * near + 1.0 / 12.0 * far)


def yz_terms(block, ny, nz):
    def part(dy, dz):
        return block[..., 2 + dy : ny + 2 + dy, 2 + dz : nz + 2 + dz]

    near = part(-1, 0) + part(1, 0) + part(0, -1) + part(0, 1)
    far = part(-2, 0) + part(2, 0) + part(0, -2) + part(0, 2)
    return 8.0 * part(0, 0) - 4.0 / 3.0 * near + 1.0 / 12.0 * far


def window(padded_array, axis_pos, offset):
    starts = [0, 2, 2, 2]
    limits = [
        padded_array.shape[0],
        padded_array.shape[1] - 2,
        padded_array.shape[2] - 2,
        padded_array.shape[3] - 2,
    ]
    starts[axis_pos] = offset
    limits[axis_pos] = offset + padded_array.shape[axis_pos] - 4
    return lax.slice(padded_array, tuple(starts), tuple(limits))


def stencil_apply(padded_array):
    total = 8.0 * window(padded_array, 1, 2)
    for axis_pos in (1, 2, 3):
        near = window(padded_array, axis_pos, 1) + window(padded_array, axis_pos, 3)
        far = window(padded_array, axis_pos, 0) + window(padded_array, axis_pos, 4)
        total = total - 4.0 / 3.0 * near + 1.0 / 12.0 * far
    return 0.25 * total


def exchange(payloads, axes):
    sizes = [lax.axis_size(axis) for axis in axes]
    groups = {}
    for offset in payloads:
        key = tuple(o % s for o, s in zip(offset, sizes))
        groups.setdefault(key, []).append(offset)
    arrived = {}
    previous = None
    for key, offsets in groups.items():
        parts = [part for offset in offsets for part in payloads[offset]]
        if previous is not None:
            previous, parts = lax.optimization_barrier((previous, parts))
        flat = jnp.concatenate([part.reshape(-1) for part in parts])
        length = flat.shape[0]
        rows = jnp.pad(flat, (0, -length % 128)).reshape(-1, 128)
        previous = rows
        if any(key):
            pairs = []
            for source in np.ndindex(*sizes):
                target = tuple((c + k) % s for c, k, s in zip(source, key, sizes))
                pairs.append((int(np.ravel_multi_index(source, sizes)), int(np.ravel_multi_index(target, sizes))))
            rows = lax.ppermute(rows, tuple(axes), pairs)
        flat = rows.reshape(-1)
        start = 0
        for offset in offsets:
            parts = []
            for part in payloads[offset]:
                size = int(np.prod(part.shape))
                parts.append(flat[start : start + size].reshape(part.shape))
                start += size
            arrived[offset] = parts
    return arrived


def placed(block, starts, shape):
    return jnp.pad(block, [(b, s - b - d) for b, d, s in zip(starts, block.shape, shape)])


def plane_round_and_stencil(extended, nx, ny):
    e = extended
    payloads = {
        (1, 0): (e[:, nx - 2 : nx, 2 : ny + 2, 2:-2], e[:-1, nx : nx + 1, 2 : ny + 3]),
        (-1, 0): (e[:, 0:2, 2 : ny + 2, 2:-2],),
        (0, 1): (e[:, :, ny : ny + 3],),
        (0, -1): (e[:, 0:nx, 2:4],),
        (1, 1): (e[:, nx - 2 : nx + 1, ny + 2], e[:, nx, ny : ny + 2]),
        (-1, 1): (e[:, 0:2, ny + 2],),
        (1, -1): (e[:, nx, 2:4],),
    }
    got = exchange(payloads, ("gx", "gy"))
    channels, _, _, depth = e.shape
    shape = (channels, nx + 4, ny + 4, depth)

    def at(block, layer, row, col=0):
        return placed(block, (0, layer, row, col), shape)

    halo_x, fold_x = got[(1, 0)]
    corner_x, corner_y = got[(1, 1)]
    total = (
        at(e, 2, 0)
        + at(halo_x, 0, 2, 2)
        + at(fold_x, 2, 2)
        + at(got[(-1, 0)][0], nx + 2, 2, 2)
        + at(got[(0, 1)][0], 2, 0)
        + at(got[(0, -1)][0], 2, ny + 2)
        + at(corner_x[:, :, None], 0, 2)
        + at(corner_y[:, None], 2, 0)
        + at(got[(-1, 1)][0][:, :, None], nx + 2, 2)
        + at(got[(1, -1)][0][:, None], 2, ny + 2)
    )
    return stencil_apply(total[:-1] * total[-1])


def body(edge_coeffs_x, edge_coeffs_y, edge_coeffs_z, flips, flags):
    closed_map, open_map = basis_tables()
    nx, ny, nz = flags.shape
    precise = lax.Precision.HIGHEST
    inputs = [
        (edge_coeffs_x, flips[0], open_map, closed_map, closed_map),
        (edge_coeffs_y, flips[1], closed_map, open_map, closed_map),
        (edge_coeffs_z, flips[2], closed_map, closed_map, open_map),
    ]
    length = nz + 4
    up_places = [nz, nz + 1, nz + 2]
    down_places = [2, 3]
    planars = []
    depths = []
    slabs = []
    for coef, flip, table_x, table_y, table_z in inputs:
        planar = planar_part(coef, flip, table_x, table_y, table_z.shape[1])
        depth_map = depth_map_of(table_z, coef.shape[4])
        edge_map = jnp.asarray(depth_map[up_places + down_places], jnp.float32)
        planars.append(planar)
        depths.append(depth_map)
        slabs.append(
            lax.dot_general(edge_map, planar, (((1,), (1,)), ((), ())), precision=lax.Precision.HIGH)
        )
    keep_own = (1 - flags).astype(jnp.float32)
    keep = jnp.pad(keep_own, ((0, 1), (2, 2), (2, 2)))
    keep_layers = [
        lax.slice_in_dim(keep_own, nz - 2, nz, axis=2),
        jnp.zeros_like(lax.slice_in_dim(keep_own, 0, 1, axis=2)),
        lax.slice_in_dim(keep_own, 0, 2, axis=2),
    ]
    keep_layers = jnp.moveaxis(jnp.concatenate(keep_layers, axis=2), 2, 0)
    slabs.append(jnp.pad(keep_layers, ((0, 0), (0, 1), (2, 2))).reshape(5, -1))
    slabs = jnp.stack(slabs)
    up = slabs[:, :3].reshape(-1, slabs.shape[2])
    down = slabs[:, 3:].reshape(-1, slabs.shape[2])
    from_prev, from_next = both_ways(up, down, "gz")
    own_parts = lax.optimization_barrier(
        [
            jnp.dot(planar, jnp.asarray(depth.T, jnp.float32), precision=lax.Precision.HIGH)
            for planar, depth in zip(planars, depths)
        ]
    )
    arrived = jnp.concatenate(
        [from_prev.reshape(4, 3, -1), from_next.reshape(4, 2, -1)], axis=1
    )
    place = np.zeros((5, length))
    for row, col in enumerate([0, 1, 2, nz + 2, nz + 3]):
        place[row, col] = 1.0
    place = jnp.asarray(place, jnp.float32)
    nodal = []
    for comp in range(3):
        folded = lax.dot_general(arrived[comp], place, (((0,), (0,)), ((), ())), precision=precise)
        nodal.append((own_parts[comp] + folded).reshape(nx + 1, ny + 4, length))
    keep_in = jnp.moveaxis(arrived[3].reshape(5, nx + 1, ny + 4), 0, 2)
    keep = keep + jnp.pad(keep_in[..., :3], ((0, 0), (0, 0), (0, length - 3))) + jnp.pad(
        keep_in[..., 3:], ((0, 0), (0, 0), (nz + 2, 0))
    )
    extended = jnp.stack(nodal + [keep])
    return plane_round_and_stencil(extended, nx, ny)


def solution(mesh):
    in_specs = (
        P("gx", None, "gy", None, "gz"),
        P("gx", None, "gy", None, "gz"),
        P("gx", None, "gy", None, "gz"),
        P(None, "gx", "gy", "gz"),
        P("gx", "gy", "gz"),
    )
    out_specs = P(None, "gx", "gy", "gz")
    return jax.shard_map(body, mesh=mesh, in_specs=in_specs, out_specs=out_specs, check_vma=False)
```

```python
import math

import jax
import jax.numpy as jnp
import numpy as np
from jax import lax
from jax.sharding import PartitionSpec as P


def lagrange_table(points, targets):
    table = np.ones((len(targets), len(points)))
    for row_pos in range(len(targets)):
        for col_pos in range(len(points)):
            for other in range(len(points)):
                if other != col_pos:
                    table[row_pos, col_pos] *= (targets[row_pos] - points[other]) / (
                        points[col_pos] - points[other]
                    )
    return table


def basis_tables():
    spread = math.sqrt(3.0 / 7.0)
    targets = [0.0, (1.0 - spread) / 2.0, 0.5, (1.0 + spread) / 2.0, 1.0]
    closed = [0.0, 0.25, 0.5, 0.75, 1.0]
    inner = math.sqrt(3.0 / 7.0 - 2.0 / 7.0 * math.sqrt(6.0 / 5.0))
    outer = math.sqrt(3.0 / 7.0 + 2.0 / 7.0 * math.sqrt(6.0 / 5.0))
    gauss = [(1.0 - outer) / 2.0, (1.0 - inner) / 2.0, (1.0 + inner) / 2.0, (1.0 + outer) / 2.0]
    closed_map = np.asarray(lagrange_table(closed, targets), dtype=np.float32).astype(np.float64)
    open_map = np.asarray(lagrange_table(gauss, targets), dtype=np.float32).astype(np.float64)
    return closed_map, open_map


def assembly_matrix(table, count):
    size = table.shape[1]
    matrix = np.zeros((4 * count + 1, count * size))
    for elem_pos in range(count):
        matrix[4 * elem_pos : 4 * elem_pos + 5, size * elem_pos : size * elem_pos + size] += table
    return matrix


def planar_part(coef, flip, table_x, table_y, size_z):
    ex_count, size_x, ey_count, size_y, merged = coef.shape
    orient = jnp.repeat((1 - 2 * flip).astype(jnp.float32), size_z, axis=2)
    signed = (coef * orient[:, None, :, None, :]).reshape(ex_count * size_x * ey_count * size_y, merged)
    rows_y = np.pad(assembly_matrix(table_y, ey_count), ((2, 1), (0, 0)))
    plane_map = np.kron(assembly_matrix(table_x, ex_count), rows_y)
    return jnp.dot(jnp.asarray(plane_map, jnp.float32), signed, precision=lax.Precision.HIGH)


def depth_map_of(table_z, merged):
    return np.pad(assembly_matrix(table_z, merged // table_z.shape[1]), ((2, 1), (0, 0)))


def shifted(block, axis, step=1):
    count = lax.axis_size(axis)
    if count == 1:
        return block
    return lax.ppermute(block, axis, [(i, (i + step) % count) for i in range(count)])


def both_ways(up, down, axis):
    if lax.axis_size(axis) <= 2:
        both = shifted(jnp.concatenate([up, down]), axis)
        return both[: up.shape[0]], both[up.shape[0] :]
    return shifted(up, axis), shifted(down, axis, -1)


def to_wire(slab, dim):
    layers = jnp.moveaxis(slab, dim, 0)
    return layers.reshape(layers.shape[0] * layers.shape[1], -1), layers.shape


def from_wire(rows, shape, dim):
    return jnp.moveaxis(rows.reshape(shape), 0, dim)


def fold_and_halo(extended, axis, dim):
    length = extended.shape[dim]
    n = length - 4
    up, up_shape = to_wire(lax.slice_in_dim(extended, n, n + 3, axis=dim), dim)
    down, down_shape = to_wire(lax.slice_in_dim(extended, 2, 4, axis=dim), dim)
    from_prev, from_next = both_ways(up, down, axis)
    widths_prev = [(0, 0)] * extended.ndim
    widths_prev[dim] = (0, length - 3)
    widths_next = [(0, 0)] * extended.ndim
    widths_next[dim] = (n + 2, 0)
    return (
        extended
        + jnp.pad(from_wire(from_prev, up_shape, dim), widths_prev)
        + jnp.pad(from_wire(from_next, down_shape, dim), widths_next)
    )


def cross_rows(plane, ny, nz):
    own = plane[:, 2 : ny + 2, 2 : nz + 2]
    strips_y = jnp.concatenate([plane[:, 0:2, 2 : nz + 2], plane[:, ny + 2 :, 2 : nz + 2]], axis=1)
    strips_z = jnp.concatenate([plane[:, 2 : ny + 2, 0:2], plane[:, 2 : ny + 2, nz + 2 :]], axis=2)
    strips_z = jnp.swapaxes(strips_z, 1, 2).reshape(-1)
    strips_z = jnp.pad(strips_z, (0, -strips_z.shape[0] % nz))
    return [own.reshape(-1, nz), strips_y.reshape(-1, nz), strips_z.reshape(-1, nz)]


def cross_plane(own, strips_y, strips_z):
    middle = jnp.concatenate([strips_z[..., 0:2], own, strips_z[..., 2:4]], axis=2)
    widths = ((0, 0), (0, 0), (2, 2))
    return jnp.concatenate(
        [jnp.pad(strips_y[:, 0:2], widths), middle, jnp.pad(strips_y[:, 2:4], widths)], axis=1
    )


def last_round_and_stencil(extended, axis, ny, nz):
    n = extended.shape[1] - 1
    comps = extended.shape[0] - 1
    data = extended[:comps]
    keep = extended[comps]

    def own(block):
        return block[..., 2 : ny + 2, 2 : nz + 2]

    halo_up = own(data[:, n - 2 : n] * keep[n - 2 : n])
    halo_down = own(data[:, 1] * keep[1])
    up_parts = [halo_up.reshape(-1, nz)] + cross_rows(data[:, n], ny, nz)
    down_parts = [own(data[:, 0]).reshape(-1, nz), own(keep[0]), halo_down.reshape(-1, nz)]
    up = jnp.concatenate(up_parts)
    down = jnp.concatenate(down_parts)
    from_prev, from_next = both_ways(up, down, axis)

    sizes = [part.shape[0] for part in up_parts]
    marks = np.cumsum([0] + sizes)
    prev_halo = from_prev[marks[0] : marks[1]].reshape(comps, 2, ny, nz)
    prev_own = from_prev[marks[1] : marks[2]].reshape(comps, ny, nz)
    prev_strips_y = from_prev[marks[2] : marks[3]].reshape(comps, 4, nz)
    prev_strips_z = from_prev[marks[3] : marks[4]].reshape(-1)[: comps * 4 * ny]
    prev_strips_z = jnp.swapaxes(prev_strips_z.reshape(comps, 4, ny), 1, 2)
    fold_in = cross_plane(prev_own, prev_strips_y, prev_strips_z)

    plane_rows = comps * ny
    next_fold = from_next[:plane_rows].reshape(comps, ny, nz)
    next_keep = from_next[plane_rows : plane_rows + ny]
    next_halo = from_next[plane_rows + ny :].reshape(comps, ny, nz)

    inner = data[:, 1:n] * keep[1:n]
    first = (data[:, 0] + fold_in) * keep[0]
    last = (own(data[:, n]) + next_fold) * next_keep
    across = jnp.concatenate([yz_terms(first[:, None], ny, nz), yz_terms(inner, ny, nz)], axis=1)
    column = jnp.concatenate(
        [prev_halo, own(first)[:, None], own(inner), last[:, None], next_halo[:, None]], axis=1
    )
    near = column[:, 1 : n + 1] + column[:, 3 : n + 3]
    far = column[:, 0:n] + column[:, 4 : n + 4]
    return 0.25 * (across - 4.0 / 3.0 * near + 1.0 / 12.0 * far)


def yz_terms(block, ny, nz):
    def part(dy, dz):
        return block[..., 2 + dy : ny + 2 + dy, 2 + dz : nz + 2 + dz]

    near = part(-1, 0) + part(1, 0) + part(0, -1) + part(0, 1)
    far = part(-2, 0) + part(2, 0) + part(0, -2) + part(0, 2)
    return 8.0 * part(0, 0) - 4.0 / 3.0 * near + 1.0 / 12.0 * far


def window(padded_array, axis_pos, offset):
    starts = [0, 2, 2, 2]
    limits = [
        padded_array.shape[0],
        padded_array.shape[1] - 2,
        padded_array.shape[2] - 2,
        padded_array.shape[3] - 2,
    ]
    starts[axis_pos] = offset
    limits[axis_pos] = offset + padded_array.shape[axis_pos] - 4
    return lax.slice(padded_array, tuple(starts), tuple(limits))


def stencil_apply(padded_array):
    total = 8.0 * window(padded_array, 1, 2)
    for axis_pos in (1, 2, 3):
        near = window(padded_array, axis_pos, 1) + window(padded_array, axis_pos, 3)
        far = window(padded_array, axis_pos, 0) + window(padded_array, axis_pos, 4)
        total = total - 4.0 / 3.0 * near + 1.0 / 12.0 * far
    return 0.25 * total


def exchange(payloads, axes):
    sizes = [lax.axis_size(axis) for axis in axes]
    groups = {}
    for offset in payloads:
        key = tuple(o % s for o, s in zip(offset, sizes))
        groups.setdefault(key, []).append(offset)
    arrived = {}
    previous = None
    for key, offsets in groups.items():
        parts = [part for offset in offsets for part in payloads[offset]]
        if previous is not None:
            previous, parts = lax.optimization_barrier((previous, parts))
        flat = jnp.concatenate([part.reshape(-1) for part in parts])
        length = flat.shape[0]
        rows = jnp.pad(flat, (0, -length % 128)).reshape(-1, 128)
        previous = rows
        if any(key):
            pairs = []
            for source in np.ndindex(*sizes):
                target = tuple((c + k) % s for c, k, s in zip(source, key, sizes))
                pairs.append((int(np.ravel_multi_index(source, sizes)), int(np.ravel_multi_index(target, sizes))))
            rows = lax.ppermute(rows, tuple(axes), pairs)
        flat = rows.reshape(-1)
        start = 0
        for offset in offsets:
            parts = []
            for part in payloads[offset]:
                size = int(np.prod(part.shape))
                parts.append(flat[start : start + size].reshape(part.shape))
                start += size
            arrived[offset] = parts
    return arrived


def placed(block, starts, shape):
    return jnp.pad(block, [(b, s - b - d) for b, d, s in zip(starts, block.shape, shape)])


def plane_round_and_stencil(extended, nx, ny):
    e = extended
    payloads = {
        (1, 0): (e[:, nx - 2 : nx, 2 : ny + 2, 2:-2], e[:-1, nx : nx + 1, 2 : ny + 3]),
        (-1, 0): (e[:, 0:2, 2 : ny + 2, 2:-2],),
        (0, 1): (e[:, :, ny : ny + 3],),
        (0, -1): (e[:, 0:nx, 2:4],),
        (1, 1): (e[:, nx - 2 : nx + 1, ny + 2], e[:, nx, ny : ny + 2]),
        (-1, 1): (e[:, 0:2, ny + 2],),
        (1, -1): (e[:, nx, 2:4],),
    }
    got = exchange(payloads, ("gx", "gy"))
    channels, _, _, depth = e.shape
    shape = (channels, nx + 4, ny + 4, depth)

    def at(block, layer, row, col=0):
        return placed(block, (0, layer, row, col), shape)

    halo_x, fold_x = got[(1, 0)]
    corner_x, corner_y = got[(1, 1)]
    total = (
        at(e, 2, 0)
        + at(halo_x, 0, 2, 2)
        + at(fold_x, 2, 2)
        + at(got[(-1, 0)][0], nx + 2, 2, 2)
        + at(got[(0, 1)][0], 2, 0)
        + at(got[(0, -1)][0], 2, ny + 2)
        + at(corner_x[:, :, None], 0, 2)
        + at(corner_y[:, None], 2, 0)
        + at(got[(-1, 1)][0][:, :, None], nx + 2, 2)
        + at(got[(1, -1)][0][:, None], 2, ny + 2)
    )
    masked = total[:-1] * total[-1]
    inner = z_terms(e[:-1, 1:nx, 3 : ny + 2] * e[-1, 1:nx, 3 : ny + 2])
    rows = jnp.concatenate([z_terms(masked[:, 3 : nx + 2, 2:3]), inner], axis=2)
    result = jnp.concatenate([z_terms(masked[:, 2:3, 2 : ny + 2]), rows], axis=1)
    for axis_pos in (1, 2):
        near = window(masked, axis_pos, 1) + window(masked, axis_pos, 3)
        far = window(masked, axis_pos, 0) + window(masked, axis_pos, 4)
        result = result - 4.0 / 3.0 * near + 1.0 / 12.0 * far
    return 0.25 * result


def z_terms(block):
    nz = block.shape[-1] - 4

    def part(dz):
        return block[..., 2 + dz : nz + 2 + dz]

    return 8.0 * part(0) - 4.0 / 3.0 * (part(-1) + part(1)) + 1.0 / 12.0 * (part(-2) + part(2))


def body(edge_coeffs_x, edge_coeffs_y, edge_coeffs_z, flips, flags):
    closed_map, open_map = basis_tables()
    nx, ny, nz = flags.shape
    precise = lax.Precision.HIGHEST
    inputs = [
        (edge_coeffs_x, flips[0], open_map, closed_map, closed_map),
        (edge_coeffs_y, flips[1], closed_map, open_map, closed_map),
        (edge_coeffs_z, flips[2], closed_map, closed_map, open_map),
    ]
    length = nz + 4
    up_places = [nz, nz + 1, nz + 2]
    down_places = [2, 3]
    planars = []
    depths = []
    slabs = []
    for coef, flip, table_x, table_y, table_z in inputs:
        planar = planar_part(coef, flip, table_x, table_y, table_z.shape[1])
        depth_map = depth_map_of(table_z, coef.shape[4])
        edge_map = jnp.asarray(depth_map[up_places + down_places], jnp.float32)
        planars.append(planar)
        depths.append(depth_map)
        slabs.append(
            lax.dot_general(edge_map, planar, (((1,), (1,)), ((), ())), precision=lax.Precision.HIGH)
        )
    keep_own = (1 - flags).astype(jnp.float32)
    keep = jnp.pad(keep_own, ((0, 1), (2, 2), (2, 2)))
    keep_layers = [
        lax.slice_in_dim(keep_own, nz - 2, nz, axis=2),
        jnp.zeros_like(lax.slice_in_dim(keep_own, 0, 1, axis=2)),
        lax.slice_in_dim(keep_own, 0, 2, axis=2),
    ]
    keep_layers = jnp.moveaxis(jnp.concatenate(keep_layers, axis=2), 2, 0)
    slabs.append(jnp.pad(keep_layers, ((0, 0), (0, 1), (2, 2))).reshape(5, -1))
    slabs = jnp.stack(slabs)
    up = slabs[:, :3].reshape(-1, slabs.shape[2])
    down = slabs[:, 3:].reshape(-1, slabs.shape[2])
    from_prev, from_next = both_ways(up, down, "gz")
    own_parts = lax.optimization_barrier(
        [
            jnp.dot(planar, jnp.asarray(depth.T, jnp.float32), precision=lax.Precision.HIGH)
            for planar, depth in zip(planars, depths)
        ]
    )
    arrived = jnp.concatenate(
        [from_prev.reshape(4, 3, -1), from_next.reshape(4, 2, -1)], axis=1
    )
    place = np.zeros((5, length))
    for row, col in enumerate([0, 1, 2, nz + 2, nz + 3]):
        place[row, col] = 1.0
    place = jnp.asarray(place, jnp.float32)
    nodal = []
    for comp in range(3):
        folded = lax.dot_general(arrived[comp], place, (((0,), (0,)), ((), ())), precision=precise)
        nodal.append((own_parts[comp] + folded).reshape(nx + 1, ny + 4, length))
    keep_in = jnp.moveaxis(arrived[3].reshape(5, nx + 1, ny + 4), 0, 2)
    keep = keep + jnp.pad(keep_in[..., :3], ((0, 0), (0, 0), (0, length - 3))) + jnp.pad(
        keep_in[..., 3:], ((0, 0), (0, 0), (nz + 2, 0))
    )
    extended = jnp.stack(nodal + [keep])
    return plane_round_and_stencil(extended, nx, ny)


def solution(mesh):
    in_specs = (
        P("gx", None, "gy", None, "gz"),
        P("gx", None, "gy", None, "gz"),
        P("gx", None, "gy", None, "gz"),
        P(None, "gx", "gy", "gz"),
        P("gx", "gy", "gz"),
    )
    out_specs = P(None, "gx", "gy", "gz")
    return jax.shard_map(body, mesh=mesh, in_specs=in_specs, out_specs=out_specs, check_vma=False)
```

```python
import math

import jax
import jax.numpy as jnp
import numpy as np
from jax import lax
from jax.sharding import PartitionSpec as P


def lagrange_table(points, targets):
    table = np.ones((len(targets), len(points)))
    for row_pos in range(len(targets)):
        for col_pos in range(len(points)):
            for other in range(len(points)):
                if other != col_pos:
                    table[row_pos, col_pos] *= (targets[row_pos] - points[other]) / (
                        points[col_pos] - points[other]
                    )
    return table


def basis_tables():
    spread = math.sqrt(3.0 / 7.0)
    targets = [0.0, (1.0 - spread) / 2.0, 0.5, (1.0 + spread) / 2.0, 1.0]
    closed = [0.0, 0.25, 0.5, 0.75, 1.0]
    inner = math.sqrt(3.0 / 7.0 - 2.0 / 7.0 * math.sqrt(6.0 / 5.0))
    outer = math.sqrt(3.0 / 7.0 + 2.0 / 7.0 * math.sqrt(6.0 / 5.0))
    gauss = [(1.0 - outer) / 2.0, (1.0 - inner) / 2.0, (1.0 + inner) / 2.0, (1.0 + outer) / 2.0]
    closed_map = np.asarray(lagrange_table(closed, targets), dtype=np.float32).astype(np.float64)
    open_map = np.asarray(lagrange_table(gauss, targets), dtype=np.float32).astype(np.float64)
    return closed_map, open_map


def assembly_matrix(table, count):
    size = table.shape[1]
    matrix = np.zeros((4 * count + 1, count * size))
    for elem_pos in range(count):
        matrix[4 * elem_pos : 4 * elem_pos + 5, size * elem_pos : size * elem_pos + size] += table
    return matrix


def planar_part(coef, flip, table_x, table_y, size_z):
    ex_count, size_x, ey_count, size_y, merged = coef.shape
    orient = jnp.repeat((1 - 2 * flip).astype(jnp.float32), size_z, axis=2)
    signed = (coef * orient[:, None, :, None, :]).reshape(ex_count * size_x * ey_count * size_y, merged)
    rows_y = np.pad(assembly_matrix(table_y, ey_count), ((2, 1), (0, 0)))
    plane_map = np.kron(assembly_matrix(table_x, ex_count), rows_y)
    return jnp.dot(jnp.asarray(plane_map, jnp.float32), signed, precision=lax.Precision.HIGH)


def depth_map_of(table_z, merged):
    return np.pad(assembly_matrix(table_z, merged // table_z.shape[1]), ((2, 1), (0, 0)))


def shifted(block, axis, step=1):
    count = lax.axis_size(axis)
    if count == 1:
        return block
    return lax.ppermute(block, axis, [(i, (i + step) % count) for i in range(count)])


def both_ways(up, down, axis):
    if lax.axis_size(axis) <= 2:
        both = shifted(jnp.concatenate([up, down]), axis)
        return both[: up.shape[0]], both[up.shape[0] :]
    return shifted(up, axis), shifted(down, axis, -1)


def to_wire(slab, dim):
    layers = jnp.moveaxis(slab, dim, 0)
    return layers.reshape(layers.shape[0] * layers.shape[1], -1), layers.shape


def from_wire(rows, shape, dim):
    return jnp.moveaxis(rows.reshape(shape), 0, dim)


def fold_and_halo(extended, axis, dim):
    length = extended.shape[dim]
    n = length - 4
    up, up_shape = to_wire(lax.slice_in_dim(extended, n, n + 3, axis=dim), dim)
    down, down_shape = to_wire(lax.slice_in_dim(extended, 2, 4, axis=dim), dim)
    from_prev, from_next = both_ways(up, down, axis)
    widths_prev = [(0, 0)] * extended.ndim
    widths_prev[dim] = (0, length - 3)
    widths_next = [(0, 0)] * extended.ndim
    widths_next[dim] = (n + 2, 0)
    return (
        extended
        + jnp.pad(from_wire(from_prev, up_shape, dim), widths_prev)
        + jnp.pad(from_wire(from_next, down_shape, dim), widths_next)
    )


def cross_rows(plane, ny, nz):
    own = plane[:, 2 : ny + 2, 2 : nz + 2]
    strips_y = jnp.concatenate([plane[:, 0:2, 2 : nz + 2], plane[:, ny + 2 :, 2 : nz + 2]], axis=1)
    strips_z = jnp.concatenate([plane[:, 2 : ny + 2, 0:2], plane[:, 2 : ny + 2, nz + 2 :]], axis=2)
    strips_z = jnp.swapaxes(strips_z, 1, 2).reshape(-1)
    strips_z = jnp.pad(strips_z, (0, -strips_z.shape[0] % nz))
    return [own.reshape(-1, nz), strips_y.reshape(-1, nz), strips_z.reshape(-1, nz)]


def cross_plane(own, strips_y, strips_z):
    middle = jnp.concatenate([strips_z[..., 0:2], own, strips_z[..., 2:4]], axis=2)
    widths = ((0, 0), (0, 0), (2, 2))
    return jnp.concatenate(
        [jnp.pad(strips_y[:, 0:2], widths), middle, jnp.pad(strips_y[:, 2:4], widths)], axis=1
    )


def last_round_and_stencil(extended, axis, ny, nz):
    n = extended.shape[1] - 1
    comps = extended.shape[0] - 1
    data = extended[:comps]
    keep = extended[comps]

    def own(block):
        return block[..., 2 : ny + 2, 2 : nz + 2]

    halo_up = own(data[:, n - 2 : n] * keep[n - 2 : n])
    halo_down = own(data[:, 1] * keep[1])
    up_parts = [halo_up.reshape(-1, nz)] + cross_rows(data[:, n], ny, nz)
    down_parts = [own(data[:, 0]).reshape(-1, nz), own(keep[0]), halo_down.reshape(-1, nz)]
    up = jnp.concatenate(up_parts)
    down = jnp.concatenate(down_parts)
    from_prev, from_next = both_ways(up, down, axis)

    sizes = [part.shape[0] for part in up_parts]
    marks = np.cumsum([0] + sizes)
    prev_halo = from_prev[marks[0] : marks[1]].reshape(comps, 2, ny, nz)
    prev_own = from_prev[marks[1] : marks[2]].reshape(comps, ny, nz)
    prev_strips_y = from_prev[marks[2] : marks[3]].reshape(comps, 4, nz)
    prev_strips_z = from_prev[marks[3] : marks[4]].reshape(-1)[: comps * 4 * ny]
    prev_strips_z = jnp.swapaxes(prev_strips_z.reshape(comps, 4, ny), 1, 2)
    fold_in = cross_plane(prev_own, prev_strips_y, prev_strips_z)

    plane_rows = comps * ny
    next_fold = from_next[:plane_rows].reshape(comps, ny, nz)
    next_keep = from_next[plane_rows : plane_rows + ny]
    next_halo = from_next[plane_rows + ny :].reshape(comps, ny, nz)

    inner = data[:, 1:n] * keep[1:n]
    first = (data[:, 0] + fold_in) * keep[0]
    last = (own(data[:, n]) + next_fold) * next_keep
    across = jnp.concatenate([yz_terms(first[:, None], ny, nz), yz_terms(inner, ny, nz)], axis=1)
    column = jnp.concatenate(
        [prev_halo, own(first)[:, None], own(inner), last[:, None], next_halo[:, None]], axis=1
    )
    near = column[:, 1 : n + 1] + column[:, 3 : n + 3]
    far = column[:, 0:n] + column[:, 4 : n + 4]
    return 0.25 * (across - 4.0 / 3.0 * near + 1.0 / 12.0 * far)


def yz_terms(block, ny, nz):
    def part(dy, dz):
        return block[..., 2 + dy : ny + 2 + dy, 2 + dz : nz + 2 + dz]

    near = part(-1, 0) + part(1, 0) + part(0, -1) + part(0, 1)
    far = part(-2, 0) + part(2, 0) + part(0, -2) + part(0, 2)
    return 8.0 * part(0, 0) - 4.0 / 3.0 * near + 1.0 / 12.0 * far


def window(padded_array, axis_pos, offset):
    starts = [0, 2, 2, 2]
    limits = [
        padded_array.shape[0],
        padded_array.shape[1] - 2,
        padded_array.shape[2] - 2,
        padded_array.shape[3] - 2,
    ]
    starts[axis_pos] = offset
    limits[axis_pos] = offset + padded_array.shape[axis_pos] - 4
    return lax.slice(padded_array, tuple(starts), tuple(limits))


def stencil_apply(padded_array):
    total = 8.0 * window(padded_array, 1, 2)
    for axis_pos in (1, 2, 3):
        near = window(padded_array, axis_pos, 1) + window(padded_array, axis_pos, 3)
        far = window(padded_array, axis_pos, 0) + window(padded_array, axis_pos, 4)
        total = total - 4.0 / 3.0 * near + 1.0 / 12.0 * far
    return 0.25 * total


def exchange(payloads, axes):
    sizes = [lax.axis_size(axis) for axis in axes]
    groups = {}
    for offset in payloads:
        key = tuple(o % s for o, s in zip(offset, sizes))
        groups.setdefault(key, []).append(offset)
    arrived = {}
    previous = None
    for key, offsets in groups.items():
        parts = [part for offset in offsets for part in payloads[offset]]
        if previous is not None:
            previous, parts = lax.optimization_barrier((previous, parts))
        flat = jnp.concatenate([part.reshape(-1) for part in parts])
        length = flat.shape[0]
        rows = jnp.pad(flat, (0, -length % 128)).reshape(-1, 128)
        previous = rows
        if any(key):
            pairs = []
            for source in np.ndindex(*sizes):
                target = tuple((c + k) % s for c, k, s in zip(source, key, sizes))
                pairs.append((int(np.ravel_multi_index(source, sizes)), int(np.ravel_multi_index(target, sizes))))
            rows = lax.ppermute(rows, tuple(axes), pairs)
        flat = rows.reshape(-1)
        start = 0
        for offset in offsets:
            parts = []
            for part in payloads[offset]:
                size = int(np.prod(part.shape))
                parts.append(flat[start : start + size].reshape(part.shape))
                start += size
            arrived[offset] = parts
    return arrived


def placed(block, starts, shape):
    return jnp.pad(block, [(b, s - b - d) for b, d, s in zip(starts, block.shape, shape)])


def plane_round_and_stencil(extended, nx, ny):
    e = extended
    payloads = {
        (1, 0): (
            e[:-1, nx - 2 : nx, 2 : ny + 2, 2:-2] * e[-1, nx - 2 : nx, 2 : ny + 2, 2:-2],
            e[-1:, nx - 2 : nx, 2:3, 2:-2],
            e[:-1, nx : nx + 1, 2 : ny + 3],
        ),
        (-1, 0): (
            e[:, 0:1, 2 : ny + 2, 2:-2],
            e[:-1, 1:2, 2 : ny + 2, 2:-2] * e[-1, 1:2, 2 : ny + 2, 2:-2],
            e[-1:, 1:2, 2:3, 2:-2],
        ),
        (0, 1): (e[:, :, ny : ny + 3],),
        (0, -1): (e[:, 0:nx, 2:4],),
        (1, 1): (e[:, nx - 2 : nx + 1, ny + 2], e[:, nx, ny : ny + 2]),
        (-1, 1): (e[:, 0:2, ny + 2],),
        (1, -1): (e[:, nx, 2:4],),
    }
    got = exchange(payloads, ("gx", "gy"))
    channels, _, _, depth = e.shape
    shape = (channels, nx + 4, ny + 4, depth)

    def at(block, layer, row, col=0):
        return placed(block, (0, layer, row, col), shape)

    halo_x, halo_keep, fold_x = got[(1, 0)]
    bottom, next_halo, next_keep = got[(-1, 0)]
    corner_x, corner_y = got[(1, 1)]
    data_shape = (channels - 1,) + shape[1:]
    premasked = placed(halo_x, (0, 0, 2, 2), data_shape) + placed(next_halo, (0, nx + 3, 2, 2), data_shape)
    total = (
        at(e, 2, 0)
        + placed(halo_keep, (channels - 1, 0, 2, 2), shape)
        + placed(next_keep, (channels - 1, nx + 3, 2, 2), shape)
        + at(fold_x, 2, 2)
        + at(bottom, nx + 2, 2, 2)
        + at(got[(0, 1)][0], 2, 0)
        + at(got[(0, -1)][0], 2, ny + 2)
        + at(corner_x[:, :, None], 0, 2)
        + at(corner_y[:, None], 2, 0)
        + at(got[(-1, 1)][0][:, :, None], nx + 2, 2)
        + at(got[(1, -1)][0][:, None], 2, ny + 2)
    )
    masked = total[:-1] * total[-1] + premasked
    inner = z_terms(e[:-1, 1:nx, 3 : ny + 2] * e[-1, 1:nx, 3 : ny + 2])
    rows = jnp.concatenate([z_terms(masked[:, 3 : nx + 2, 2:3]), inner], axis=2)
    result = jnp.concatenate([z_terms(masked[:, 2:3, 2 : ny + 2]), rows], axis=1)
    for axis_pos in (1, 2):
        near = window(masked, axis_pos, 1) + window(masked, axis_pos, 3)
        far = window(masked, axis_pos, 0) + window(masked, axis_pos, 4)
        result = result - 4.0 / 3.0 * near + 1.0 / 12.0 * far
    return 0.25 * result


def z_terms(block):
    nz = block.shape[-1] - 4

    def part(dz):
        return block[..., 2 + dz : nz + 2 + dz]

    return 8.0 * part(0) - 4.0 / 3.0 * (part(-1) + part(1)) + 1.0 / 12.0 * (part(-2) + part(2))


def body(edge_coeffs_x, edge_coeffs_y, edge_coeffs_z, flips, flags):
    closed_map, open_map = basis_tables()
    nx, ny, nz = flags.shape
    precise = lax.Precision.HIGHEST
    inputs = [
        (edge_coeffs_x, flips[0], open_map, closed_map, closed_map),
        (edge_coeffs_y, flips[1], closed_map, open_map, closed_map),
        (edge_coeffs_z, flips[2], closed_map, closed_map, open_map),
    ]
    length = nz + 4
    up_places = [nz, nz + 1, nz + 2]
    down_places = [2, 3]
    planars = []
    depths = []
    slabs = []
    for coef, flip, table_x, table_y, table_z in inputs:
        planar = planar_part(coef, flip, table_x, table_y, table_z.shape[1])
        depth_map = depth_map_of(table_z, coef.shape[4])
        edge_map = jnp.asarray(depth_map[up_places + down_places], jnp.float32)
        planars.append(planar)
        depths.append(depth_map)
        slabs.append(
            lax.dot_general(edge_map, planar, (((1,), (1,)), ((), ())), precision=lax.Precision.HIGH)
        )
    keep_own = (1 - flags).astype(jnp.float32)
    keep = jnp.pad(keep_own, ((0, 1), (2, 2), (2, 2)))
    keep_layers = [
        lax.slice_in_dim(keep_own, nz - 2, nz, axis=2),
        jnp.zeros_like(lax.slice_in_dim(keep_own, 0, 1, axis=2)),
        lax.slice_in_dim(keep_own, 0, 2, axis=2),
    ]
    keep_layers = jnp.moveaxis(jnp.concatenate(keep_layers, axis=2), 2, 0)
    slabs.append(jnp.pad(keep_layers, ((0, 0), (0, 1), (2, 2))).reshape(5, -1))
    slabs = jnp.stack(slabs)
    up = slabs[:, :3].reshape(-1, slabs.shape[2])
    down = slabs[:, 3:].reshape(-1, slabs.shape[2])
    from_prev, from_next = both_ways(up, down, "gz")
    own_parts = lax.optimization_barrier(
        [
            jnp.dot(planar, jnp.asarray(depth.T, jnp.float32), precision=lax.Precision.HIGH)
            for planar, depth in zip(planars, depths)
        ]
    )
    arrived = jnp.concatenate(
        [from_prev.reshape(4, 3, -1), from_next.reshape(4, 2, -1)], axis=1
    )
    place = np.zeros((5, length))
    for row, col in enumerate([0, 1, 2, nz + 2, nz + 3]):
        place[row, col] = 1.0
    place = jnp.asarray(place, jnp.float32)
    nodal = []
    for comp in range(3):
        folded = lax.dot_general(arrived[comp], place, (((0,), (0,)), ((), ())), precision=precise)
        nodal.append((own_parts[comp] + folded).reshape(nx + 1, ny + 4, length))
    keep_in = jnp.moveaxis(arrived[3].reshape(5, nx + 1, ny + 4), 0, 2)
    keep = keep + jnp.pad(keep_in[..., :3], ((0, 0), (0, 0), (0, length - 3))) + jnp.pad(
        keep_in[..., 3:], ((0, 0), (0, 0), (nz + 2, 0))
    )
    extended = jnp.stack(nodal + [keep])
    return plane_round_and_stencil(extended, nx, ny)


def solution(mesh):
    in_specs = (
        P("gx", None, "gy", None, "gz"),
        P("gx", None, "gy", None, "gz"),
        P("gx", None, "gy", None, "gz"),
        P(None, "gx", "gy", "gz"),
        P("gx", "gy", "gz"),
    )
    out_specs = P(None, "gx", "gy", "gz")
    return jax.shard_map(body, mesh=mesh, in_specs=in_specs, out_specs=out_specs, check_vma=False)
```

```python
import math

import jax
import jax.numpy as jnp
import numpy as np
from jax import lax
from jax.sharding import PartitionSpec as P


def lagrange_table(points, targets):
    table = np.ones((len(targets), len(points)))
    for row_pos in range(len(targets)):
        for col_pos in range(len(points)):
            for other in range(len(points)):
                if other != col_pos:
                    table[row_pos, col_pos] *= (targets[row_pos] - points[other]) / (
                        points[col_pos] - points[other]
                    )
    return table


def basis_tables():
    spread = math.sqrt(3.0 / 7.0)
    targets = [0.0, (1.0 - spread) / 2.0, 0.5, (1.0 + spread) / 2.0, 1.0]
    closed = [0.0, 0.25, 0.5, 0.75, 1.0]
    inner = math.sqrt(3.0 / 7.0 - 2.0 / 7.0 * math.sqrt(6.0 / 5.0))
    outer = math.sqrt(3.0 / 7.0 + 2.0 / 7.0 * math.sqrt(6.0 / 5.0))
    gauss = [(1.0 - outer) / 2.0, (1.0 - inner) / 2.0, (1.0 + inner) / 2.0, (1.0 + outer) / 2.0]
    closed_map = np.asarray(lagrange_table(closed, targets), dtype=np.float32).astype(np.float64)
    open_map = np.asarray(lagrange_table(gauss, targets), dtype=np.float32).astype(np.float64)
    return closed_map, open_map


def assembly_matrix(table, count):
    size = table.shape[1]
    matrix = np.zeros((4 * count + 1, count * size))
    for elem_pos in range(count):
        matrix[4 * elem_pos : 4 * elem_pos + 5, size * elem_pos : size * elem_pos + size] += table
    return matrix


def planar_part(coef, flip, table_x, table_y, size_z):
    ex_count, size_x, ey_count, size_y, merged = coef.shape
    orient = jnp.repeat((1 - 2 * flip).astype(jnp.float32), size_z, axis=2)
    signed = (coef * orient[:, None, :, None, :]).reshape(ex_count * size_x * ey_count * size_y, merged)
    rows_y = np.pad(assembly_matrix(table_y, ey_count), ((2, 1), (0, 0)))
    plane_map = np.kron(assembly_matrix(table_x, ex_count), rows_y)
    return jnp.dot(jnp.asarray(plane_map, jnp.float32), signed, precision=lax.Precision.HIGH)


def depth_map_of(table_z, merged):
    return np.pad(assembly_matrix(table_z, merged // table_z.shape[1]), ((2, 1), (0, 0)))


def shifted(block, axis, step=1):
    count = lax.axis_size(axis)
    if count == 1:
        return block
    return lax.ppermute(block, axis, [(i, (i + step) % count) for i in range(count)])


def both_ways(up, down, axis):
    if lax.axis_size(axis) <= 2:
        both = shifted(jnp.concatenate([up, down]), axis)
        return both[: up.shape[0]], both[up.shape[0] :]
    return shifted(up, axis), shifted(down, axis, -1)


def to_wire(slab, dim):
    layers = jnp.moveaxis(slab, dim, 0)
    return layers.reshape(layers.shape[0] * layers.shape[1], -1), layers.shape


def from_wire(rows, shape, dim):
    return jnp.moveaxis(rows.reshape(shape), 0, dim)


def fold_and_halo(extended, axis, dim):
    length = extended.shape[dim]
    n = length - 4
    up, up_shape = to_wire(lax.slice_in_dim(extended, n, n + 3, axis=dim), dim)
    down, down_shape = to_wire(lax.slice_in_dim(extended, 2, 4, axis=dim), dim)
    from_prev, from_next = both_ways(up, down, axis)
    widths_prev = [(0, 0)] * extended.ndim
    widths_prev[dim] = (0, length - 3)
    widths_next = [(0, 0)] * extended.ndim
    widths_next[dim] = (n + 2, 0)
    return (
        extended
        + jnp.pad(from_wire(from_prev, up_shape, dim), widths_prev)
        + jnp.pad(from_wire(from_next, down_shape, dim), widths_next)
    )


def cross_rows(plane, ny, nz):
    own = plane[:, 2 : ny + 2, 2 : nz + 2]
    strips_y = jnp.concatenate([plane[:, 0:2, 2 : nz + 2], plane[:, ny + 2 :, 2 : nz + 2]], axis=1)
    strips_z = jnp.concatenate([plane[:, 2 : ny + 2, 0:2], plane[:, 2 : ny + 2, nz + 2 :]], axis=2)
    strips_z = jnp.swapaxes(strips_z, 1, 2).reshape(-1)
    strips_z = jnp.pad(strips_z, (0, -strips_z.shape[0] % nz))
    return [own.reshape(-1, nz), strips_y.reshape(-1, nz), strips_z.reshape(-1, nz)]


def cross_plane(own, strips_y, strips_z):
    middle = jnp.concatenate([strips_z[..., 0:2], own, strips_z[..., 2:4]], axis=2)
    widths = ((0, 0), (0, 0), (2, 2))
    return jnp.concatenate(
        [jnp.pad(strips_y[:, 0:2], widths), middle, jnp.pad(strips_y[:, 2:4], widths)], axis=1
    )


def last_round_and_stencil(extended, axis, ny, nz):
    n = extended.shape[1] - 1
    comps = extended.shape[0] - 1
    data = extended[:comps]
    keep = extended[comps]

    def own(block):
        return block[..., 2 : ny + 2, 2 : nz + 2]

    halo_up = own(data[:, n - 2 : n] * keep[n - 2 : n])
    halo_down = own(data[:, 1] * keep[1])
    up_parts = [halo_up.reshape(-1, nz)] + cross_rows(data[:, n], ny, nz)
    down_parts = [own(data[:, 0]).reshape(-1, nz), own(keep[0]), halo_down.reshape(-1, nz)]
    up = jnp.concatenate(up_parts)
    down = jnp.concatenate(down_parts)
    from_prev, from_next = both_ways(up, down, axis)

    sizes = [part.shape[0] for part in up_parts]
    marks = np.cumsum([0] + sizes)
    prev_halo = from_prev[marks[0] : marks[1]].reshape(comps, 2, ny, nz)
    prev_own = from_prev[marks[1] : marks[2]].reshape(comps, ny, nz)
    prev_strips_y = from_prev[marks[2] : marks[3]].reshape(comps, 4, nz)
    prev_strips_z = from_prev[marks[3] : marks[4]].reshape(-1)[: comps * 4 * ny]
    prev_strips_z = jnp.swapaxes(prev_strips_z.reshape(comps, 4, ny), 1, 2)
    fold_in = cross_plane(prev_own, prev_strips_y, prev_strips_z)

    plane_rows = comps * ny
    next_fold = from_next[:plane_rows].reshape(comps, ny, nz)
    next_keep = from_next[plane_rows : plane_rows + ny]
    next_halo = from_next[plane_rows + ny :].reshape(comps, ny, nz)

    inner = data[:, 1:n] * keep[1:n]
    first = (data[:, 0] + fold_in) * keep[0]
    last = (own(data[:, n]) + next_fold) * next_keep
    across = jnp.concatenate([yz_terms(first[:, None], ny, nz), yz_terms(inner, ny, nz)], axis=1)
    column = jnp.concatenate(
        [prev_halo, own(first)[:, None], own(inner), last[:, None], next_halo[:, None]], axis=1
    )
    near = column[:, 1 : n + 1] + column[:, 3 : n + 3]
    far = column[:, 0:n] + column[:, 4 : n + 4]
    return 0.25 * (across - 4.0 / 3.0 * near + 1.0 / 12.0 * far)


def yz_terms(block, ny, nz):
    def part(dy, dz):
        return block[..., 2 + dy : ny + 2 + dy, 2 + dz : nz + 2 + dz]

    near = part(-1, 0) + part(1, 0) + part(0, -1) + part(0, 1)
    far = part(-2, 0) + part(2, 0) + part(0, -2) + part(0, 2)
    return 8.0 * part(0, 0) - 4.0 / 3.0 * near + 1.0 / 12.0 * far


def window(padded_array, axis_pos, offset):
    starts = [0, 2, 2, 2]
    limits = [
        padded_array.shape[0],
        padded_array.shape[1] - 2,
        padded_array.shape[2] - 2,
        padded_array.shape[3] - 2,
    ]
    starts[axis_pos] = offset
    limits[axis_pos] = offset + padded_array.shape[axis_pos] - 4
    return lax.slice(padded_array, tuple(starts), tuple(limits))


def stencil_apply(padded_array):
    total = 8.0 * window(padded_array, 1, 2)
    for axis_pos in (1, 2, 3):
        near = window(padded_array, axis_pos, 1) + window(padded_array, axis_pos, 3)
        far = window(padded_array, axis_pos, 0) + window(padded_array, axis_pos, 4)
        total = total - 4.0 / 3.0 * near + 1.0 / 12.0 * far
    return 0.25 * total


def exchange(payloads, axes):
    sizes = [lax.axis_size(axis) for axis in axes]
    groups = {}
    for offset in payloads:
        key = tuple(o % s for o, s in zip(offset, sizes))
        groups.setdefault(key, []).append(offset)
    arrived = {}
    previous = None
    for key, offsets in groups.items():
        parts = [part for offset in offsets for part in payloads[offset]]
        if previous is not None:
            previous, parts = lax.optimization_barrier((previous, parts))
        flat = jnp.concatenate([part.reshape(-1) for part in parts])
        length = flat.shape[0]
        rows = jnp.pad(flat, (0, -length % 128)).reshape(-1, 128)
        previous = rows
        if any(key):
            pairs = []
            for source in np.ndindex(*sizes):
                target = tuple((c + k) % s for c, k, s in zip(source, key, sizes))
                pairs.append((int(np.ravel_multi_index(source, sizes)), int(np.ravel_multi_index(target, sizes))))
            rows = lax.ppermute(rows, tuple(axes), pairs)
        flat = rows.reshape(-1)
        start = 0
        for offset in offsets:
            parts = []
            for part in payloads[offset]:
                size = int(np.prod(part.shape))
                parts.append(flat[start : start + size].reshape(part.shape))
                start += size
            arrived[offset] = parts
    return arrived


def placed(block, starts, shape):
    return jnp.pad(block, [(b, s - b - d) for b, d, s in zip(starts, block.shape, shape)])


def plane_round_and_stencil(extended, nx, ny):
    e = extended
    payloads = {
        (-1, 0): (e[:, 0:2, 2 : ny + 2, 2:-2],),
        (1, 0): (e[:, nx - 2 : nx, 2 : ny + 2, 2:-2], e[:-1, nx : nx + 1, 2 : ny + 3]),
        (0, 1): (e[:, :, ny : ny + 3],),
        (0, -1): (e[:, 0:nx, 2:4],),
        (1, 1): (e[:, nx - 2 : nx + 1, ny + 2], e[:, nx, ny : ny + 2]),
        (-1, 1): (e[:, 0:2, ny + 2],),
        (1, -1): (e[:, nx, 2:4],),
    }
    got = exchange(payloads, ("gx", "gy"))
    channels, _, _, depth = e.shape
    shape = (channels, nx + 4, ny + 4, depth)

    def at(block, layer, row, col=0):
        return placed(block, (0, layer, row, col), shape)

    halo_x, fold_x = got[(1, 0)]
    corner_x, corner_y = got[(1, 1)]
    total = (
        at(e, 2, 0)
        + at(halo_x, 0, 2, 2)
        + at(fold_x, 2, 2)
        + at(got[(-1, 0)][0], nx + 2, 2, 2)
        + at(got[(0, 1)][0], 2, 0)
        + at(got[(0, -1)][0], 2, ny + 2)
        + at(corner_x[:, :, None], 0, 2)
        + at(corner_y[:, None], 2, 0)
        + at(got[(-1, 1)][0][:, :, None], nx + 2, 2)
        + at(got[(1, -1)][0][:, None], 2, ny + 2)
    )
    masked = total[:-1] * total[-1]
    inner = z_terms(e[:-1, 1:nx, 3 : ny + 2] * e[-1, 1:nx, 3 : ny + 2])
    rows = jnp.concatenate([z_terms(masked[:, 3 : nx + 2, 2:3]), inner], axis=2)
    result = jnp.concatenate([z_terms(masked[:, 2:3, 2 : ny + 2]), rows], axis=1)
    for axis_pos in (1, 2):
        near = window(masked, axis_pos, 1) + window(masked, axis_pos, 3)
        far = window(masked, axis_pos, 0) + window(masked, axis_pos, 4)
        result = result - 4.0 / 3.0 * near + 1.0 / 12.0 * far
    return 0.25 * result


def z_terms(block):
    nz = block.shape[-1] - 4

    def part(dz):
        return block[..., 2 + dz : nz + 2 + dz]

    return 8.0 * part(0) - 4.0 / 3.0 * (part(-1) + part(1)) + 1.0 / 12.0 * (part(-2) + part(2))


def body(edge_coeffs_x, edge_coeffs_y, edge_coeffs_z, flips, flags):
    closed_map, open_map = basis_tables()
    nx, ny, nz = flags.shape
    precise = lax.Precision.HIGHEST
    inputs = [
        (edge_coeffs_x, flips[0], open_map, closed_map, closed_map),
        (edge_coeffs_y, flips[1], closed_map, open_map, closed_map),
        (edge_coeffs_z, flips[2], closed_map, closed_map, open_map),
    ]
    length = nz + 4
    up_places = [nz, nz + 1, nz + 2]
    down_places = [2, 3]
    planars = []
    depths = []
    slabs = []
    for coef, flip, table_x, table_y, table_z in inputs:
        planar = planar_part(coef, flip, table_x, table_y, table_z.shape[1])
        depth_map = depth_map_of(table_z, coef.shape[4])
        edge_map = jnp.asarray(depth_map[up_places + down_places], jnp.float32)
        planars.append(planar)
        depths.append(depth_map)
        slabs.append(
            lax.dot_general(edge_map, planar, (((1,), (1,)), ((), ())), precision=lax.Precision.HIGH)
        )
    keep_own = (1 - flags).astype(jnp.float32)
    keep = jnp.pad(keep_own, ((0, 1), (2, 2), (2, 2)))
    keep_layers = [
        lax.slice_in_dim(keep_own, nz - 2, nz, axis=2),
        jnp.zeros_like(lax.slice_in_dim(keep_own, 0, 1, axis=2)),
        lax.slice_in_dim(keep_own, 0, 2, axis=2),
    ]
    keep_layers = jnp.moveaxis(jnp.concatenate(keep_layers, axis=2), 2, 0)
    slabs.append(jnp.pad(keep_layers, ((0, 0), (0, 1), (2, 2))).reshape(5, -1))
    slabs = jnp.stack(slabs)
    up = slabs[:, :3].reshape(-1, slabs.shape[2])
    down = slabs[:, 3:].reshape(-1, slabs.shape[2])
    from_prev, from_next = both_ways(up, down, "gz")
    own_parts = lax.optimization_barrier(
        [
            jnp.dot(planar, jnp.asarray(depth.T, jnp.float32), precision=lax.Precision.HIGH)
            for planar, depth in zip(planars, depths)
        ]
    )
    arrived = jnp.concatenate(
        [from_prev.reshape(4, 3, -1), from_next.reshape(4, 2, -1)], axis=1
    )
    place = np.zeros((5, length))
    for row, col in enumerate([0, 1, 2, nz + 2, nz + 3]):
        place[row, col] = 1.0
    place = jnp.asarray(place, jnp.float32)
    nodal = []
    for comp in range(3):
        folded = lax.dot_general(arrived[comp], place, (((0,), (0,)), ((), ())), precision=precise)
        nodal.append((own_parts[comp] + folded).reshape(nx + 1, ny + 4, length))
    keep_in = jnp.moveaxis(arrived[3].reshape(5, nx + 1, ny + 4), 0, 2)
    keep = keep + jnp.pad(keep_in[..., :3], ((0, 0), (0, 0), (0, length - 3))) + jnp.pad(
        keep_in[..., 3:], ((0, 0), (0, 0), (nz + 2, 0))
    )
    extended = jnp.stack(nodal + [keep])
    return plane_round_and_stencil(extended, nx, ny)


def solution(mesh):
    in_specs = (
        P("gx", None, "gy", None, "gz"),
        P("gx", None, "gy", None, "gz"),
        P("gx", None, "gy", None, "gz"),
        P(None, "gx", "gy", "gz"),
        P("gx", "gy", "gz"),
    )
    out_specs = P(None, "gx", "gy", "gz")
    return jax.shard_map(body, mesh=mesh, in_specs=in_specs, out_specs=out_specs, check_vma=False)
```

```python
import math

import jax
import jax.numpy as jnp
import numpy as np
from jax import lax
from jax.sharding import PartitionSpec as P


def lagrange_table(points, targets):
    table = np.ones((len(targets), len(points)))
    for row_pos in range(len(targets)):
        for col_pos in range(len(points)):
            for other in range(len(points)):
                if other != col_pos:
                    table[row_pos, col_pos] *= (targets[row_pos] - points[other]) / (
                        points[col_pos] - points[other]
                    )
    return table


def basis_tables():
    spread = math.sqrt(3.0 / 7.0)
    targets = [0.0, (1.0 - spread) / 2.0, 0.5, (1.0 + spread) / 2.0, 1.0]
    closed = [0.0, 0.25, 0.5, 0.75, 1.0]
    inner = math.sqrt(3.0 / 7.0 - 2.0 / 7.0 * math.sqrt(6.0 / 5.0))
    outer = math.sqrt(3.0 / 7.0 + 2.0 / 7.0 * math.sqrt(6.0 / 5.0))
    gauss = [(1.0 - outer) / 2.0, (1.0 - inner) / 2.0, (1.0 + inner) / 2.0, (1.0 + outer) / 2.0]
    closed_map = np.asarray(lagrange_table(closed, targets), dtype=np.float32).astype(np.float64)
    open_map = np.asarray(lagrange_table(gauss, targets), dtype=np.float32).astype(np.float64)
    return closed_map, open_map


def assembly_matrix(table, count):
    size = table.shape[1]
    matrix = np.zeros((4 * count + 1, count * size))
    for elem_pos in range(count):
        matrix[4 * elem_pos : 4 * elem_pos + 5, size * elem_pos : size * elem_pos + size] += table
    return matrix


def planar_part(coef, flip, table_x, table_y, size_z):
    ex_count, size_x, ey_count, size_y, merged = coef.shape
    orient = jnp.repeat((1 - 2 * flip).astype(jnp.float32), size_z, axis=2)
    signed = (coef * orient[:, None, :, None, :]).reshape(ex_count * size_x * ey_count * size_y, merged)
    rows_y = np.pad(assembly_matrix(table_y, ey_count), ((2, 1), (0, 0)))
    plane_map = np.kron(assembly_matrix(table_x, ex_count), rows_y)
    return jnp.dot(jnp.asarray(plane_map, jnp.float32), signed, precision=lax.Precision.HIGH)


def depth_map_of(table_z, merged):
    return np.pad(assembly_matrix(table_z, merged // table_z.shape[1]), ((2, 1), (0, 0)))


def shifted(block, axis, step=1):
    count = lax.axis_size(axis)
    if count == 1:
        return block
    return lax.ppermute(block, axis, [(i, (i + step) % count) for i in range(count)])


def both_ways(up, down, axis):
    if lax.axis_size(axis) <= 2:
        both = shifted(jnp.concatenate([up, down]), axis)
        return both[: up.shape[0]], both[up.shape[0] :]
    return shifted(up, axis), shifted(down, axis, -1)


def to_wire(slab, dim):
    layers = jnp.moveaxis(slab, dim, 0)
    return layers.reshape(layers.shape[0] * layers.shape[1], -1), layers.shape


def from_wire(rows, shape, dim):
    return jnp.moveaxis(rows.reshape(shape), 0, dim)


def fold_and_halo(extended, axis, dim):
    length = extended.shape[dim]
    n = length - 4
    up, up_shape = to_wire(lax.slice_in_dim(extended, n, n + 3, axis=dim), dim)
    down, down_shape = to_wire(lax.slice_in_dim(extended, 2, 4, axis=dim), dim)
    from_prev, from_next = both_ways(up, down, axis)
    widths_prev = [(0, 0)] * extended.ndim
    widths_prev[dim] = (0, length - 3)
    widths_next = [(0, 0)] * extended.ndim
    widths_next[dim] = (n + 2, 0)
    return (
        extended
        + jnp.pad(from_wire(from_prev, up_shape, dim), widths_prev)
        + jnp.pad(from_wire(from_next, down_shape, dim), widths_next)
    )


def cross_rows(plane, ny, nz):
    own = plane[:, 2 : ny + 2, 2 : nz + 2]
    strips_y = jnp.concatenate([plane[:, 0:2, 2 : nz + 2], plane[:, ny + 2 :, 2 : nz + 2]], axis=1)
    strips_z = jnp.concatenate([plane[:, 2 : ny + 2, 0:2], plane[:, 2 : ny + 2, nz + 2 :]], axis=2)
    strips_z = jnp.swapaxes(strips_z, 1, 2).reshape(-1)
    strips_z = jnp.pad(strips_z, (0, -strips_z.shape[0] % nz))
    return [own.reshape(-1, nz), strips_y.reshape(-1, nz), strips_z.reshape(-1, nz)]


def cross_plane(own, strips_y, strips_z):
    middle = jnp.concatenate([strips_z[..., 0:2], own, strips_z[..., 2:4]], axis=2)
    widths = ((0, 0), (0, 0), (2, 2))
    return jnp.concatenate(
        [jnp.pad(strips_y[:, 0:2], widths), middle, jnp.pad(strips_y[:, 2:4], widths)], axis=1
    )


def last_round_and_stencil(extended, axis, ny, nz):
    n = extended.shape[1] - 1
    comps = extended.shape[0] - 1
    data = extended[:comps]
    keep = extended[comps]

    def own(block):
        return block[..., 2 : ny + 2, 2 : nz + 2]

    halo_up = own(data[:, n - 2 : n] * keep[n - 2 : n])
    halo_down = own(data[:, 1] * keep[1])
    up_parts = [halo_up.reshape(-1, nz)] + cross_rows(data[:, n], ny, nz)
    down_parts = [own(data[:, 0]).reshape(-1, nz), own(keep[0]), halo_down.reshape(-1, nz)]
    up = jnp.concatenate(up_parts)
    down = jnp.concatenate(down_parts)
    from_prev, from_next = both_ways(up, down, axis)

    sizes = [part.shape[0] for part in up_parts]
    marks = np.cumsum([0] + sizes)
    prev_halo = from_prev[marks[0] : marks[1]].reshape(comps, 2, ny, nz)
    prev_own = from_prev[marks[1] : marks[2]].reshape(comps, ny, nz)
    prev_strips_y = from_prev[marks[2] : marks[3]].reshape(comps, 4, nz)
    prev_strips_z = from_prev[marks[3] : marks[4]].reshape(-1)[: comps * 4 * ny]
    prev_strips_z = jnp.swapaxes(prev_strips_z.reshape(comps, 4, ny), 1, 2)
    fold_in = cross_plane(prev_own, prev_strips_y, prev_strips_z)

    plane_rows = comps * ny
    next_fold = from_next[:plane_rows].reshape(comps, ny, nz)
    next_keep = from_next[plane_rows : plane_rows + ny]
    next_halo = from_next[plane_rows + ny :].reshape(comps, ny, nz)

    inner = data[:, 1:n] * keep[1:n]
    first = (data[:, 0] + fold_in) * keep[0]
    last = (own(data[:, n]) + next_fold) * next_keep
    across = jnp.concatenate([yz_terms(first[:, None], ny, nz), yz_terms(inner, ny, nz)], axis=1)
    column = jnp.concatenate(
        [prev_halo, own(first)[:, None], own(inner), last[:, None], next_halo[:, None]], axis=1
    )
    near = column[:, 1 : n + 1] + column[:, 3 : n + 3]
    far = column[:, 0:n] + column[:, 4 : n + 4]
    return 0.25 * (across - 4.0 / 3.0 * near + 1.0 / 12.0 * far)


def yz_terms(block, ny, nz):
    def part(dy, dz):
        return block[..., 2 + dy : ny + 2 + dy, 2 + dz : nz + 2 + dz]

    near = part(-1, 0) + part(1, 0) + part(0, -1) + part(0, 1)
    far = part(-2, 0) + part(2, 0) + part(0, -2) + part(0, 2)
    return 8.0 * part(0, 0) - 4.0 / 3.0 * near + 1.0 / 12.0 * far


def window(padded_array, axis_pos, offset):
    starts = [0, 2, 2, 2]
    limits = [
        padded_array.shape[0],
        padded_array.shape[1] - 2,
        padded_array.shape[2] - 2,
        padded_array.shape[3] - 2,
    ]
    starts[axis_pos] = offset
    limits[axis_pos] = offset + padded_array.shape[axis_pos] - 4
    return lax.slice(padded_array, tuple(starts), tuple(limits))


def stencil_apply(padded_array):
    total = 8.0 * window(padded_array, 1, 2)
    for axis_pos in (1, 2, 3):
        near = window(padded_array, axis_pos, 1) + window(padded_array, axis_pos, 3)
        far = window(padded_array, axis_pos, 0) + window(padded_array, axis_pos, 4)
        total = total - 4.0 / 3.0 * near + 1.0 / 12.0 * far
    return 0.25 * total


def exchange(payloads, axes):
    sizes = [lax.axis_size(axis) for axis in axes]
    groups = {}
    for offset in payloads:
        key = tuple(o % s for o, s in zip(offset, sizes))
        groups.setdefault(key, []).append(offset)
    arrived = {}
    previous = None
    for key, offsets in groups.items():
        parts = [part for offset in offsets for part in payloads[offset]]
        if previous is not None:
            previous, parts = lax.optimization_barrier((previous, parts))
        flat = jnp.concatenate([part.reshape(-1) for part in parts])
        length = flat.shape[0]
        rows = jnp.pad(flat, (0, -length % 128)).reshape(-1, 128)
        previous = rows
        if any(key):
            pairs = []
            for source in np.ndindex(*sizes):
                target = tuple((c + k) % s for c, k, s in zip(source, key, sizes))
                pairs.append((int(np.ravel_multi_index(source, sizes)), int(np.ravel_multi_index(target, sizes))))
            rows = lax.ppermute(rows, tuple(axes), pairs)
        flat = rows.reshape(-1)
        start = 0
        for offset in offsets:
            parts = []
            for part in payloads[offset]:
                size = int(np.prod(part.shape))
                parts.append(flat[start : start + size].reshape(part.shape))
                start += size
            arrived[offset] = parts
    return arrived


def placed(block, starts, shape):
    return jnp.pad(block, [(b, s - b - d) for b, d, s in zip(starts, block.shape, shape)])


class Channels:
    def __init__(self, parts):
        self.parts = parts
        self.shape = (len(parts),) + parts[0].shape

    def __getitem__(self, index):
        picked = self.parts[index[0]]
        if isinstance(index[0], int):
            return picked[index[1:]]
        return jnp.stack([part[index[1:]] for part in picked])


def plane_round_and_stencil(extended, nx, ny):
    e = extended
    payloads = {
        (1, 0): (e[:, nx - 2 : nx, 2 : ny + 2, 2:-2], e[:-1, nx : nx + 1, 2 : ny + 3]),
        (-1, 0): (e[:, 0:2, 2 : ny + 2, 2:-2],),
        (0, 1): (e[:, :, ny : ny + 3],),
        (0, -1): (e[:, 0:nx, 2:4],),
        (1, 1): (e[:, nx - 2 : nx + 1, ny + 2], e[:, nx, ny : ny + 2]),
        (-1, 1): (e[:, 0:2, ny + 2],),
        (1, -1): (e[:, nx, 2:4],),
    }
    got = exchange(payloads, ("gx", "gy"))
    channels, _, _, depth = e.shape
    shape = (channels, nx + 4, ny + 4, depth)

    def at(block, layer, row, col=0):
        return placed(block, (0, layer, row, col), shape)

    halo_x, fold_x = got[(1, 0)]
    corner_x, corner_y = got[(1, 1)]
    total = (
        at(jnp.stack(e.parts), 2, 0)
        + at(halo_x, 0, 2, 2)
        + at(fold_x, 2, 2)
        + at(got[(-1, 0)][0], nx + 2, 2, 2)
        + at(got[(0, 1)][0], 2, 0)
        + at(got[(0, -1)][0], 2, ny + 2)
        + at(corner_x[:, :, None], 0, 2)
        + at(corner_y[:, None], 2, 0)
        + at(got[(-1, 1)][0][:, :, None], nx + 2, 2)
        + at(got[(1, -1)][0][:, None], 2, ny + 2)
    )
    masked = total[:-1] * total[-1]
    inner = z_terms(e[:-1, 1:nx, 3 : ny + 2] * e[-1, 1:nx, 3 : ny + 2])
    rows = jnp.concatenate([z_terms(masked[:, 3 : nx + 2, 2:3]), inner], axis=2)
    result = jnp.concatenate([z_terms(masked[:, 2:3, 2 : ny + 2]), rows], axis=1)
    for axis_pos in (1, 2):
        near = window(masked, axis_pos, 1) + window(masked, axis_pos, 3)
        far = window(masked, axis_pos, 0) + window(masked, axis_pos, 4)
        result = result - 4.0 / 3.0 * near + 1.0 / 12.0 * far
    return 0.25 * result


def z_terms(block):
    nz = block.shape[-1] - 4

    def part(dz):
        return block[..., 2 + dz : nz + 2 + dz]

    return 8.0 * part(0) - 4.0 / 3.0 * (part(-1) + part(1)) + 1.0 / 12.0 * (part(-2) + part(2))


def body(edge_coeffs_x, edge_coeffs_y, edge_coeffs_z, flips, flags):
    closed_map, open_map = basis_tables()
    nx, ny, nz = flags.shape
    precise = lax.Precision.HIGHEST
    inputs = [
        (edge_coeffs_x, flips[0], open_map, closed_map, closed_map),
        (edge_coeffs_y, flips[1], closed_map, open_map, closed_map),
        (edge_coeffs_z, flips[2], closed_map, closed_map, open_map),
    ]
    length = nz + 4
    up_places = [nz, nz + 1, nz + 2]
    down_places = [2, 3]
    planars = []
    depths = []
    slabs = []
    for coef, flip, table_x, table_y, table_z in inputs:
        planar = planar_part(coef, flip, table_x, table_y, table_z.shape[1])
        depth_map = depth_map_of(table_z, coef.shape[4])
        edge_map = jnp.asarray(depth_map[up_places + down_places], jnp.float32)
        planars.append(planar)
        depths.append(depth_map)
        slabs.append(
            lax.dot_general(edge_map, planar, (((1,), (1,)), ((), ())), precision=lax.Precision.HIGH)
        )
    keep_own = (1 - flags).astype(jnp.float32)
    keep = jnp.pad(keep_own, ((0, 1), (2, 2), (2, 2)))
    keep_layers = [
        lax.slice_in_dim(keep_own, nz - 2, nz, axis=2),
        jnp.zeros_like(lax.slice_in_dim(keep_own, 0, 1, axis=2)),
        lax.slice_in_dim(keep_own, 0, 2, axis=2),
    ]
    keep_layers = jnp.moveaxis(jnp.concatenate(keep_layers, axis=2), 2, 0)
    slabs.append(jnp.pad(keep_layers, ((0, 0), (0, 1), (2, 2))).reshape(5, -1))
    slabs = jnp.stack(slabs)
    up = slabs[:, :3].reshape(-1, slabs.shape[2])
    down = slabs[:, 3:].reshape(-1, slabs.shape[2])
    from_prev, from_next = both_ways(up, down, "gz")
    own_parts = lax.optimization_barrier(
        [
            jnp.dot(planar, jnp.asarray(depth.T, jnp.float32), precision=lax.Precision.HIGH)
            for planar, depth in zip(planars, depths)
        ]
    )
    arrived = jnp.concatenate(
        [from_prev.reshape(4, 3, -1), from_next.reshape(4, 2, -1)], axis=1
    )
    place = np.zeros((5, length))
    for row, col in enumerate([0, 1, 2, nz + 2, nz + 3]):
        place[row, col] = 1.0
    place = jnp.asarray(place, jnp.float32)
    nodal = []
    for comp in range(3):
        folded = lax.dot_general(arrived[comp], place, (((0,), (0,)), ((), ())), precision=precise)
        nodal.append((own_parts[comp] + folded).reshape(nx + 1, ny + 4, length))
    keep_in = jnp.moveaxis(arrived[3].reshape(5, nx + 1, ny + 4), 0, 2)
    keep = keep + jnp.pad(keep_in[..., :3], ((0, 0), (0, 0), (0, length - 3))) + jnp.pad(
        keep_in[..., 3:], ((0, 0), (0, 0), (nz + 2, 0))
    )
    extended = Channels(nodal + [keep])
    return plane_round_and_stencil(extended, nx, ny)


def solution(mesh):
    in_specs = (
        P("gx", None, "gy", None, "gz"),
        P("gx", None, "gy", None, "gz"),
        P("gx", None, "gy", None, "gz"),
        P(None, "gx", "gy", "gz"),
        P("gx", "gy", "gz"),
    )
    out_specs = P(None, "gx", "gy", "gz")
    return jax.shard_map(body, mesh=mesh, in_specs=in_specs, out_specs=out_specs, check_vma=False)
```

```python
import math

import jax
import jax.numpy as jnp
import numpy as np
from jax import lax
from jax.sharding import PartitionSpec as P


def lagrange_table(points, targets):
    table = np.ones((len(targets), len(points)))
    for row_pos in range(len(targets)):
        for col_pos in range(len(points)):
            for other in range(len(points)):
                if other != col_pos:
                    table[row_pos, col_pos] *= (targets[row_pos] - points[other]) / (
                        points[col_pos] - points[other]
                    )
    return table


def basis_tables():
    spread = math.sqrt(3.0 / 7.0)
    targets = [0.0, (1.0 - spread) / 2.0, 0.5, (1.0 + spread) / 2.0, 1.0]
    closed = [0.0, 0.25, 0.5, 0.75, 1.0]
    inner = math.sqrt(3.0 / 7.0 - 2.0 / 7.0 * math.sqrt(6.0 / 5.0))
    outer = math.sqrt(3.0 / 7.0 + 2.0 / 7.0 * math.sqrt(6.0 / 5.0))
    gauss = [(1.0 - outer) / 2.0, (1.0 - inner) / 2.0, (1.0 + inner) / 2.0, (1.0 + outer) / 2.0]
    closed_map = np.asarray(lagrange_table(closed, targets), dtype=np.float32).astype(np.float64)
    open_map = np.asarray(lagrange_table(gauss, targets), dtype=np.float32).astype(np.float64)
    return closed_map, open_map


def assembly_matrix(table, count):
    size = table.shape[1]
    matrix = np.zeros((4 * count + 1, count * size))
    for elem_pos in range(count):
        matrix[4 * elem_pos : 4 * elem_pos + 5, size * elem_pos : size * elem_pos + size] += table
    return matrix


def planar_part(coef, flip, table_x, table_y, size_z):
    ex_count, size_x, ey_count, size_y, merged = coef.shape
    orient = jnp.repeat((1 - 2 * flip).astype(jnp.float32), size_z, axis=2)
    signed = (coef * orient[:, None, :, None, :]).reshape(ex_count * size_x * ey_count * size_y, merged)
    rows_y = np.pad(assembly_matrix(table_y, ey_count), ((2, 1), (0, 0)))
    plane_map = np.kron(assembly_matrix(table_x, ex_count), rows_y)
    return jnp.dot(jnp.asarray(plane_map, jnp.float32), signed, precision=lax.Precision.HIGH)


def depth_map_of(table_z, merged):
    return np.pad(assembly_matrix(table_z, merged // table_z.shape[1]), ((2, 1), (0, 0)))


def shifted(block, axis, step=1):
    count = lax.axis_size(axis)
    if count == 1:
        return block
    return lax.ppermute(block, axis, [(i, (i + step) % count) for i in range(count)])


def both_ways(up, down, axis):
    if lax.axis_size(axis) <= 2:
        both = shifted(jnp.concatenate([up, down]), axis)
        return both[: up.shape[0]], both[up.shape[0] :]
    return shifted(up, axis), shifted(down, axis, -1)


def to_wire(slab, dim):
    layers = jnp.moveaxis(slab, dim, 0)
    return layers.reshape(layers.shape[0] * layers.shape[1], -1), layers.shape


def from_wire(rows, shape, dim):
    return jnp.moveaxis(rows.reshape(shape), 0, dim)


def fold_and_halo(extended, axis, dim):
    length = extended.shape[dim]
    n = length - 4
    up, up_shape = to_wire(lax.slice_in_dim(extended, n, n + 3, axis=dim), dim)
    down, down_shape = to_wire(lax.slice_in_dim(extended, 2, 4, axis=dim), dim)
    from_prev, from_next = both_ways(up, down, axis)
    widths_prev = [(0, 0)] * extended.ndim
    widths_prev[dim] = (0, length - 3)
    widths_next = [(0, 0)] * extended.ndim
    widths_next[dim] = (n + 2, 0)
    return (
        extended
        + jnp.pad(from_wire(from_prev, up_shape, dim), widths_prev)
        + jnp.pad(from_wire(from_next, down_shape, dim), widths_next)
    )


def cross_rows(plane, ny, nz):
    own = plane[:, 2 : ny + 2, 2 : nz + 2]
    strips_y = jnp.concatenate([plane[:, 0:2, 2 : nz + 2], plane[:, ny + 2 :, 2 : nz + 2]], axis=1)
    strips_z = jnp.concatenate([plane[:, 2 : ny + 2, 0:2], plane[:, 2 : ny + 2, nz + 2 :]], axis=2)
    strips_z = jnp.swapaxes(strips_z, 1, 2).reshape(-1)
    strips_z = jnp.pad(strips_z, (0, -strips_z.shape[0] % nz))
    return [own.reshape(-1, nz), strips_y.reshape(-1, nz), strips_z.reshape(-1, nz)]


def cross_plane(own, strips_y, strips_z):
    middle = jnp.concatenate([strips_z[..., 0:2], own, strips_z[..., 2:4]], axis=2)
    widths = ((0, 0), (0, 0), (2, 2))
    return jnp.concatenate(
        [jnp.pad(strips_y[:, 0:2], widths), middle, jnp.pad(strips_y[:, 2:4], widths)], axis=1
    )


def last_round_and_stencil(extended, axis, ny, nz):
    n = extended.shape[1] - 1
    comps = extended.shape[0] - 1
    data = extended[:comps]
    keep = extended[comps]

    def own(block):
        return block[..., 2 : ny + 2, 2 : nz + 2]

    halo_up = own(data[:, n - 2 : n] * keep[n - 2 : n])
    halo_down = own(data[:, 1] * keep[1])
    up_parts = [halo_up.reshape(-1, nz)] + cross_rows(data[:, n], ny, nz)
    down_parts = [own(data[:, 0]).reshape(-1, nz), own(keep[0]), halo_down.reshape(-1, nz)]
    up = jnp.concatenate(up_parts)
    down = jnp.concatenate(down_parts)
    from_prev, from_next = both_ways(up, down, axis)

    sizes = [part.shape[0] for part in up_parts]
    marks = np.cumsum([0] + sizes)
    prev_halo = from_prev[marks[0] : marks[1]].reshape(comps, 2, ny, nz)
    prev_own = from_prev[marks[1] : marks[2]].reshape(comps, ny, nz)
    prev_strips_y = from_prev[marks[2] : marks[3]].reshape(comps, 4, nz)
    prev_strips_z = from_prev[marks[3] : marks[4]].reshape(-1)[: comps * 4 * ny]
    prev_strips_z = jnp.swapaxes(prev_strips_z.reshape(comps, 4, ny), 1, 2)
    fold_in = cross_plane(prev_own, prev_strips_y, prev_strips_z)

    plane_rows = comps * ny
    next_fold = from_next[:plane_rows].reshape(comps, ny, nz)
    next_keep = from_next[plane_rows : plane_rows + ny]
    next_halo = from_next[plane_rows + ny :].reshape(comps, ny, nz)

    inner = data[:, 1:n] * keep[1:n]
    first = (data[:, 0] + fold_in) * keep[0]
    last = (own(data[:, n]) + next_fold) * next_keep
    across = jnp.concatenate([yz_terms(first[:, None], ny, nz), yz_terms(inner, ny, nz)], axis=1)
    column = jnp.concatenate(
        [prev_halo, own(first)[:, None], own(inner), last[:, None], next_halo[:, None]], axis=1
    )
    near = column[:, 1 : n + 1] + column[:, 3 : n + 3]
    far = column[:, 0:n] + column[:, 4 : n + 4]
    return 0.25 * (across - 4.0 / 3.0 * near + 1.0 / 12.0 * far)


def yz_terms(block, ny, nz):
    def part(dy, dz):
        return block[..., 2 + dy : ny + 2 + dy, 2 + dz : nz + 2 + dz]

    near = part(-1, 0) + part(1, 0) + part(0, -1) + part(0, 1)
    far = part(-2, 0) + part(2, 0) + part(0, -2) + part(0, 2)
    return 8.0 * part(0, 0) - 4.0 / 3.0 * near + 1.0 / 12.0 * far


def window(padded_array, axis_pos, offset):
    starts = [0, 2, 2, 2]
    limits = [
        padded_array.shape[0],
        padded_array.shape[1] - 2,
        padded_array.shape[2] - 2,
        padded_array.shape[3] - 2,
    ]
    starts[axis_pos] = offset
    limits[axis_pos] = offset + padded_array.shape[axis_pos] - 4
    return lax.slice(padded_array, tuple(starts), tuple(limits))


def stencil_apply(padded_array):
    total = 8.0 * window(padded_array, 1, 2)
    for axis_pos in (1, 2, 3):
        near = window(padded_array, axis_pos, 1) + window(padded_array, axis_pos, 3)
        far = window(padded_array, axis_pos, 0) + window(padded_array, axis_pos, 4)
        total = total - 4.0 / 3.0 * near + 1.0 / 12.0 * far
    return 0.25 * total


def exchange(payloads, axes):
    sizes = [lax.axis_size(axis) for axis in axes]
    groups = {}
    for offset in payloads:
        key = tuple(o % s for o, s in zip(offset, sizes))
        groups.setdefault(key, []).append(offset)
    arrived = {}
    previous = None
    for key, offsets in groups.items():
        parts = [part for offset in offsets for part in payloads[offset]]
        if previous is not None:
            previous, parts = lax.optimization_barrier((previous, parts))
        flat = jnp.concatenate([part.reshape(-1) for part in parts])
        length = flat.shape[0]
        rows = jnp.pad(flat, (0, -length % 128)).reshape(-1, 128)
        previous = rows
        if any(key):
            pairs = []
            for source in np.ndindex(*sizes):
                target = tuple((c + k) % s for c, k, s in zip(source, key, sizes))
                pairs.append((int(np.ravel_multi_index(source, sizes)), int(np.ravel_multi_index(target, sizes))))
            rows = lax.ppermute(rows, tuple(axes), pairs)
        flat = rows.reshape(-1)
        start = 0
        for offset in offsets:
            parts = []
            for part in payloads[offset]:
                size = int(np.prod(part.shape))
                parts.append(flat[start : start + size].reshape(part.shape))
                start += size
            arrived[offset] = parts
    return arrived


def placed(block, starts, shape):
    return jnp.pad(block, [(b, s - b - d) for b, d, s in zip(starts, block.shape, shape)])


def plane_round_and_stencil(extended, nx, ny):
    e = extended
    payloads = {
        (1, 0): (e[:, nx - 2 : nx, 2 : ny + 2, 2:-2], e[:-1, nx : nx + 1, 2 : ny + 3]),
        (-1, 0): (e[:, 0:2, 2 : ny + 2, 2:-2],),
        (0, 1): (e[:, :, ny : ny + 3],),
        (0, -1): (e[:, 0:nx, 2:4],),
        (1, 1): (e[:, nx - 2 : nx + 1, ny + 2], e[:, nx, ny : ny + 2]),
        (-1, 1): (e[:, 0:2, ny + 2],),
        (1, -1): (e[:, nx, 2:4],),
    }
    got = exchange(payloads, ("gx", "gy"))
    channels, _, _, depth = e.shape
    shape = (channels, nx + 4, ny + 4, depth)

    def at(block, layer, row, col=0):
        return placed(block, (0, layer, row, col), shape)

    halo_x, fold_x = got[(1, 0)]
    corner_x, corner_y = got[(1, 1)]
    total = (
        at(e, 2, 0)
        + at(halo_x, 0, 2, 2)
        + at(fold_x, 2, 2)
        + at(got[(-1, 0)][0], nx + 2, 2, 2)
        + at(got[(0, 1)][0], 2, 0)
        + at(got[(0, -1)][0], 2, ny + 2)
        + at(corner_x[:, :, None], 0, 2)
        + at(corner_y[:, None], 2, 0)
        + at(got[(-1, 1)][0][:, :, None], nx + 2, 2)
        + at(got[(1, -1)][0][:, None], 2, ny + 2)
    )
    masked = total[:-1] * total[-1]
    inner = z_terms(e[:-1, 1:nx, 3 : ny + 2] * e[-1, 1:nx, 3 : ny + 2])
    rows = jnp.concatenate([z_terms(masked[:, 3 : nx + 2, 2:3]), inner], axis=2)
    result = jnp.concatenate([z_terms(masked[:, 2:3, 2 : ny + 2]), rows], axis=1)
    for axis_pos in (1, 2):
        near = window(masked, axis_pos, 1) + window(masked, axis_pos, 3)
        far = window(masked, axis_pos, 0) + window(masked, axis_pos, 4)
        result = result - 4.0 / 3.0 * near + 1.0 / 12.0 * far
    return 0.25 * result


def z_terms(block):
    nz = block.shape[-1] - 4

    def part(dz):
        return block[..., 2 + dz : nz + 2 + dz]

    return 8.0 * part(0) - 4.0 / 3.0 * (part(-1) + part(1)) + 1.0 / 12.0 * (part(-2) + part(2))


def body(edge_coeffs_x, edge_coeffs_y, edge_coeffs_z, flips, flags):
    closed_map, open_map = basis_tables()
    nx, ny, nz = flags.shape
    precise = lax.Precision.HIGHEST
    inputs = [
        (edge_coeffs_x, flips[0], open_map, closed_map, closed_map),
        (edge_coeffs_y, flips[1], closed_map, open_map, closed_map),
        (edge_coeffs_z, flips[2], closed_map, closed_map, open_map),
    ]
    length = nz + 4
    up_places = [nz, nz + 1, nz + 2]
    down_places = [2, 3]
    planars = []
    depths = []
    slabs = []
    for coef, flip, table_x, table_y, table_z in inputs:
        planar = planar_part(coef, flip, table_x, table_y, table_z.shape[1])
        depth_map = depth_map_of(table_z, coef.shape[4])
        edge_map = jnp.asarray(depth_map[up_places + down_places], jnp.float32)
        planars.append(planar)
        depths.append(depth_map)
        slabs.append(
            lax.dot_general(edge_map, planar, (((1,), (1,)), ((), ())), precision=lax.Precision.HIGH)
        )
    keep_layers = [
        lax.slice_in_dim(flags, nz - 2, nz, axis=2),
        jnp.ones_like(lax.slice_in_dim(flags, 0, 1, axis=2)),
        lax.slice_in_dim(flags, 0, 2, axis=2),
    ]
    keep_layers = (1 - jnp.moveaxis(jnp.concatenate(keep_layers, axis=2), 2, 0)).astype(jnp.float32)
    slabs.append(jnp.pad(keep_layers, ((0, 0), (0, 1), (2, 2))).reshape(5, -1))
    slabs = jnp.stack(slabs)
    up = slabs[:, :3].reshape(-1, slabs.shape[2])
    down = slabs[:, 3:].reshape(-1, slabs.shape[2])
    from_prev, from_next = both_ways(up, down, "gz")
    own_parts = lax.optimization_barrier(
        [
            jnp.dot(planar, jnp.asarray(depth.T, jnp.float32), precision=lax.Precision.HIGH)
            for planar, depth in zip(planars, depths)
        ]
    )
    arrived = jnp.concatenate(
        [from_prev.reshape(4, 3, -1), from_next.reshape(4, 2, -1)], axis=1
    )
    place = np.zeros((5, length))
    for row, col in enumerate([0, 1, 2, nz + 2, nz + 3]):
        place[row, col] = 1.0
    place = jnp.asarray(place, jnp.float32)
    nodal = []
    for comp in range(3):
        folded = lax.dot_general(arrived[comp], place, (((0,), (0,)), ((), ())), precision=precise)
        nodal.append((own_parts[comp] + folded).reshape(nx + 1, ny + 4, length))
    keep = jnp.pad((1 - flags).astype(jnp.float32), ((0, 1), (2, 2), (2, 2)))
    keep_in = jnp.moveaxis(arrived[3].reshape(5, nx + 1, ny + 4), 0, 2)
    keep = keep + jnp.pad(keep_in[..., :3], ((0, 0), (0, 0), (0, length - 3))) + jnp.pad(
        keep_in[..., 3:], ((0, 0), (0, 0), (nz + 2, 0))
    )
    extended = jnp.stack(nodal + [keep])
    return plane_round_and_stencil(extended, nx, ny)


def solution(mesh):
    in_specs = (
        P("gx", None, "gy", None, "gz"),
        P("gx", None, "gy", None, "gz"),
        P("gx", None, "gy", None, "gz"),
        P(None, "gx", "gy", "gz"),
        P("gx", "gy", "gz"),
    )
    out_specs = P(None, "gx", "gy", "gz")
    return jax.shard_map(body, mesh=mesh, in_specs=in_specs, out_specs=out_specs, check_vma=False)
```

```python
import math

import jax
import jax.numpy as jnp
import numpy as np
from jax import lax
from jax.sharding import PartitionSpec as P


def lagrange_table(points, targets):
    table = np.ones((len(targets), len(points)))
    for row_pos in range(len(targets)):
        for col_pos in range(len(points)):
            for other in range(len(points)):
                if other != col_pos:
                    table[row_pos, col_pos] *= (targets[row_pos] - points[other]) / (
                        points[col_pos] - points[other]
                    )
    return table


def basis_tables():
    spread = math.sqrt(3.0 / 7.0)
    targets = [0.0, (1.0 - spread) / 2.0, 0.5, (1.0 + spread) / 2.0, 1.0]
    closed = [0.0, 0.25, 0.5, 0.75, 1.0]
    inner = math.sqrt(3.0 / 7.0 - 2.0 / 7.0 * math.sqrt(6.0 / 5.0))
    outer = math.sqrt(3.0 / 7.0 + 2.0 / 7.0 * math.sqrt(6.0 / 5.0))
    gauss = [(1.0 - outer) / 2.0, (1.0 - inner) / 2.0, (1.0 + inner) / 2.0, (1.0 + outer) / 2.0]
    closed_map = np.asarray(lagrange_table(closed, targets), dtype=np.float32).astype(np.float64)
    open_map = np.asarray(lagrange_table(gauss, targets), dtype=np.float32).astype(np.float64)
    return closed_map, open_map


def assembly_matrix(table, count):
    size = table.shape[1]
    matrix = np.zeros((4 * count + 1, count * size))
    for elem_pos in range(count):
        matrix[4 * elem_pos : 4 * elem_pos + 5, size * elem_pos : size * elem_pos + size] += table
    return matrix


def planar_part(coef, flip, table_x, table_y, size_z):
    ex_count, size_x, ey_count, size_y, merged = coef.shape
    orient = jnp.repeat((1 - 2 * flip).astype(jnp.float32), size_z, axis=2)
    signed = (coef * orient[:, None, :, None, :]).reshape(ex_count * size_x * ey_count * size_y, merged)
    rows_y = np.pad(assembly_matrix(table_y, ey_count), ((2, 1), (0, 0)))
    plane_map = np.kron(assembly_matrix(table_x, ex_count), rows_y)
    return jnp.dot(jnp.asarray(plane_map, jnp.float32), signed, precision=lax.Precision.HIGH)


def depth_map_of(table_z, merged):
    return np.pad(assembly_matrix(table_z, merged // table_z.shape[1]), ((2, 1), (0, 0)))


def shifted(block, axis, step=1):
    count = lax.axis_size(axis)
    if count == 1:
        return block
    return lax.ppermute(block, axis, [(i, (i + step) % count) for i in range(count)])


def both_ways(up, down, axis):
    if lax.axis_size(axis) <= 2:
        both = shifted(jnp.concatenate([up, down]), axis)
        return both[: up.shape[0]], both[up.shape[0] :]
    return shifted(up, axis), shifted(down, axis, -1)


def to_wire(slab, dim):
    layers = jnp.moveaxis(slab, dim, 0)
    return layers.reshape(layers.shape[0] * layers.shape[1], -1), layers.shape


def from_wire(rows, shape, dim):
    return jnp.moveaxis(rows.reshape(shape), 0, dim)


def fold_and_halo(extended, axis, dim):
    length = extended.shape[dim]
    n = length - 4
    up, up_shape = to_wire(lax.slice_in_dim(extended, n, n + 3, axis=dim), dim)
    down, down_shape = to_wire(lax.slice_in_dim(extended, 2, 4, axis=dim), dim)
    from_prev, from_next = both_ways(up, down, axis)
    widths_prev = [(0, 0)] * extended.ndim
    widths_prev[dim] = (0, length - 3)
    widths_next = [(0, 0)] * extended.ndim
    widths_next[dim] = (n + 2, 0)
    return (
        extended
        + jnp.pad(from_wire(from_prev, up_shape, dim), widths_prev)
        + jnp.pad(from_wire(from_next, down_shape, dim), widths_next)
    )


def cross_rows(plane, ny, nz):
    own = plane[:, 2 : ny + 2, 2 : nz + 2]
    strips_y = jnp.concatenate([plane[:, 0:2, 2 : nz + 2], plane[:, ny + 2 :, 2 : nz + 2]], axis=1)
    strips_z = jnp.concatenate([plane[:, 2 : ny + 2, 0:2], plane[:, 2 : ny + 2, nz + 2 :]], axis=2)
    strips_z = jnp.swapaxes(strips_z, 1, 2).reshape(-1)
    strips_z = jnp.pad(strips_z, (0, -strips_z.shape[0] % nz))
    return [own.reshape(-1, nz), strips_y.reshape(-1, nz), strips_z.reshape(-1, nz)]


def cross_plane(own, strips_y, strips_z):
    middle = jnp.concatenate([strips_z[..., 0:2], own, strips_z[..., 2:4]], axis=2)
    widths = ((0, 0), (0, 0), (2, 2))
    return jnp.concatenate(
        [jnp.pad(strips_y[:, 0:2], widths), middle, jnp.pad(strips_y[:, 2:4], widths)], axis=1
    )


def last_round_and_stencil(extended, axis, ny, nz):
    n = extended.shape[1] - 1
    comps = extended.shape[0] - 1
    data = extended[:comps]
    keep = extended[comps]

    def own(block):
        return block[..., 2 : ny + 2, 2 : nz + 2]

    halo_up = own(data[:, n - 2 : n] * keep[n - 2 : n])
    halo_down = own(data[:, 1] * keep[1])
    up_parts = [halo_up.reshape(-1, nz)] + cross_rows(data[:, n], ny, nz)
    down_parts = [own(data[:, 0]).reshape(-1, nz), own(keep[0]), halo_down.reshape(-1, nz)]
    up = jnp.concatenate(up_parts)
    down = jnp.concatenate(down_parts)
    from_prev, from_next = both_ways(up, down, axis)

    sizes = [part.shape[0] for part in up_parts]
    marks = np.cumsum([0] + sizes)
    prev_halo = from_prev[marks[0] : marks[1]].reshape(comps, 2, ny, nz)
    prev_own = from_prev[marks[1] : marks[2]].reshape(comps, ny, nz)
    prev_strips_y = from_prev[marks[2] : marks[3]].reshape(comps, 4, nz)
    prev_strips_z = from_prev[marks[3] : marks[4]].reshape(-1)[: comps * 4 * ny]
    prev_strips_z = jnp.swapaxes(prev_strips_z.reshape(comps, 4, ny), 1, 2)
    fold_in = cross_plane(prev_own, prev_strips_y, prev_strips_z)

    plane_rows = comps * ny
    next_fold = from_next[:plane_rows].reshape(comps, ny, nz)
    next_keep = from_next[plane_rows : plane_rows + ny]
    next_halo = from_next[plane_rows + ny :].reshape(comps, ny, nz)

    inner = data[:, 1:n] * keep[1:n]
    first = (data[:, 0] + fold_in) * keep[0]
    last = (own(data[:, n]) + next_fold) * next_keep
    across = jnp.concatenate([yz_terms(first[:, None], ny, nz), yz_terms(inner, ny, nz)], axis=1)
    column = jnp.concatenate(
        [prev_halo, own(first)[:, None], own(inner), last[:, None], next_halo[:, None]], axis=1
    )
    near = column[:, 1 : n + 1] + column[:, 3 : n + 3]
    far = column[:, 0:n] + column[:, 4 : n + 4]
    return 0.25 * (across - 4.0 / 3.0 * near + 1.0 / 12.0 * far)


def yz_terms(block, ny, nz):
    def part(dy, dz):
        return block[..., 2 + dy : ny + 2 + dy, 2 + dz : nz + 2 + dz]

    near = part(-1, 0) + part(1, 0) + part(0, -1) + part(0, 1)
    far = part(-2, 0) + part(2, 0) + part(0, -2) + part(0, 2)
    return 8.0 * part(0, 0) - 4.0 / 3.0 * near + 1.0 / 12.0 * far


def window(padded_array, axis_pos, offset):
    starts = [0, 2, 2, 2]
    limits = [
        padded_array.shape[0],
        padded_array.shape[1] - 2,
        padded_array.shape[2] - 2,
        padded_array.shape[3] - 2,
    ]
    starts[axis_pos] = offset
    limits[axis_pos] = offset + padded_array.shape[axis_pos] - 4
    return lax.slice(padded_array, tuple(starts), tuple(limits))


def stencil_apply(padded_array):
    total = 8.0 * window(padded_array, 1, 2)
    for axis_pos in (1, 2, 3):
        near = window(padded_array, axis_pos, 1) + window(padded_array, axis_pos, 3)
        far = window(padded_array, axis_pos, 0) + window(padded_array, axis_pos, 4)
        total = total - 4.0 / 3.0 * near + 1.0 / 12.0 * far
    return 0.25 * total


def exchange(payloads, axes):
    sizes = [lax.axis_size(axis) for axis in axes]
    groups = {}
    for offset in payloads:
        key = tuple(o % s for o, s in zip(offset, sizes))
        groups.setdefault(key, []).append(offset)
    arrived = {}
    previous = None
    for key, offsets in groups.items():
        parts = [part for offset in offsets for part in payloads[offset]]
        if previous is not None:
            previous, parts = lax.optimization_barrier((previous, parts))
        flat = jnp.concatenate([jnp.pad(part.reshape(-1), (0, -part.size % 1024)) for part in parts])
        length = flat.shape[0]
        rows = jnp.pad(flat, (0, -length % 128)).reshape(-1, 128)
        previous = rows
        if any(key):
            pairs = []
            for source in np.ndindex(*sizes):
                target = tuple((c + k) % s for c, k, s in zip(source, key, sizes))
                pairs.append((int(np.ravel_multi_index(source, sizes)), int(np.ravel_multi_index(target, sizes))))
            rows = lax.ppermute(rows, tuple(axes), pairs)
        flat = rows.reshape(-1)
        start = 0
        for offset in offsets:
            parts = []
            for part in payloads[offset]:
                size = int(np.prod(part.shape))
                parts.append(flat[start : start + size].reshape(part.shape))
                start += size + (-size % 1024)
            arrived[offset] = parts
    return arrived


def placed(block, starts, shape):
    return jnp.pad(block, [(b, s - b - d) for b, d, s in zip(starts, block.shape, shape)])


def plane_round_and_stencil(extended, nx, ny):
    e = extended
    payloads = {
        (1, 0): (e[:, nx - 2 : nx, 2 : ny + 2, 2:-2], e[:-1, nx : nx + 1, 2 : ny + 3]),
        (-1, 0): (e[:, 0:2, 2 : ny + 2, 2:-2],),
        (0, 1): (e[:, :, ny : ny + 3],),
        (0, -1): (e[:, 0:nx, 2:4],),
        (1, 1): (e[:, nx - 2 : nx + 1, ny + 2], e[:, nx, ny : ny + 2]),
        (-1, 1): (e[:, 0:2, ny + 2],),
        (1, -1): (e[:, nx, 2:4],),
    }
    got = exchange(payloads, ("gx", "gy"))
    channels, _, _, depth = e.shape
    shape = (channels, nx + 4, ny + 4, depth)

    def at(block, layer, row, col=0):
        return placed(block, (0, layer, row, col), shape)

    halo_x, fold_x = got[(1, 0)]
    corner_x, corner_y = got[(1, 1)]
    total = (
        at(e, 2, 0)
        + at(halo_x, 0, 2, 2)
        + at(fold_x, 2, 2)
        + at(got[(-1, 0)][0], nx + 2, 2, 2)
        + at(got[(0, 1)][0], 2, 0)
        + at(got[(0, -1)][0], 2, ny + 2)
        + at(corner_x[:, :, None], 0, 2)
        + at(corner_y[:, None], 2, 0)
        + at(got[(-1, 1)][0][:, :, None], nx + 2, 2)
        + at(got[(1, -1)][0][:, None], 2, ny + 2)
    )
    masked = total[:-1] * total[-1]
    inner = z_terms(e[:-1, 1:nx, 3 : ny + 2] * e[-1, 1:nx, 3 : ny + 2])
    rows = jnp.concatenate([z_terms(masked[:, 3 : nx + 2, 2:3]), inner], axis=2)
    result = jnp.concatenate([z_terms(masked[:, 2:3, 2 : ny + 2]), rows], axis=1)
    for axis_pos in (1, 2):
        near = window(masked, axis_pos, 1) + window(masked, axis_pos, 3)
        far = window(masked, axis_pos, 0) + window(masked, axis_pos, 4)
        result = result - 4.0 / 3.0 * near + 1.0 / 12.0 * far
    return 0.25 * result


def z_terms(block):
    nz = block.shape[-1] - 4

    def part(dz):
        return block[..., 2 + dz : nz + 2 + dz]

    return 8.0 * part(0) - 4.0 / 3.0 * (part(-1) + part(1)) + 1.0 / 12.0 * (part(-2) + part(2))


def body(edge_coeffs_x, edge_coeffs_y, edge_coeffs_z, flips, flags):
    closed_map, open_map = basis_tables()
    nx, ny, nz = flags.shape
    precise = lax.Precision.HIGHEST
    inputs = [
        (edge_coeffs_x, flips[0], open_map, closed_map, closed_map),
        (edge_coeffs_y, flips[1], closed_map, open_map, closed_map),
        (edge_coeffs_z, flips[2], closed_map, closed_map, open_map),
    ]
    length = nz + 4
    up_places = [nz, nz + 1, nz + 2]
    down_places = [2, 3]
    planars = []
    depths = []
    slabs = []
    for coef, flip, table_x, table_y, table_z in inputs:
        planar = planar_part(coef, flip, table_x, table_y, table_z.shape[1])
        depth_map = depth_map_of(table_z, coef.shape[4])
        edge_map = jnp.asarray(depth_map[up_places + down_places], jnp.float32)
        planars.append(planar)
        depths.append(depth_map)
        slabs.append(
            lax.dot_general(edge_map, planar, (((1,), (1,)), ((), ())), precision=lax.Precision.HIGH)
        )
    keep_own = (1 - flags).astype(jnp.float32)
    keep = jnp.pad(keep_own, ((0, 1), (2, 2), (2, 2)))
    keep_layers = [
        lax.slice_in_dim(keep_own, nz - 2, nz, axis=2),
        jnp.zeros_like(lax.slice_in_dim(keep_own, 0, 1, axis=2)),
        lax.slice_in_dim(keep_own, 0, 2, axis=2),
    ]
    keep_layers = jnp.moveaxis(jnp.concatenate(keep_layers, axis=2), 2, 0)
    slabs.append(jnp.pad(keep_layers, ((0, 0), (0, 1), (2, 2))).reshape(5, -1))
    slabs = jnp.stack(slabs)
    up = slabs[:, :3].reshape(-1, slabs.shape[2])
    down = slabs[:, 3:].reshape(-1, slabs.shape[2])
    from_prev, from_next = both_ways(up, down, "gz")
    own_parts = lax.optimization_barrier(
        [
            jnp.dot(planar, jnp.asarray(depth.T, jnp.float32), precision=lax.Precision.HIGH)
            for planar, depth in zip(planars, depths)
        ]
    )
    arrived = jnp.concatenate(
        [from_prev.reshape(4, 3, -1), from_next.reshape(4, 2, -1)], axis=1
    )
    place = np.zeros((5, length))
    for row, col in enumerate([0, 1, 2, nz + 2, nz + 3]):
        place[row, col] = 1.0
    place = jnp.asarray(place, jnp.float32)
    nodal = []
    for comp in range(3):
        folded = lax.dot_general(arrived[comp], place, (((0,), (0,)), ((), ())), precision=precise)
        nodal.append((own_parts[comp] + folded).reshape(nx + 1, ny + 4, length))
    keep_in = jnp.moveaxis(arrived[3].reshape(5, nx + 1, ny + 4), 0, 2)
    keep = keep + jnp.pad(keep_in[..., :3], ((0, 0), (0, 0), (0, length - 3))) + jnp.pad(
        keep_in[..., 3:], ((0, 0), (0, 0), (nz + 2, 0))
    )
    extended = jnp.stack(nodal + [keep])
    return plane_round_and_stencil(extended, nx, ny)


def solution(mesh):
    in_specs = (
        P("gx", None, "gy", None, "gz"),
        P("gx", None, "gy", None, "gz"),
        P("gx", None, "gy", None, "gz"),
        P(None, "gx", "gy", "gz"),
        P("gx", "gy", "gz"),
    )
    out_specs = P(None, "gx", "gy", "gz")
    return jax.shard_map(body, mesh=mesh, in_specs=in_specs, out_specs=out_specs, check_vma=False)
```

```python
import math

import jax
import jax.numpy as jnp
import numpy as np
from jax import lax
from jax.sharding import PartitionSpec as P


def lagrange_table(points, targets):
    table = np.ones((len(targets), len(points)))
    for row_pos in range(len(targets)):
        for col_pos in range(len(points)):
            for other in range(len(points)):
                if other != col_pos:
                    table[row_pos, col_pos] *= (targets[row_pos] - points[other]) / (
                        points[col_pos] - points[other]
                    )
    return table


def basis_tables():
    spread = math.sqrt(3.0 / 7.0)
    targets = [0.0, (1.0 - spread) / 2.0, 0.5, (1.0 + spread) / 2.0, 1.0]
    closed = [0.0, 0.25, 0.5, 0.75, 1.0]
    inner = math.sqrt(3.0 / 7.0 - 2.0 / 7.0 * math.sqrt(6.0 / 5.0))
    outer = math.sqrt(3.0 / 7.0 + 2.0 / 7.0 * math.sqrt(6.0 / 5.0))
    gauss = [(1.0 - outer) / 2.0, (1.0 - inner) / 2.0, (1.0 + inner) / 2.0, (1.0 + outer) / 2.0]
    closed_map = np.asarray(lagrange_table(closed, targets), dtype=np.float32).astype(np.float64)
    open_map = np.asarray(lagrange_table(gauss, targets), dtype=np.float32).astype(np.float64)
    return closed_map, open_map


def assembly_matrix(table, count):
    size = table.shape[1]
    matrix = np.zeros((4 * count + 1, count * size))
    for elem_pos in range(count):
        matrix[4 * elem_pos : 4 * elem_pos + 5, size * elem_pos : size * elem_pos + size] += table
    return matrix


def planar_part(coef, flip, table_x, table_y, size_z):
    ex_count, size_x, ey_count, size_y, merged = coef.shape
    orient = jnp.repeat((1 - 2 * flip).astype(jnp.float32), size_z, axis=2)
    signed = (coef * orient[:, None, :, None, :]).reshape(ex_count * size_x * ey_count * size_y, merged)
    rows_y = np.pad(assembly_matrix(table_y, ey_count), ((2, 1), (0, 0)))
    plane_map = np.kron(assembly_matrix(table_x, ex_count), rows_y)
    return jnp.dot(jnp.asarray(plane_map, jnp.float32), signed, precision=lax.Precision.HIGH)


def depth_map_of(table_z, merged):
    return np.pad(assembly_matrix(table_z, merged // table_z.shape[1]), ((2, 1), (0, 0)))


def shifted(block, axis, step=1):
    count = lax.axis_size(axis)
    if count == 1:
        return block
    return lax.ppermute(block, axis, [(i, (i + step) % count) for i in range(count)])


def both_ways(up, down, axis):
    if lax.axis_size(axis) <= 2:
        both = shifted(jnp.concatenate([up, down]), axis)
        return both[: up.shape[0]], both[up.shape[0] :]
    return shifted(up, axis), shifted(down, axis, -1)


def to_wire(slab, dim):
    layers = jnp.moveaxis(slab, dim, 0)
    return layers.reshape(layers.shape[0] * layers.shape[1], -1), layers.shape


def from_wire(rows, shape, dim):
    return jnp.moveaxis(rows.reshape(shape), 0, dim)


def fold_and_halo(extended, axis, dim):
    length = extended.shape[dim]
    n = length - 4
    up, up_shape = to_wire(lax.slice_in_dim(extended, n, n + 3, axis=dim), dim)
    down, down_shape = to_wire(lax.slice_in_dim(extended, 2, 4, axis=dim), dim)
    from_prev, from_next = both_ways(up, down, axis)
    widths_prev = [(0, 0)] * extended.ndim
    widths_prev[dim] = (0, length - 3)
    widths_next = [(0, 0)] * extended.ndim
    widths_next[dim] = (n + 2, 0)
    return (
        extended
        + jnp.pad(from_wire(from_prev, up_shape, dim), widths_prev)
        + jnp.pad(from_wire(from_next, down_shape, dim), widths_next)
    )


def cross_rows(plane, ny, nz):
    own = plane[:, 2 : ny + 2, 2 : nz + 2]
    strips_y = jnp.concatenate([plane[:, 0:2, 2 : nz + 2], plane[:, ny + 2 :, 2 : nz + 2]], axis=1)
    strips_z = jnp.concatenate([plane[:, 2 : ny + 2, 0:2], plane[:, 2 : ny + 2, nz + 2 :]], axis=2)
    strips_z = jnp.swapaxes(strips_z, 1, 2).reshape(-1)
    strips_z = jnp.pad(strips_z, (0, -strips_z.shape[0] % nz))
    return [own.reshape(-1, nz), strips_y.reshape(-1, nz), strips_z.reshape(-1, nz)]


def cross_plane(own, strips_y, strips_z):
    middle = jnp.concatenate([strips_z[..., 0:2], own, strips_z[..., 2:4]], axis=2)
    widths = ((0, 0), (0, 0), (2, 2))
    return jnp.concatenate(
        [jnp.pad(strips_y[:, 0:2], widths), middle, jnp.pad(strips_y[:, 2:4], widths)], axis=1
    )


def last_round_and_stencil(extended, axis, ny, nz):
    n = extended.shape[1] - 1
    comps = extended.shape[0] - 1
    data = extended[:comps]
    keep = extended[comps]

    def own(block):
        return block[..., 2 : ny + 2, 2 : nz + 2]

    halo_up = own(data[:, n - 2 : n] * keep[n - 2 : n])
    halo_down = own(data[:, 1] * keep[1])
    up_parts = [halo_up.reshape(-1, nz)] + cross_rows(data[:, n], ny, nz)
    down_parts = [own(data[:, 0]).reshape(-1, nz), own(keep[0]), halo_down.reshape(-1, nz)]
    up = jnp.concatenate(up_parts)
    down = jnp.concatenate(down_parts)
    from_prev, from_next = both_ways(up, down, axis)

    sizes = [part.shape[0] for part in up_parts]
    marks = np.cumsum([0] + sizes)
    prev_halo = from_prev[marks[0] : marks[1]].reshape(comps, 2, ny, nz)
    prev_own = from_prev[marks[1] : marks[2]].reshape(comps, ny, nz)
    prev_strips_y = from_prev[marks[2] : marks[3]].reshape(comps, 4, nz)
    prev_strips_z = from_prev[marks[3] : marks[4]].reshape(-1)[: comps * 4 * ny]
    prev_strips_z = jnp.swapaxes(prev_strips_z.reshape(comps, 4, ny), 1, 2)
    fold_in = cross_plane(prev_own, prev_strips_y, prev_strips_z)

    plane_rows = comps * ny
    next_fold = from_next[:plane_rows].reshape(comps, ny, nz)
    next_keep = from_next[plane_rows : plane_rows + ny]
    next_halo = from_next[plane_rows + ny :].reshape(comps, ny, nz)

    inner = data[:, 1:n] * keep[1:n]
    first = (data[:, 0] + fold_in) * keep[0]
    last = (own(data[:, n]) + next_fold) * next_keep
    across = jnp.concatenate([yz_terms(first[:, None], ny, nz), yz_terms(inner, ny, nz)], axis=1)
    column = jnp.concatenate(
        [prev_halo, own(first)[:, None], own(inner), last[:, None], next_halo[:, None]], axis=1
    )
    near = column[:, 1 : n + 1] + column[:, 3 : n + 3]
    far = column[:, 0:n] + column[:, 4 : n + 4]
    return 0.25 * (across - 4.0 / 3.0 * near + 1.0 / 12.0 * far)


def yz_terms(block, ny, nz):
    def part(dy, dz):
        return block[..., 2 + dy : ny + 2 + dy, 2 + dz : nz + 2 + dz]

    near = part(-1, 0) + part(1, 0) + part(0, -1) + part(0, 1)
    far = part(-2, 0) + part(2, 0) + part(0, -2) + part(0, 2)
    return 8.0 * part(0, 0) - 4.0 / 3.0 * near + 1.0 / 12.0 * far


def window(padded_array, axis_pos, offset):
    starts = [0, 2, 2, 2]
    limits = [
        padded_array.shape[0],
        padded_array.shape[1] - 2,
        padded_array.shape[2] - 2,
        padded_array.shape[3] - 2,
    ]
    starts[axis_pos] = offset
    limits[axis_pos] = offset + padded_array.shape[axis_pos] - 4
    return lax.slice(padded_array, tuple(starts), tuple(limits))


def stencil_apply(padded_array):
    total = 8.0 * window(padded_array, 1, 2)
    for axis_pos in (1, 2, 3):
        near = window(padded_array, axis_pos, 1) + window(padded_array, axis_pos, 3)
        far = window(padded_array, axis_pos, 0) + window(padded_array, axis_pos, 4)
        total = total - 4.0 / 3.0 * near + 1.0 / 12.0 * far
    return 0.25 * total


def exchange(payloads, axes):
    sizes = [lax.axis_size(axis) for axis in axes]
    groups = {}
    for offset in payloads:
        key = tuple(o % s for o, s in zip(offset, sizes))
        groups.setdefault(key, []).append(offset)
    arrived = {}
    previous = None
    for key, offsets in groups.items():
        parts = [part for offset in offsets for part in payloads[offset]]
        if previous is not None:
            previous, parts = lax.optimization_barrier((previous, parts))
        rows = jnp.concatenate([as_rows(part) for part in parts])
        previous = rows
        if any(key):
            pairs = []
            for source in np.ndindex(*sizes):
                target = tuple((c + k) % s for c, k, s in zip(source, key, sizes))
                pairs.append((int(np.ravel_multi_index(source, sizes)), int(np.ravel_multi_index(target, sizes))))
            rows = lax.ppermute(rows, tuple(axes), pairs)
        start = 0
        for offset in offsets:
            parts = []
            for part in payloads[offset]:
                count = -(-part.size // 128)
                parts.append(rows[start : start + count].reshape(-1)[: part.size].reshape(part.shape))
                start += count
            arrived[offset] = parts
    return arrived


def as_rows(part):
    if part.shape[-1] == 128:
        return part.reshape(-1, 128)
    flat = part.reshape(-1)
    return jnp.pad(flat, (0, -flat.shape[0] % 128)).reshape(-1, 128)


def placed(block, starts, shape):
    return jnp.pad(block, [(b, s - b - d) for b, d, s in zip(starts, block.shape, shape)])


def plane_round_and_stencil(extended, nx, ny):
    e = extended
    payloads = {
        (1, 0): (e[:, nx - 2 : nx, 2 : ny + 2, 2:-2], e[:-1, nx : nx + 1, 2 : ny + 3]),
        (-1, 0): (e[:, 0:2, 2 : ny + 2, 2:-2],),
        (0, 1): (e[:, :, ny : ny + 3],),
        (0, -1): (e[:, 0:nx, 2:4],),
        (1, 1): (e[:, nx - 2 : nx + 1, ny + 2], e[:, nx, ny : ny + 2]),
        (-1, 1): (e[:, 0:2, ny + 2],),
        (1, -1): (e[:, nx, 2:4],),
    }
    got = exchange(payloads, ("gx", "gy"))
    channels, _, _, depth = e.shape
    shape = (channels, nx + 4, ny + 4, depth)

    def at(block, layer, row, col=0):
        return placed(block, (0, layer, row, col), shape)

    halo_x, fold_x = got[(1, 0)]
    corner_x, corner_y = got[(1, 1)]
    total = (
        at(e, 2, 0)
        + at(halo_x, 0, 2, 2)
        + at(fold_x, 2, 2)
        + at(got[(-1, 0)][0], nx + 2, 2, 2)
        + at(got[(0, 1)][0], 2, 0)
        + at(got[(0, -1)][0], 2, ny + 2)
        + at(corner_x[:, :, None], 0, 2)
        + at(corner_y[:, None], 2, 0)
        + at(got[(-1, 1)][0][:, :, None], nx + 2, 2)
        + at(got[(1, -1)][0][:, None], 2, ny + 2)
    )
    masked = total[:-1] * total[-1]
    inner = z_terms(e[:-1, 1:nx, 3 : ny + 2] * e[-1, 1:nx, 3 : ny + 2])
    rows = jnp.concatenate([z_terms(masked[:, 3 : nx + 2, 2:3]), inner], axis=2)
    result = jnp.concatenate([z_terms(masked[:, 2:3, 2 : ny + 2]), rows], axis=1)
    for axis_pos in (1, 2):
        near = window(masked, axis_pos, 1) + window(masked, axis_pos, 3)
        far = window(masked, axis_pos, 0) + window(masked, axis_pos, 4)
        result = result - 4.0 / 3.0 * near + 1.0 / 12.0 * far
    return 0.25 * result


def z_terms(block):
    nz = block.shape[-1] - 4

    def part(dz):
        return block[..., 2 + dz : nz + 2 + dz]

    return 8.0 * part(0) - 4.0 / 3.0 * (part(-1) + part(1)) + 1.0 / 12.0 * (part(-2) + part(2))


def body(edge_coeffs_x, edge_coeffs_y, edge_coeffs_z, flips, flags):
    closed_map, open_map = basis_tables()
    nx, ny, nz = flags.shape
    precise = lax.Precision.HIGHEST
    inputs = [
        (edge_coeffs_x, flips[0], open_map, closed_map, closed_map),
        (edge_coeffs_y, flips[1], closed_map, open_map, closed_map),
        (edge_coeffs_z, flips[2], closed_map, closed_map, open_map),
    ]
    length = nz + 4
    up_places = [nz, nz + 1, nz + 2]
    down_places = [2, 3]
    planars = []
    depths = []
    slabs = []
    for coef, flip, table_x, table_y, table_z in inputs:
        planar = planar_part(coef, flip, table_x, table_y, table_z.shape[1])
        depth_map = depth_map_of(table_z, coef.shape[4])
        edge_map = jnp.asarray(depth_map[up_places + down_places], jnp.float32)
        planars.append(planar)
        depths.append(depth_map)
        slabs.append(
            lax.dot_general(edge_map, planar, (((1,), (1,)), ((), ())), precision=lax.Precision.HIGH)
        )
    keep_own = (1 - flags).astype(jnp.float32)
    keep = jnp.pad(keep_own, ((0, 1), (2, 2), (2, 2)))
    keep_layers = [
        lax.slice_in_dim(keep_own, nz - 2, nz, axis=2),
        jnp.zeros_like(lax.slice_in_dim(keep_own, 0, 1, axis=2)),
        lax.slice_in_dim(keep_own, 0, 2, axis=2),
    ]
    keep_layers = jnp.moveaxis(jnp.concatenate(keep_layers, axis=2), 2, 0)
    slabs.append(jnp.pad(keep_layers, ((0, 0), (0, 1), (2, 2))).reshape(5, -1))
    slabs = jnp.stack(slabs)
    up = slabs[:, :3].reshape(-1, slabs.shape[2])
    down = slabs[:, 3:].reshape(-1, slabs.shape[2])
    from_prev, from_next = both_ways(up, down, "gz")
    own_parts = lax.optimization_barrier(
        [
            jnp.dot(planar, jnp.asarray(depth.T, jnp.float32), precision=lax.Precision.HIGH)
            for planar, depth in zip(planars, depths)
        ]
    )
    arrived = jnp.concatenate(
        [from_prev.reshape(4, 3, -1), from_next.reshape(4, 2, -1)], axis=1
    )
    place = np.zeros((5, length))
    for row, col in enumerate([0, 1, 2, nz + 2, nz + 3]):
        place[row, col] = 1.0
    place = jnp.asarray(place, jnp.float32)
    nodal = []
    for comp in range(3):
        folded = lax.dot_general(arrived[comp], place, (((0,), (0,)), ((), ())), precision=precise)
        nodal.append((own_parts[comp] + folded).reshape(nx + 1, ny + 4, length))
    keep_in = jnp.moveaxis(arrived[3].reshape(5, nx + 1, ny + 4), 0, 2)
    keep = keep + jnp.pad(keep_in[..., :3], ((0, 0), (0, 0), (0, length - 3))) + jnp.pad(
        keep_in[..., 3:], ((0, 0), (0, 0), (nz + 2, 0))
    )
    extended = jnp.stack(nodal + [keep])
    return plane_round_and_stencil(extended, nx, ny)


def solution(mesh):
    in_specs = (
        P("gx", None, "gy", None, "gz"),
        P("gx", None, "gy", None, "gz"),
        P("gx", None, "gy", None, "gz"),
        P(None, "gx", "gy", "gz"),
        P("gx", "gy", "gz"),
    )
    out_specs = P(None, "gx", "gy", "gz")
    return jax.shard_map(body, mesh=mesh, in_specs=in_specs, out_specs=out_specs, check_vma=False)
```

```python
import math

import jax
import jax.numpy as jnp
import numpy as np
from jax import lax
from jax.sharding import PartitionSpec as P


def lagrange_table(points, targets):
    table = np.ones((len(targets), len(points)))
    for row_pos in range(len(targets)):
        for col_pos in range(len(points)):
            for other in range(len(points)):
                if other != col_pos:
                    table[row_pos, col_pos] *= (targets[row_pos] - points[other]) / (
                        points[col_pos] - points[other]
                    )
    return table


def basis_tables():
    spread = math.sqrt(3.0 / 7.0)
    targets = [0.0, (1.0 - spread) / 2.0, 0.5, (1.0 + spread) / 2.0, 1.0]
    closed = [0.0, 0.25, 0.5, 0.75, 1.0]
    inner = math.sqrt(3.0 / 7.0 - 2.0 / 7.0 * math.sqrt(6.0 / 5.0))
    outer = math.sqrt(3.0 / 7.0 + 2.0 / 7.0 * math.sqrt(6.0 / 5.0))
    gauss = [(1.0 - outer) / 2.0, (1.0 - inner) / 2.0, (1.0 + inner) / 2.0, (1.0 + outer) / 2.0]
    closed_map = np.asarray(lagrange_table(closed, targets), dtype=np.float32).astype(np.float64)
    open_map = np.asarray(lagrange_table(gauss, targets), dtype=np.float32).astype(np.float64)
    return closed_map, open_map


def assembly_matrix(table, count):
    size = table.shape[1]
    matrix = np.zeros((4 * count + 1, count * size))
    for elem_pos in range(count):
        matrix[4 * elem_pos : 4 * elem_pos + 5, size * elem_pos : size * elem_pos + size] += table
    return matrix


def planar_part(coef, flip, table_x, table_y, size_z):
    ex_count, size_x, ey_count, size_y, merged = coef.shape
    orient = jnp.repeat((1 - 2 * flip).astype(jnp.float32), size_z, axis=2)
    signed = (coef * orient[:, None, :, None, :]).reshape(ex_count * size_x * ey_count * size_y, merged)
    rows_y = np.pad(assembly_matrix(table_y, ey_count), ((2, 1), (0, 0)))
    plane_map = np.kron(assembly_matrix(table_x, ex_count), rows_y)
    return jnp.dot(jnp.asarray(plane_map, jnp.float32), signed, precision=lax.Precision.HIGH)


def depth_map_of(table_z, merged):
    return np.pad(assembly_matrix(table_z, merged // table_z.shape[1]), ((2, 1), (0, 0)))


def shifted(block, axis, step=1):
    count = lax.axis_size(axis)
    if count == 1:
        return block
    return lax.ppermute(block, axis, [(i, (i + step) % count) for i in range(count)])


def both_ways(up, down, axis):
    if lax.axis_size(axis) <= 2:
        both = shifted(jnp.concatenate([up, down]), axis)
        return both[: up.shape[0]], both[up.shape[0] :]
    return shifted(up, axis), shifted(down, axis, -1)


def to_wire(slab, dim):
    layers = jnp.moveaxis(slab, dim, 0)
    return layers.reshape(layers.shape[0] * layers.shape[1], -1), layers.shape


def from_wire(rows, shape, dim):
    return jnp.moveaxis(rows.reshape(shape), 0, dim)


def fold_and_halo(extended, axis, dim):
    length = extended.shape[dim]
    n = length - 4
    up, up_shape = to_wire(lax.slice_in_dim(extended, n, n + 3, axis=dim), dim)
    down, down_shape = to_wire(lax.slice_in_dim(extended, 2, 4, axis=dim), dim)
    from_prev, from_next = both_ways(up, down, axis)
    widths_prev = [(0, 0)] * extended.ndim
    widths_prev[dim] = (0, length - 3)
    widths_next = [(0, 0)] * extended.ndim
    widths_next[dim] = (n + 2, 0)
    return (
        extended
        + jnp.pad(from_wire(from_prev, up_shape, dim), widths_prev)
        + jnp.pad(from_wire(from_next, down_shape, dim), widths_next)
    )


def cross_rows(plane, ny, nz):
    own = plane[:, 2 : ny + 2, 2 : nz + 2]
    strips_y = jnp.concatenate([plane[:, 0:2, 2 : nz + 2], plane[:, ny + 2 :, 2 : nz + 2]], axis=1)
    strips_z = jnp.concatenate([plane[:, 2 : ny + 2, 0:2], plane[:, 2 : ny + 2, nz + 2 :]], axis=2)
    strips_z = jnp.swapaxes(strips_z, 1, 2).reshape(-1)
    strips_z = jnp.pad(strips_z, (0, -strips_z.shape[0] % nz))
    return [own.reshape(-1, nz), strips_y.reshape(-1, nz), strips_z.reshape(-1, nz)]


def cross_plane(own, strips_y, strips_z):
    middle = jnp.concatenate([strips_z[..., 0:2], own, strips_z[..., 2:4]], axis=2)
    widths = ((0, 0), (0, 0), (2, 2))
    return jnp.concatenate(
        [jnp.pad(strips_y[:, 0:2], widths), middle, jnp.pad(strips_y[:, 2:4], widths)], axis=1
    )


def last_round_and_stencil(extended, axis, ny, nz):
    n = extended.shape[1] - 1
    comps = extended.shape[0] - 1
    data = extended[:comps]
    keep = extended[comps]

    def own(block):
        return block[..., 2 : ny + 2, 2 : nz + 2]

    halo_up = own(data[:, n - 2 : n] * keep[n - 2 : n])
    halo_down = own(data[:, 1] * keep[1])
    up_parts = [halo_up.reshape(-1, nz)] + cross_rows(data[:, n], ny, nz)
    down_parts = [own(data[:, 0]).reshape(-1, nz), own(keep[0]), halo_down.reshape(-1, nz)]
    up = jnp.concatenate(up_parts)
    down = jnp.concatenate(down_parts)
    from_prev, from_next = both_ways(up, down, axis)

    sizes = [part.shape[0] for part in up_parts]
    marks = np.cumsum([0] + sizes)
    prev_halo = from_prev[marks[0] : marks[1]].reshape(comps, 2, ny, nz)
    prev_own = from_prev[marks[1] : marks[2]].reshape(comps, ny, nz)
    prev_strips_y = from_prev[marks[2] : marks[3]].reshape(comps, 4, nz)
    prev_strips_z = from_prev[marks[3] : marks[4]].reshape(-1)[: comps * 4 * ny]
    prev_strips_z = jnp.swapaxes(prev_strips_z.reshape(comps, 4, ny), 1, 2)
    fold_in = cross_plane(prev_own, prev_strips_y, prev_strips_z)

    plane_rows = comps * ny
    next_fold = from_next[:plane_rows].reshape(comps, ny, nz)
    next_keep = from_next[plane_rows : plane_rows + ny]
    next_halo = from_next[plane_rows + ny :].reshape(comps, ny, nz)

    inner = data[:, 1:n] * keep[1:n]
    first = (data[:, 0] + fold_in) * keep[0]
    last = (own(data[:, n]) + next_fold) * next_keep
    across = jnp.concatenate([yz_terms(first[:, None], ny, nz), yz_terms(inner, ny, nz)], axis=1)
    column = jnp.concatenate(
        [prev_halo, own(first)[:, None], own(inner), last[:, None], next_halo[:, None]], axis=1
    )
    near = column[:, 1 : n + 1] + column[:, 3 : n + 3]
    far = column[:, 0:n] + column[:, 4 : n + 4]
    return 0.25 * (across - 4.0 / 3.0 * near + 1.0 / 12.0 * far)


def yz_terms(block, ny, nz):
    def part(dy, dz):
        return block[..., 2 + dy : ny + 2 + dy, 2 + dz : nz + 2 + dz]

    near = part(-1, 0) + part(1, 0) + part(0, -1) + part(0, 1)
    far = part(-2, 0) + part(2, 0) + part(0, -2) + part(0, 2)
    return 8.0 * part(0, 0) - 4.0 / 3.0 * near + 1.0 / 12.0 * far


def window(padded_array, axis_pos, offset):
    starts = [0, 2, 2, 2]
    limits = [
        padded_array.shape[0],
        padded_array.shape[1] - 2,
        padded_array.shape[2] - 2,
        padded_array.shape[3] - 2,
    ]
    starts[axis_pos] = offset
    limits[axis_pos] = offset + padded_array.shape[axis_pos] - 4
    return lax.slice(padded_array, tuple(starts), tuple(limits))


def stencil_apply(padded_array):
    total = 8.0 * window(padded_array, 1, 2)
    for axis_pos in (1, 2, 3):
        near = window(padded_array, axis_pos, 1) + window(padded_array, axis_pos, 3)
        far = window(padded_array, axis_pos, 0) + window(padded_array, axis_pos, 4)
        total = total - 4.0 / 3.0 * near + 1.0 / 12.0 * far
    return 0.25 * total


def exchange(payloads, axes):
    sizes = [lax.axis_size(axis) for axis in axes]
    groups = {}
    for offset in payloads:
        key = tuple(o % s for o, s in zip(offset, sizes))
        groups.setdefault(key, []).append(offset)
    arrived = {}
    previous = None
    for key, offsets in groups.items():
        parts = [part for offset in offsets for part in payloads[offset]]
        if previous is not None:
            previous, parts = lax.optimization_barrier((previous, parts))
        rows = jnp.concatenate([as_rows(part) for part in parts])
        previous = rows
        if any(key):
            pairs = []
            for source in np.ndindex(*sizes):
                target = tuple((c + k) % s for c, k, s in zip(source, key, sizes))
                pairs.append((int(np.ravel_multi_index(source, sizes)), int(np.ravel_multi_index(target, sizes))))
            rows = lax.ppermute(rows, tuple(axes), pairs)
        start = 0
        for offset in offsets:
            parts = []
            for part in payloads[offset]:
                count = -(-part.size // 128)
                parts.append(rows[start : start + count].reshape(-1)[: part.size].reshape(part.shape))
                start += count
            arrived[offset] = parts
    return arrived


def as_rows(part):
    if part.shape[-1] == 128:
        return part.reshape(-1, 128)
    flat = part.reshape(-1)
    return jnp.pad(flat, (0, -flat.shape[0] % 128)).reshape(-1, 128)


def placed(block, starts, shape):
    return jnp.pad(block, [(b, s - b - d) for b, d, s in zip(starts, block.shape, shape)])


def plane_round_and_stencil(extended, nx, ny):
    e = extended
    payloads = {
        (1, 0): (
            e[:, nx - 2 : nx, 2 : ny + 2, 2:-2],
            e[:-1, nx : nx + 1, 2 : ny + 2, 2:-2],
            e[:-1, nx, ny + 2],
            e[:-1, nx : nx + 1, 2 : ny + 2, 0:2],
            e[:-1, nx : nx + 1, 2 : ny + 2, -2:],
        ),
        (-1, 0): (e[:, 0:2, 2 : ny + 2, 2:-2],),
        (0, 1): (e[:, :, ny : ny + 3],),
        (0, -1): (e[:, 0:nx, 2:4],),
        (1, 1): (e[:, nx - 2 : nx + 1, ny + 2], e[:, nx, ny : ny + 2]),
        (-1, 1): (e[:, 0:2, ny + 2],),
        (1, -1): (e[:, nx, 2:4],),
    }
    got = exchange(payloads, ("gx", "gy"))
    channels, _, _, depth = e.shape
    shape = (channels, nx + 4, ny + 4, depth)

    def at(block, layer, row, col=0):
        return placed(block, (0, layer, row, col), shape)

    halo_x, fold_own, fold_row, fold_low, fold_high = got[(1, 0)]
    corner_x, corner_y = got[(1, 1)]
    total = (
        at(e, 2, 0)
        + at(halo_x, 0, 2, 2)
        + at(fold_own, 2, 2, 2)
        + at(fold_row[:, None, None], 2, ny + 2)
        + at(fold_low, 2, 2)
        + at(fold_high, 2, 2, depth - 2)
        + at(got[(-1, 0)][0], nx + 2, 2, 2)
        + at(got[(0, 1)][0], 2, 0)
        + at(got[(0, -1)][0], 2, ny + 2)
        + at(corner_x[:, :, None], 0, 2)
        + at(corner_y[:, None], 2, 0)
        + at(got[(-1, 1)][0][:, :, None], nx + 2, 2)
        + at(got[(1, -1)][0][:, None], 2, ny + 2)
    )
    masked = total[:-1] * total[-1]
    inner = z_terms(e[:-1, 1:nx, 3 : ny + 2] * e[-1, 1:nx, 3 : ny + 2])
    rows = jnp.concatenate([z_terms(masked[:, 3 : nx + 2, 2:3]), inner], axis=2)
    result = jnp.concatenate([z_terms(masked[:, 2:3, 2 : ny + 2]), rows], axis=1)
    for axis_pos in (1, 2):
        near = window(masked, axis_pos, 1) + window(masked, axis_pos, 3)
        far = window(masked, axis_pos, 0) + window(masked, axis_pos, 4)
        result = result - 4.0 / 3.0 * near + 1.0 / 12.0 * far
    return 0.25 * result


def z_terms(block):
    nz = block.shape[-1] - 4

    def part(dz):
        return block[..., 2 + dz : nz + 2 + dz]

    return 8.0 * part(0) - 4.0 / 3.0 * (part(-1) + part(1)) + 1.0 / 12.0 * (part(-2) + part(2))


def body(edge_coeffs_x, edge_coeffs_y, edge_coeffs_z, flips, flags):
    closed_map, open_map = basis_tables()
    nx, ny, nz = flags.shape
    precise = lax.Precision.HIGHEST
    inputs = [
        (edge_coeffs_x, flips[0], open_map, closed_map, closed_map),
        (edge_coeffs_y, flips[1], closed_map, open_map, closed_map),
        (edge_coeffs_z, flips[2], closed_map, closed_map, open_map),
    ]
    length = nz + 4
    up_places = [nz, nz + 1, nz + 2]
    down_places = [2, 3]
    planars = []
    depths = []
    slabs = []
    for coef, flip, table_x, table_y, table_z in inputs:
        planar = planar_part(coef, flip, table_x, table_y, table_z.shape[1])
        depth_map = depth_map_of(table_z, coef.shape[4])
        edge_map = jnp.asarray(depth_map[up_places + down_places], jnp.float32)
        planars.append(planar)
        depths.append(depth_map)
        slabs.append(
            lax.dot_general(edge_map, planar, (((1,), (1,)), ((), ())), precision=lax.Precision.HIGH)
        )
    keep_own = (1 - flags).astype(jnp.float32)
    keep = jnp.pad(keep_own, ((0, 1), (2, 2), (2, 2)))
    keep_layers = [
        lax.slice_in_dim(keep_own, nz - 2, nz, axis=2),
        jnp.zeros_like(lax.slice_in_dim(keep_own, 0, 1, axis=2)),
        lax.slice_in_dim(keep_own, 0, 2, axis=2),
    ]
    keep_layers = jnp.moveaxis(jnp.concatenate(keep_layers, axis=2), 2, 0)
    slabs.append(jnp.pad(keep_layers, ((0, 0), (0, 1), (2, 2))).reshape(5, -1))
    slabs = jnp.stack(slabs)
    up = slabs[:, :3].reshape(-1, slabs.shape[2])
    down = slabs[:, 3:].reshape(-1, slabs.shape[2])
    from_prev, from_next = both_ways(up, down, "gz")
    own_parts = lax.optimization_barrier(
        [
            jnp.dot(planar, jnp.asarray(depth.T, jnp.float32), precision=lax.Precision.HIGH)
            for planar, depth in zip(planars, depths)
        ]
    )
    arrived = jnp.concatenate(
        [from_prev.reshape(4, 3, -1), from_next.reshape(4, 2, -1)], axis=1
    )
    place = np.zeros((5, length))
    for row, col in enumerate([0, 1, 2, nz + 2, nz + 3]):
        place[row, col] = 1.0
    place = jnp.asarray(place, jnp.float32)
    nodal = []
    for comp in range(3):
        folded = lax.dot_general(arrived[comp], place, (((0,), (0,)), ((), ())), precision=precise)
        nodal.append((own_parts[comp] + folded).reshape(nx + 1, ny + 4, length))
    keep_in = jnp.moveaxis(arrived[3].reshape(5, nx + 1, ny + 4), 0, 2)
    keep = keep + jnp.pad(keep_in[..., :3], ((0, 0), (0, 0), (0, length - 3))) + jnp.pad(
        keep_in[..., 3:], ((0, 0), (0, 0), (nz + 2, 0))
    )
    extended = jnp.stack(nodal + [keep])
    return plane_round_and_stencil(extended, nx, ny)


def solution(mesh):
    in_specs = (
        P("gx", None, "gy", None, "gz"),
        P("gx", None, "gy", None, "gz"),
        P("gx", None, "gy", None, "gz"),
        P(None, "gx", "gy", "gz"),
        P("gx", "gy", "gz"),
    )
    out_specs = P(None, "gx", "gy", "gz")
    return jax.shard_map(body, mesh=mesh, in_specs=in_specs, out_specs=out_specs, check_vma=False)
```

```python
import math

import jax
import jax.numpy as jnp
import numpy as np
from jax import lax
from jax.sharding import PartitionSpec as P


def lagrange_table(points, targets):
    table = np.ones((len(targets), len(points)))
    for row_pos in range(len(targets)):
        for col_pos in range(len(points)):
            for other in range(len(points)):
                if other != col_pos:
                    table[row_pos, col_pos] *= (targets[row_pos] - points[other]) / (
                        points[col_pos] - points[other]
                    )
    return table


def basis_tables():
    spread = math.sqrt(3.0 / 7.0)
    targets = [0.0, (1.0 - spread) / 2.0, 0.5, (1.0 + spread) / 2.0, 1.0]
    closed = [0.0, 0.25, 0.5, 0.75, 1.0]
    inner = math.sqrt(3.0 / 7.0 - 2.0 / 7.0 * math.sqrt(6.0 / 5.0))
    outer = math.sqrt(3.0 / 7.0 + 2.0 / 7.0 * math.sqrt(6.0 / 5.0))
    gauss = [(1.0 - outer) / 2.0, (1.0 - inner) / 2.0, (1.0 + inner) / 2.0, (1.0 + outer) / 2.0]
    closed_map = np.asarray(lagrange_table(closed, targets), dtype=np.float32).astype(np.float64)
    open_map = np.asarray(lagrange_table(gauss, targets), dtype=np.float32).astype(np.float64)
    return closed_map, open_map


def assembly_matrix(table, count):
    size = table.shape[1]
    matrix = np.zeros((4 * count + 1, count * size))
    for elem_pos in range(count):
        matrix[4 * elem_pos : 4 * elem_pos + 5, size * elem_pos : size * elem_pos + size] += table
    return matrix


def planar_part(coef, flip, table_x, table_y, size_z):
    ex_count, size_x, ey_count, size_y, merged = coef.shape
    orient = jnp.repeat((1 - 2 * flip).astype(jnp.float32), size_z, axis=2)
    signed = (coef * orient[:, None, :, None, :]).reshape(ex_count * size_x * ey_count * size_y, merged)
    rows_y = np.pad(assembly_matrix(table_y, ey_count), ((2, 1), (0, 0)))
    plane_map = np.kron(assembly_matrix(table_x, ex_count), rows_y)
    return jnp.dot(jnp.asarray(plane_map, jnp.float32), signed, precision=lax.Precision.HIGH)


def depth_map_of(table_z, merged):
    return np.pad(assembly_matrix(table_z, merged // table_z.shape[1]), ((2, 1), (0, 0)))


def shifted(block, axis, step=1):
    count = lax.axis_size(axis)
    if count == 1:
        return block
    return lax.ppermute(block, axis, [(i, (i + step) % count) for i in range(count)])


def both_ways(up, down, axis):
    if lax.axis_size(axis) <= 2:
        both = shifted(jnp.concatenate([up, down]), axis)
        return both[: up.shape[0]], both[up.shape[0] :]
    return shifted(up, axis), shifted(down, axis, -1)


def to_wire(slab, dim):
    layers = jnp.moveaxis(slab, dim, 0)
    return layers.reshape(layers.shape[0] * layers.shape[1], -1), layers.shape


def from_wire(rows, shape, dim):
    return jnp.moveaxis(rows.reshape(shape), 0, dim)


def fold_and_halo(extended, axis, dim):
    length = extended.shape[dim]
    n = length - 4
    up, up_shape = to_wire(lax.slice_in_dim(extended, n, n + 3, axis=dim), dim)
    down, down_shape = to_wire(lax.slice_in_dim(extended, 2, 4, axis=dim), dim)
    from_prev, from_next = both_ways(up, down, axis)
    widths_prev = [(0, 0)] * extended.ndim
    widths_prev[dim] = (0, length - 3)
    widths_next = [(0, 0)] * extended.ndim
    widths_next[dim] = (n + 2, 0)
    return (
        extended
        + jnp.pad(from_wire(from_prev, up_shape, dim), widths_prev)
        + jnp.pad(from_wire(from_next, down_shape, dim), widths_next)
    )


def cross_rows(plane, ny, nz):
    own = plane[:, 2 : ny + 2, 2 : nz + 2]
    strips_y = jnp.concatenate([plane[:, 0:2, 2 : nz + 2], plane[:, ny + 2 :, 2 : nz + 2]], axis=1)
    strips_z = jnp.concatenate([plane[:, 2 : ny + 2, 0:2], plane[:, 2 : ny + 2, nz + 2 :]], axis=2)
    strips_z = jnp.swapaxes(strips_z, 1, 2).reshape(-1)
    strips_z = jnp.pad(strips_z, (0, -strips_z.shape[0] % nz))
    return [own.reshape(-1, nz), strips_y.reshape(-1, nz), strips_z.reshape(-1, nz)]


def cross_plane(own, strips_y, strips_z):
    middle = jnp.concatenate([strips_z[..., 0:2], own, strips_z[..., 2:4]], axis=2)
    widths = ((0, 0), (0, 0), (2, 2))
    return jnp.concatenate(
        [jnp.pad(strips_y[:, 0:2], widths), middle, jnp.pad(strips_y[:, 2:4], widths)], axis=1
    )


def last_round_and_stencil(extended, axis, ny, nz):
    n = extended.shape[1] - 1
    comps = extended.shape[0] - 1
    data = extended[:comps]
    keep = extended[comps]

    def own(block):
        return block[..., 2 : ny + 2, 2 : nz + 2]

    halo_up = own(data[:, n - 2 : n] * keep[n - 2 : n])
    halo_down = own(data[:, 1] * keep[1])
    up_parts = [halo_up.reshape(-1, nz)] + cross_rows(data[:, n], ny, nz)
    down_parts = [own(data[:, 0]).reshape(-1, nz), own(keep[0]), halo_down.reshape(-1, nz)]
    up = jnp.concatenate(up_parts)
    down = jnp.concatenate(down_parts)
    from_prev, from_next = both_ways(up, down, axis)

    sizes = [part.shape[0] for part in up_parts]
    marks = np.cumsum([0] + sizes)
    prev_halo = from_prev[marks[0] : marks[1]].reshape(comps, 2, ny, nz)
    prev_own = from_prev[marks[1] : marks[2]].reshape(comps, ny, nz)
    prev_strips_y = from_prev[marks[2] : marks[3]].reshape(comps, 4, nz)
    prev_strips_z = from_prev[marks[3] : marks[4]].reshape(-1)[: comps * 4 * ny]
    prev_strips_z = jnp.swapaxes(prev_strips_z.reshape(comps, 4, ny), 1, 2)
    fold_in = cross_plane(prev_own, prev_strips_y, prev_strips_z)

    plane_rows = comps * ny
    next_fold = from_next[:plane_rows].reshape(comps, ny, nz)
    next_keep = from_next[plane_rows : plane_rows + ny]
    next_halo = from_next[plane_rows + ny :].reshape(comps, ny, nz)

    inner = data[:, 1:n] * keep[1:n]
    first = (data[:, 0] + fold_in) * keep[0]
    last = (own(data[:, n]) + next_fold) * next_keep
    across = jnp.concatenate([yz_terms(first[:, None], ny, nz), yz_terms(inner, ny, nz)], axis=1)
    column = jnp.concatenate(
        [prev_halo, own(first)[:, None], own(inner), last[:, None], next_halo[:, None]], axis=1
    )
    near = column[:, 1 : n + 1] + column[:, 3 : n + 3]
    far = column[:, 0:n] + column[:, 4 : n + 4]
    return 0.25 * (across - 4.0 / 3.0 * near + 1.0 / 12.0 * far)


def yz_terms(block, ny, nz):
    def part(dy, dz):
        return block[..., 2 + dy : ny + 2 + dy, 2 + dz : nz + 2 + dz]

    near = part(-1, 0) + part(1, 0) + part(0, -1) + part(0, 1)
    far = part(-2, 0) + part(2, 0) + part(0, -2) + part(0, 2)
    return 8.0 * part(0, 0) - 4.0 / 3.0 * near + 1.0 / 12.0 * far


def window(padded_array, axis_pos, offset):
    starts = [0, 2, 2, 2]
    limits = [
        padded_array.shape[0],
        padded_array.shape[1] - 2,
        padded_array.shape[2] - 2,
        padded_array.shape[3] - 2,
    ]
    starts[axis_pos] = offset
    limits[axis_pos] = offset + padded_array.shape[axis_pos] - 4
    return lax.slice(padded_array, tuple(starts), tuple(limits))


def stencil_apply(padded_array):
    total = 8.0 * window(padded_array, 1, 2)
    for axis_pos in (1, 2, 3):
        near = window(padded_array, axis_pos, 1) + window(padded_array, axis_pos, 3)
        far = window(padded_array, axis_pos, 0) + window(padded_array, axis_pos, 4)
        total = total - 4.0 / 3.0 * near + 1.0 / 12.0 * far
    return 0.25 * total


def exchange(payloads, axes):
    sizes = [lax.axis_size(axis) for axis in axes]
    groups = {}
    for offset in payloads:
        key = tuple(o % s for o, s in zip(offset, sizes))
        groups.setdefault(key, []).append(offset)
    arrived = {}
    previous = None
    for key, offsets in groups.items():
        parts = [part for offset in offsets for part in payloads[offset]]
        if previous is not None:
            previous, parts = lax.optimization_barrier((previous, parts))
        rows = jnp.concatenate([as_rows(part) for part in parts])
        previous = rows
        if any(key):
            pairs = []
            for source in np.ndindex(*sizes):
                target = tuple((c + k) % s for c, k, s in zip(source, key, sizes))
                pairs.append((int(np.ravel_multi_index(source, sizes)), int(np.ravel_multi_index(target, sizes))))
            rows = lax.ppermute(rows, tuple(axes), pairs)
        start = 0
        for offset in offsets:
            parts = []
            for part in payloads[offset]:
                count = -(-part.size // 128)
                parts.append(rows[start : start + count].reshape(-1)[: part.size].reshape(part.shape))
                start += count
            arrived[offset] = parts
    return arrived


def as_rows(part):
    if part.shape[-1] == 128:
        return part.reshape(-1, 128)
    flat = part.reshape(-1)
    return jnp.pad(flat, (0, -flat.shape[0] % 128)).reshape(-1, 128)


def placed(block, starts, shape):
    return jnp.pad(block, [(b, s - b - d) for b, d, s in zip(starts, block.shape, shape)])


def plane_round_and_stencil(extended, nx, ny):
    e = extended
    payloads = {
        (1, 0): (e[:, nx - 2 : nx, 2 : ny + 2, 2:-2], e[:-1, nx : nx + 1, 2 : ny + 3]),
        (-1, 0): (e[:, 0:2, 2 : ny + 2, 2:-2],),
        (0, 1): (e[:, :, ny : ny + 3],),
        (0, -1): (e[:, 0:nx, 2:4],),
        (1, 1): (e[:, nx - 2 : nx + 1, ny + 2], e[:, nx, ny : ny + 2]),
        (-1, 1): (e[:, 0:2, ny + 2],),
        (1, -1): (e[:, nx, 2:4],),
    }
    got = exchange(payloads, ("gx", "gy"))
    channels, _, _, depth = e.shape
    shape = (channels, nx + 4, ny + 4, depth)

    def at(block, layer, row, col=0):
        return placed(block, (0, layer, row, col), shape)

    halo_x, fold_x = got[(1, 0)]
    corner_x, corner_y = got[(1, 1)]
    total = (
        at(e, 2, 0)
        + at(halo_x, 0, 2, 2)
        + at(fold_x, 2, 2)
        + at(got[(-1, 0)][0], nx + 2, 2, 2)
        + at(got[(0, 1)][0], 2, 0)
        + at(got[(0, -1)][0], 2, ny + 2)
        + at(corner_x[:, :, None], 0, 2)
        + at(corner_y[:, None], 2, 0)
        + at(got[(-1, 1)][0][:, :, None], nx + 2, 2)
        + at(got[(1, -1)][0][:, None], 2, ny + 2)
    )
    masked = total[:-1] * total[-1]
    inner = z_terms(e[:-1, 1:nx, 3 : ny + 2] * e[-1, 1:nx, 3 : ny + 2])
    rows = jnp.concatenate([z_terms(masked[:, 3 : nx + 2, 2:3]), inner], axis=2)
    result = jnp.concatenate([z_terms(masked[:, 2:3, 2 : ny + 2]), rows], axis=1)
    for axis_pos in (1, 2):
        near = window(masked, axis_pos, 1) + window(masked, axis_pos, 3)
        far = window(masked, axis_pos, 0) + window(masked, axis_pos, 4)
        result = result - 4.0 / 3.0 * near + 1.0 / 12.0 * far
    return 0.25 * result


def z_terms(block):
    nz = block.shape[-1] - 4

    def part(dz):
        return block[..., 2 + dz : nz + 2 + dz]

    return 8.0 * part(0) - 4.0 / 3.0 * (part(-1) + part(1)) + 1.0 / 12.0 * (part(-2) + part(2))


def body(edge_coeffs_x, edge_coeffs_y, edge_coeffs_z, flips, flags):
    closed_map, open_map = basis_tables()
    nx, ny, nz = flags.shape
    precise = lax.Precision.HIGHEST
    inputs = [
        (edge_coeffs_x, flips[0], open_map, closed_map, closed_map),
        (edge_coeffs_y, flips[1], closed_map, open_map, closed_map),
        (edge_coeffs_z, flips[2], closed_map, closed_map, open_map),
    ]
    length = nz + 4
    up_places = [nz, nz + 1, nz + 2]
    down_places = [2, 3]
    planars = []
    depths = []
    slabs = []
    for coef, flip, table_x, table_y, table_z in inputs:
        planar = planar_part(coef, flip, table_x, table_y, table_z.shape[1])
        depth_map = depth_map_of(table_z, coef.shape[4])
        edge_map = jnp.asarray(depth_map[up_places + down_places], jnp.float32)
        planars.append(planar)
        depths.append(depth_map)
        slabs.append(
            lax.dot_general(edge_map, planar, (((1,), (1,)), ((), ())), precision=lax.Precision.HIGH)
        )
    keep_own = (1 - flags).astype(jnp.float32)
    keep = jnp.pad(keep_own, ((0, 1), (2, 2), (2, 2)))
    keep_layers = [
        lax.slice_in_dim(keep_own, nz - 2, nz, axis=2),
        jnp.zeros_like(lax.slice_in_dim(keep_own, 0, 1, axis=2)),
        lax.slice_in_dim(keep_own, 0, 2, axis=2),
    ]
    keep_layers = jnp.moveaxis(jnp.concatenate(keep_layers, axis=2), 2, 0)
    slabs.append(jnp.pad(keep_layers, ((0, 0), (0, 1), (2, 2))).reshape(5, -1))
    slabs = jnp.stack(slabs)
    up = slabs[:, :3].reshape(-1, slabs.shape[2])
    down = slabs[:, 3:].reshape(-1, slabs.shape[2])
    from_prev, from_next = both_ways(up, down, "gz")
    own_parts = lax.optimization_barrier(
        [
            jnp.dot(planar, jnp.asarray(depth.T, jnp.float32), precision=lax.Precision.HIGH)
            for planar, depth in zip(planars, depths)
        ]
    )
    arrived = jnp.concatenate(
        [from_prev.reshape(4, 3, -1), from_next.reshape(4, 2, -1)], axis=1
    )
    place = np.zeros((5, length))
    for row, col in enumerate([0, 1, 2, nz + 2, nz + 3]):
        place[row, col] = 1.0
    place = jnp.asarray(place, jnp.float32)
    nodal = []
    for comp in range(3):
        folded = lax.dot_general(arrived[comp], place, (((0,), (0,)), ((), ())), precision=lax.Precision.HIGH)
        nodal.append((own_parts[comp] + folded).reshape(nx + 1, ny + 4, length))
    keep_in = jnp.moveaxis(arrived[3].reshape(5, nx + 1, ny + 4), 0, 2)
    keep = keep + jnp.pad(keep_in[..., :3], ((0, 0), (0, 0), (0, length - 3))) + jnp.pad(
        keep_in[..., 3:], ((0, 0), (0, 0), (nz + 2, 0))
    )
    extended = jnp.stack(nodal + [keep])
    return plane_round_and_stencil(extended, nx, ny)


def solution(mesh):
    in_specs = (
        P("gx", None, "gy", None, "gz"),
        P("gx", None, "gy", None, "gz"),
        P("gx", None, "gy", None, "gz"),
        P(None, "gx", "gy", "gz"),
        P("gx", "gy", "gz"),
    )
    out_specs = P(None, "gx", "gy", "gz")
    return jax.shard_map(body, mesh=mesh, in_specs=in_specs, out_specs=out_specs, check_vma=False)
```

```python
import math

import jax
import jax.numpy as jnp
import numpy as np
from jax import lax
from jax.sharding import PartitionSpec as P


def lagrange_table(points, targets):
    table = np.ones((len(targets), len(points)))
    for row_pos in range(len(targets)):
        for col_pos in range(len(points)):
            for other in range(len(points)):
                if other != col_pos:
                    table[row_pos, col_pos] *= (targets[row_pos] - points[other]) / (
                        points[col_pos] - points[other]
                    )
    return table


def basis_tables():
    spread = math.sqrt(3.0 / 7.0)
    targets = [0.0, (1.0 - spread) / 2.0, 0.5, (1.0 + spread) / 2.0, 1.0]
    closed = [0.0, 0.25, 0.5, 0.75, 1.0]
    inner = math.sqrt(3.0 / 7.0 - 2.0 / 7.0 * math.sqrt(6.0 / 5.0))
    outer = math.sqrt(3.0 / 7.0 + 2.0 / 7.0 * math.sqrt(6.0 / 5.0))
    gauss = [(1.0 - outer) / 2.0, (1.0 - inner) / 2.0, (1.0 + inner) / 2.0, (1.0 + outer) / 2.0]
    closed_map = np.asarray(lagrange_table(closed, targets), dtype=np.float32).astype(np.float64)
    open_map = np.asarray(lagrange_table(gauss, targets), dtype=np.float32).astype(np.float64)
    return closed_map, open_map


def assembly_matrix(table, count):
    size = table.shape[1]
    matrix = np.zeros((4 * count + 1, count * size))
    for elem_pos in range(count):
        matrix[4 * elem_pos : 4 * elem_pos + 5, size * elem_pos : size * elem_pos + size] += table
    return matrix


def planar_part(coef, flip, table_x, table_y, size_z):
    ex_count, size_x, ey_count, size_y, merged = coef.shape
    orient = jnp.repeat((1 - 2 * flip).astype(jnp.float32), size_z, axis=2)
    signed = (coef * orient[:, None, :, None, :]).reshape(ex_count * size_x * ey_count * size_y, merged)
    rows_y = np.pad(assembly_matrix(table_y, ey_count), ((2, 1), (0, 0)))
    plane_map = np.kron(assembly_matrix(table_x, ex_count), rows_y)
    return jnp.dot(jnp.asarray(plane_map, jnp.float32), signed, precision=lax.Precision.HIGH)


def depth_map_of(table_z, merged):
    return np.pad(assembly_matrix(table_z, merged // table_z.shape[1]), ((2, 1), (0, 0)))


def shifted(block, axis, step=1):
    count = lax.axis_size(axis)
    if count == 1:
        return block
    return lax.ppermute(block, axis, [(i, (i + step) % count) for i in range(count)])


def both_ways(up, down, axis):
    if lax.axis_size(axis) <= 2:
        both = shifted(jnp.concatenate([up, down]), axis)
        return both[: up.shape[0]], both[up.shape[0] :]
    return shifted(up, axis), shifted(down, axis, -1)


def to_wire(slab, dim):
    layers = jnp.moveaxis(slab, dim, 0)
    return layers.reshape(layers.shape[0] * layers.shape[1], -1), layers.shape


def from_wire(rows, shape, dim):
    return jnp.moveaxis(rows.reshape(shape), 0, dim)


def fold_and_halo(extended, axis, dim):
    length = extended.shape[dim]
    n = length - 4
    up, up_shape = to_wire(lax.slice_in_dim(extended, n, n + 3, axis=dim), dim)
    down, down_shape = to_wire(lax.slice_in_dim(extended, 2, 4, axis=dim), dim)
    from_prev, from_next = both_ways(up, down, axis)
    widths_prev = [(0, 0)] * extended.ndim
    widths_prev[dim] = (0, length - 3)
    widths_next = [(0, 0)] * extended.ndim
    widths_next[dim] = (n + 2, 0)
    return (
        extended
        + jnp.pad(from_wire(from_prev, up_shape, dim), widths_prev)
        + jnp.pad(from_wire(from_next, down_shape, dim), widths_next)
    )


def cross_rows(plane, ny, nz):
    own = plane[:, 2 : ny + 2, 2 : nz + 2]
    strips_y = jnp.concatenate([plane[:, 0:2, 2 : nz + 2], plane[:, ny + 2 :, 2 : nz + 2]], axis=1)
    strips_z = jnp.concatenate([plane[:, 2 : ny + 2, 0:2], plane[:, 2 : ny + 2, nz + 2 :]], axis=2)
    strips_z = jnp.swapaxes(strips_z, 1, 2).reshape(-1)
    strips_z = jnp.pad(strips_z, (0, -strips_z.shape[0] % nz))
    return [own.reshape(-1, nz), strips_y.reshape(-1, nz), strips_z.reshape(-1, nz)]


def cross_plane(own, strips_y, strips_z):
    middle = jnp.concatenate([strips_z[..., 0:2], own, strips_z[..., 2:4]], axis=2)
    widths = ((0, 0), (0, 0), (2, 2))
    return jnp.concatenate(
        [jnp.pad(strips_y[:, 0:2], widths), middle, jnp.pad(strips_y[:, 2:4], widths)], axis=1
    )


def last_round_and_stencil(extended, axis, ny, nz):
    n = extended.shape[1] - 1
    comps = extended.shape[0] - 1
    data = extended[:comps]
    keep = extended[comps]

    def own(block):
        return block[..., 2 : ny + 2, 2 : nz + 2]

    halo_up = own(data[:, n - 2 : n] * keep[n - 2 : n])
    halo_down = own(data[:, 1] * keep[1])
    up_parts = [halo_up.reshape(-1, nz)] + cross_rows(data[:, n], ny, nz)
    down_parts = [own(data[:, 0]).reshape(-1, nz), own(keep[0]), halo_down.reshape(-1, nz)]
    up = jnp.concatenate(up_parts)
    down = jnp.concatenate(down_parts)
    from_prev, from_next = both_ways(up, down, axis)

    sizes = [part.shape[0] for part in up_parts]
    marks = np.cumsum([0] + sizes)
    prev_halo = from_prev[marks[0] : marks[1]].reshape(comps, 2, ny, nz)
    prev_own = from_prev[marks[1] : marks[2]].reshape(comps, ny, nz)
    prev_strips_y = from_prev[marks[2] : marks[3]].reshape(comps, 4, nz)
    prev_strips_z = from_prev[marks[3] : marks[4]].reshape(-1)[: comps * 4 * ny]
    prev_strips_z = jnp.swapaxes(prev_strips_z.reshape(comps, 4, ny), 1, 2)
    fold_in = cross_plane(prev_own, prev_strips_y, prev_strips_z)

    plane_rows = comps * ny
    next_fold = from_next[:plane_rows].reshape(comps, ny, nz)
    next_keep = from_next[plane_rows : plane_rows + ny]
    next_halo = from_next[plane_rows + ny :].reshape(comps, ny, nz)

    inner = data[:, 1:n] * keep[1:n]
    first = (data[:, 0] + fold_in) * keep[0]
    last = (own(data[:, n]) + next_fold) * next_keep
    across = jnp.concatenate([yz_terms(first[:, None], ny, nz), yz_terms(inner, ny, nz)], axis=1)
    column = jnp.concatenate(
        [prev_halo, own(first)[:, None], own(inner), last[:, None], next_halo[:, None]], axis=1
    )
    near = column[:, 1 : n + 1] + column[:, 3 : n + 3]
    far = column[:, 0:n] + column[:, 4 : n + 4]
    return 0.25 * (across - 4.0 / 3.0 * near + 1.0 / 12.0 * far)


def yz_terms(block, ny, nz):
    def part(dy, dz):
        return block[..., 2 + dy : ny + 2 + dy, 2 + dz : nz + 2 + dz]

    near = part(-1, 0) + part(1, 0) + part(0, -1) + part(0, 1)
    far = part(-2, 0) + part(2, 0) + part(0, -2) + part(0, 2)
    return 8.0 * part(0, 0) - 4.0 / 3.0 * near + 1.0 / 12.0 * far


def window(padded_array, axis_pos, offset):
    starts = [0, 2, 2, 2]
    limits = [
        padded_array.shape[0],
        padded_array.shape[1] - 2,
        padded_array.shape[2] - 2,
        padded_array.shape[3] - 2,
    ]
    starts[axis_pos] = offset
    limits[axis_pos] = offset + padded_array.shape[axis_pos] - 4
    return lax.slice(padded_array, tuple(starts), tuple(limits))


def stencil_apply(padded_array):
    total = 8.0 * window(padded_array, 1, 2)
    for axis_pos in (1, 2, 3):
        near = window(padded_array, axis_pos, 1) + window(padded_array, axis_pos, 3)
        far = window(padded_array, axis_pos, 0) + window(padded_array, axis_pos, 4)
        total = total - 4.0 / 3.0 * near + 1.0 / 12.0 * far
    return 0.25 * total


def exchange(payloads, axes):
    sizes = [lax.axis_size(axis) for axis in axes]
    groups = {}
    for offset in payloads:
        key = tuple(o % s for o, s in zip(offset, sizes))
        groups.setdefault(key, []).append(offset)
    arrived = {}
    previous = None
    for key, offsets in groups.items():
        parts = [part for offset in offsets for part in payloads[offset]]
        if previous is not None:
            previous, parts = lax.optimization_barrier((previous, parts))
        rows = jnp.concatenate([as_rows(part) for part in parts])
        previous = rows
        if any(key):
            pairs = []
            for source in np.ndindex(*sizes):
                target = tuple((c + k) % s for c, k, s in zip(source, key, sizes))
                pairs.append((int(np.ravel_multi_index(source, sizes)), int(np.ravel_multi_index(target, sizes))))
            rows = lax.ppermute(rows, tuple(axes), pairs)
        start = 0
        for offset in offsets:
            parts = []
            for part in payloads[offset]:
                count = -(-part.size // 128)
                parts.append(rows[start : start + count].reshape(-1)[: part.size].reshape(part.shape))
                start += count
            arrived[offset] = parts
    return arrived


def as_rows(part):
    if part.shape[-1] == 128:
        return part.reshape(-1, 128)
    flat = part.reshape(-1)
    return jnp.pad(flat, (0, -flat.shape[0] % 128)).reshape(-1, 128)


def placed(block, starts, shape):
    return jnp.pad(block, [(b, s - b - d) for b, d, s in zip(starts, block.shape, shape)])


def plane_round_and_stencil(extended, nx, ny):
    e = extended
    payloads = {
        (1, 0): (e[:, nx - 2 : nx, 2 : ny + 2, 2:-2], e[:-1, nx : nx + 1, 2 : ny + 3]),
        (-1, 0): (e[:, 0:2, 2 : ny + 2, 2:-2],),
        (1, 1): (e[:, nx - 2 : nx + 1, ny + 2], e[:, nx, ny : ny + 2]),
        (-1, 1): (e[:, 0:2, ny + 2],),
        (1, -1): (e[:, nx, 2:4],),
        (0, 1): (e[:, :, ny : ny + 3],),
        (0, -1): (e[:, 0:nx, 2:4],),
    }
    got = exchange(payloads, ("gx", "gy"))
    channels, _, _, depth = e.shape
    shape = (channels, nx + 4, ny + 4, depth)

    def at(block, layer, row, col=0):
        return placed(block, (0, layer, row, col), shape)

    halo_x, fold_x = got[(1, 0)]
    corner_x, corner_y = got[(1, 1)]
    total = (
        at(e, 2, 0)
        + at(halo_x, 0, 2, 2)
        + at(fold_x, 2, 2)
        + at(got[(-1, 0)][0], nx + 2, 2, 2)
        + at(got[(0, 1)][0], 2, 0)
        + at(got[(0, -1)][0], 2, ny + 2)
        + at(corner_x[:, :, None], 0, 2)
        + at(corner_y[:, None], 2, 0)
        + at(got[(-1, 1)][0][:, :, None], nx + 2, 2)
        + at(got[(1, -1)][0][:, None], 2, ny + 2)
    )
    masked = total[:-1] * total[-1]
    inner = z_terms(e[:-1, 1:nx, 3 : ny + 2] * e[-1, 1:nx, 3 : ny + 2])
    rows = jnp.concatenate([z_terms(masked[:, 3 : nx + 2, 2:3]), inner], axis=2)
    result = jnp.concatenate([z_terms(masked[:, 2:3, 2 : ny + 2]), rows], axis=1)
    for axis_pos in (1, 2):
        near = window(masked, axis_pos, 1) + window(masked, axis_pos, 3)
        far = window(masked, axis_pos, 0) + window(masked, axis_pos, 4)
        result = result - 4.0 / 3.0 * near + 1.0 / 12.0 * far
    return 0.25 * result


def z_terms(block):
    nz = block.shape[-1] - 4

    def part(dz):
        return block[..., 2 + dz : nz + 2 + dz]

    return 8.0 * part(0) - 4.0 / 3.0 * (part(-1) + part(1)) + 1.0 / 12.0 * (part(-2) + part(2))


def body(edge_coeffs_x, edge_coeffs_y, edge_coeffs_z, flips, flags):
    closed_map, open_map = basis_tables()
    nx, ny, nz = flags.shape
    precise = lax.Precision.HIGHEST
    inputs = [
        (edge_coeffs_x, flips[0], open_map, closed_map, closed_map),
        (edge_coeffs_y, flips[1], closed_map, open_map, closed_map),
        (edge_coeffs_z, flips[2], closed_map, closed_map, open_map),
    ]
    length = nz + 4
    up_places = [nz, nz + 1, nz + 2]
    down_places = [2, 3]
    planars = []
    depths = []
    slabs = []
    for coef, flip, table_x, table_y, table_z in inputs:
        planar = planar_part(coef, flip, table_x, table_y, table_z.shape[1])
        depth_map = depth_map_of(table_z, coef.shape[4])
        edge_map = jnp.asarray(depth_map[up_places + down_places], jnp.float32)
        planars.append(planar)
        depths.append(depth_map)
        slabs.append(
            lax.dot_general(edge_map, planar, (((1,), (1,)), ((), ())), precision=lax.Precision.HIGH)
        )
    keep_own = (1 - flags).astype(jnp.float32)
    keep = jnp.pad(keep_own, ((0, 1), (2, 2), (2, 2)))
    keep_layers = [
        lax.slice_in_dim(keep_own, nz - 2, nz, axis=2),
        jnp.zeros_like(lax.slice_in_dim(keep_own, 0, 1, axis=2)),
        lax.slice_in_dim(keep_own, 0, 2, axis=2),
    ]
    keep_layers = jnp.moveaxis(jnp.concatenate(keep_layers, axis=2), 2, 0)
    slabs.append(jnp.pad(keep_layers, ((0, 0), (0, 1), (2, 2))).reshape(5, -1))
    slabs = jnp.stack(slabs)
    up = slabs[:, :3].reshape(-1, slabs.shape[2])
    down = slabs[:, 3:].reshape(-1, slabs.shape[2])
    from_prev, from_next = both_ways(up, down, "gz")
    own_parts = lax.optimization_barrier(
        [
            jnp.dot(planar, jnp.asarray(depth.T, jnp.float32), precision=lax.Precision.HIGH)
            for planar, depth in zip(planars, depths)
        ]
    )
    arrived = jnp.concatenate(
        [from_prev.reshape(4, 3, -1), from_next.reshape(4, 2, -1)], axis=1
    )
    place = np.zeros((5, length))
    for row, col in enumerate([0, 1, 2, nz + 2, nz + 3]):
        place[row, col] = 1.0
    place = jnp.asarray(place, jnp.float32)
    nodal = []
    for comp in range(3):
        folded = lax.dot_general(arrived[comp], place, (((0,), (0,)), ((), ())), precision=lax.Precision.HIGH)
        nodal.append((own_parts[comp] + folded).reshape(nx + 1, ny + 4, length))
    keep_in = jnp.moveaxis(arrived[3].reshape(5, nx + 1, ny + 4), 0, 2)
    keep = keep + jnp.pad(keep_in[..., :3], ((0, 0), (0, 0), (0, length - 3))) + jnp.pad(
        keep_in[..., 3:], ((0, 0), (0, 0), (nz + 2, 0))
    )
    extended = jnp.stack(nodal + [keep])
    return plane_round_and_stencil(extended, nx, ny)


def solution(mesh):
    in_specs = (
        P("gx", None, "gy", None, "gz"),
        P("gx", None, "gy", None, "gz"),
        P("gx", None, "gy", None, "gz"),
        P(None, "gx", "gy", "gz"),
        P("gx", "gy", "gz"),
    )
    out_specs = P(None, "gx", "gy", "gz")
    return jax.shard_map(body, mesh=mesh, in_specs=in_specs, out_specs=out_specs, check_vma=False)
```

```python
import math

import jax
import jax.numpy as jnp
import numpy as np
from jax import lax
from jax.sharding import PartitionSpec as P


def lagrange_table(points, targets):
    table = np.ones((len(targets), len(points)))
    for row_pos in range(len(targets)):
        for col_pos in range(len(points)):
            for other in range(len(points)):
                if other != col_pos:
                    table[row_pos, col_pos] *= (targets[row_pos] - points[other]) / (
                        points[col_pos] - points[other]
                    )
    return table


def basis_tables():
    spread = math.sqrt(3.0 / 7.0)
    targets = [0.0, (1.0 - spread) / 2.0, 0.5, (1.0 + spread) / 2.0, 1.0]
    closed = [0.0, 0.25, 0.5, 0.75, 1.0]
    inner = math.sqrt(3.0 / 7.0 - 2.0 / 7.0 * math.sqrt(6.0 / 5.0))
    outer = math.sqrt(3.0 / 7.0 + 2.0 / 7.0 * math.sqrt(6.0 / 5.0))
    gauss = [(1.0 - outer) / 2.0, (1.0 - inner) / 2.0, (1.0 + inner) / 2.0, (1.0 + outer) / 2.0]
    closed_map = np.asarray(lagrange_table(closed, targets), dtype=np.float32).astype(np.float64)
    open_map = np.asarray(lagrange_table(gauss, targets), dtype=np.float32).astype(np.float64)
    return closed_map, open_map


def assembly_matrix(table, count):
    size = table.shape[1]
    matrix = np.zeros((4 * count + 1, count * size))
    for elem_pos in range(count):
        matrix[4 * elem_pos : 4 * elem_pos + 5, size * elem_pos : size * elem_pos + size] += table
    return matrix


def planar_part(coef, flip, table_x, table_y, size_z):
    ex_count, size_x, ey_count, size_y, merged = coef.shape
    orient = jnp.repeat((1 - 2 * flip).astype(jnp.float32), size_z, axis=2)
    signed = (coef * orient[:, None, :, None, :]).reshape(ex_count * size_x * ey_count * size_y, merged)
    rows_y = np.pad(assembly_matrix(table_y, ey_count), ((2, 1), (0, 0)))
    plane_map = np.kron(assembly_matrix(table_x, ex_count), rows_y)
    return jnp.dot(jnp.asarray(plane_map, jnp.float32), signed, precision=lax.Precision.HIGH)


def depth_map_of(table_z, merged):
    return np.pad(assembly_matrix(table_z, merged // table_z.shape[1]), ((2, 1), (0, 0)))


def shifted(block, axis, step=1):
    count = lax.axis_size(axis)
    if count == 1:
        return block
    return lax.ppermute(block, axis, [(i, (i + step) % count) for i in range(count)])


def both_ways(up, down, axis):
    if lax.axis_size(axis) <= 2:
        both = shifted(jnp.concatenate([up, down]), axis)
        return both[: up.shape[0]], both[up.shape[0] :]
    return shifted(up, axis), shifted(down, axis, -1)


def to_wire(slab, dim):
    layers = jnp.moveaxis(slab, dim, 0)
    return layers.reshape(layers.shape[0] * layers.shape[1], -1), layers.shape


def from_wire(rows, shape, dim):
    return jnp.moveaxis(rows.reshape(shape), 0, dim)


def fold_and_halo(extended, axis, dim):
    length = extended.shape[dim]
    n = length - 4
    up, up_shape = to_wire(lax.slice_in_dim(extended, n, n + 3, axis=dim), dim)
    down, down_shape = to_wire(lax.slice_in_dim(extended, 2, 4, axis=dim), dim)
    from_prev, from_next = both_ways(up, down, axis)
    widths_prev = [(0, 0)] * extended.ndim
    widths_prev[dim] = (0, length - 3)
    widths_next = [(0, 0)] * extended.ndim
    widths_next[dim] = (n + 2, 0)
    return (
        extended
        + jnp.pad(from_wire(from_prev, up_shape, dim), widths_prev)
        + jnp.pad(from_wire(from_next, down_shape, dim), widths_next)
    )


def cross_rows(plane, ny, nz):
    own = plane[:, 2 : ny + 2, 2 : nz + 2]
    strips_y = jnp.concatenate([plane[:, 0:2, 2 : nz + 2], plane[:, ny + 2 :, 2 : nz + 2]], axis=1)
    strips_z = jnp.concatenate([plane[:, 2 : ny + 2, 0:2], plane[:, 2 : ny + 2, nz + 2 :]], axis=2)
    strips_z = jnp.swapaxes(strips_z, 1, 2).reshape(-1)
    strips_z = jnp.pad(strips_z, (0, -strips_z.shape[0] % nz))
    return [own.reshape(-1, nz), strips_y.reshape(-1, nz), strips_z.reshape(-1, nz)]


def cross_plane(own, strips_y, strips_z):
    middle = jnp.concatenate([strips_z[..., 0:2], own, strips_z[..., 2:4]], axis=2)
    widths = ((0, 0), (0, 0), (2, 2))
    return jnp.concatenate(
        [jnp.pad(strips_y[:, 0:2], widths), middle, jnp.pad(strips_y[:, 2:4], widths)], axis=1
    )


def last_round_and_stencil(extended, axis, ny, nz):
    n = extended.shape[1] - 1
    comps = extended.shape[0] - 1
    data = extended[:comps]
    keep = extended[comps]

    def own(block):
        return block[..., 2 : ny + 2, 2 : nz + 2]

    halo_up = own(data[:, n - 2 : n] * keep[n - 2 : n])
    halo_down = own(data[:, 1] * keep[1])
    up_parts = [halo_up.reshape(-1, nz)] + cross_rows(data[:, n], ny, nz)
    down_parts = [own(data[:, 0]).reshape(-1, nz), own(keep[0]), halo_down.reshape(-1, nz)]
    up = jnp.concatenate(up_parts)
    down = jnp.concatenate(down_parts)
    from_prev, from_next = both_ways(up, down, axis)

    sizes = [part.shape[0] for part in up_parts]
    marks = np.cumsum([0] + sizes)
    prev_halo = from_prev[marks[0] : marks[1]].reshape(comps, 2, ny, nz)
    prev_own = from_prev[marks[1] : marks[2]].reshape(comps, ny, nz)
    prev_strips_y = from_prev[marks[2] : marks[3]].reshape(comps, 4, nz)
    prev_strips_z = from_prev[marks[3] : marks[4]].reshape(-1)[: comps * 4 * ny]
    prev_strips_z = jnp.swapaxes(prev_strips_z.reshape(comps, 4, ny), 1, 2)
    fold_in = cross_plane(prev_own, prev_strips_y, prev_strips_z)

    plane_rows = comps * ny
    next_fold = from_next[:plane_rows].reshape(comps, ny, nz)
    next_keep = from_next[plane_rows : plane_rows + ny]
    next_halo = from_next[plane_rows + ny :].reshape(comps, ny, nz)

    inner = data[:, 1:n] * keep[1:n]
    first = (data[:, 0] + fold_in) * keep[0]
    last = (own(data[:, n]) + next_fold) * next_keep
    across = jnp.concatenate([yz_terms(first[:, None], ny, nz), yz_terms(inner, ny, nz)], axis=1)
    column = jnp.concatenate(
        [prev_halo, own(first)[:, None], own(inner), last[:, None], next_halo[:, None]], axis=1
    )
    near = column[:, 1 : n + 1] + column[:, 3 : n + 3]
    far = column[:, 0:n] + column[:, 4 : n + 4]
    return 0.25 * (across - 4.0 / 3.0 * near + 1.0 / 12.0 * far)


def yz_terms(block, ny, nz):
    def part(dy, dz):
        return block[..., 2 + dy : ny + 2 + dy, 2 + dz : nz + 2 + dz]

    near = part(-1, 0) + part(1, 0) + part(0, -1) + part(0, 1)
    far = part(-2, 0) + part(2, 0) + part(0, -2) + part(0, 2)
    return 8.0 * part(0, 0) - 4.0 / 3.0 * near + 1.0 / 12.0 * far


def window(padded_array, axis_pos, offset):
    starts = [0, 2, 2, 2]
    limits = [
        padded_array.shape[0],
        padded_array.shape[1] - 2,
        padded_array.shape[2] - 2,
        padded_array.shape[3] - 2,
    ]
    starts[axis_pos] = offset
    limits[axis_pos] = offset + padded_array.shape[axis_pos] - 4
    return lax.slice(padded_array, tuple(starts), tuple(limits))


def stencil_apply(padded_array):
    total = 8.0 * window(padded_array, 1, 2)
    for axis_pos in (1, 2, 3):
        near = window(padded_array, axis_pos, 1) + window(padded_array, axis_pos, 3)
        far = window(padded_array, axis_pos, 0) + window(padded_array, axis_pos, 4)
        total = total - 4.0 / 3.0 * near + 1.0 / 12.0 * far
    return 0.25 * total


def exchange(payloads, axes):
    sizes = [lax.axis_size(axis) for axis in axes]
    groups = {}
    for offset in payloads:
        key = tuple(o % s for o, s in zip(offset, sizes))
        groups.setdefault(key, []).append(offset)
    arrived = {}
    previous = None
    for key, offsets in groups.items():
        parts = [part for offset in offsets for part in payloads[offset]]
        if previous is not None:
            previous, parts = lax.optimization_barrier((previous, parts))
        rows = jnp.concatenate([as_rows(part) for part in parts])
        previous = rows
        if any(key):
            pairs = []
            for source in np.ndindex(*sizes):
                target = tuple((c + k) % s for c, k, s in zip(source, key, sizes))
                pairs.append((int(np.ravel_multi_index(source, sizes)), int(np.ravel_multi_index(target, sizes))))
            rows = lax.ppermute(rows, tuple(axes), pairs)
        start = 0
        for offset in offsets:
            parts = []
            for part in payloads[offset]:
                count = -(-part.size // 128)
                parts.append(rows[start : start + count].reshape(-1)[: part.size].reshape(part.shape))
                start += count
            arrived[offset] = parts
    return arrived


def as_rows(part):
    if part.shape[-1] == 128:
        return part.reshape(-1, 128)
    flat = part.reshape(-1)
    return jnp.pad(flat, (0, -flat.shape[0] % 128)).reshape(-1, 128)


def placed(block, starts, shape):
    return jnp.pad(block, [(b, s - b - d) for b, d, s in zip(starts, block.shape, shape)])


def plane_round_and_stencil(extended, nx, ny):
    e = extended
    payloads = {
        (1, 0): (e[:, nx - 2 : nx, 2 : ny + 2, 2:-2], e[:-1, nx : nx + 1, 2 : ny + 3]),
        (-1, 0): (e[:, 0:2, 2 : ny + 2, 2:-2],),
        (0, 1): (e[:, :, ny : ny + 3],),
        (0, -1): (e[:, 0:nx, 2:4],),
        (1, 1): (e[:, nx - 2 : nx + 1, ny + 2], e[:, nx, ny : ny + 2]),
        (-1, 1): (e[:, 0:2, ny + 2],),
        (1, -1): (e[:, nx, 2:4],),
    }
    got = exchange(payloads, ("gx", "gy"))
    channels, _, _, depth = e.shape
    shape = (channels, nx + 4, ny + 4, depth)

    def at(block, layer, row, col=0):
        return placed(block, (0, layer, row, col), shape)

    halo_x, fold_x = got[(1, 0)]
    corner_x, corner_y = got[(1, 1)]
    total = (
        at(e, 2, 0)
        + at(halo_x, 0, 2, 2)
        + at(fold_x, 2, 2)
        + at(got[(-1, 0)][0], nx + 2, 2, 2)
        + at(got[(0, 1)][0], 2, 0)
        + at(got[(0, -1)][0], 2, ny + 2)
        + at(corner_x[:, :, None], 0, 2)
        + at(corner_y[:, None], 2, 0)
        + at(got[(-1, 1)][0][:, :, None], nx + 2, 2)
        + at(got[(1, -1)][0][:, None], 2, ny + 2)
    )
    masked = total[:-1] * total[-1]
    inner = z_terms(e[:-1, 1:nx, 3 : ny + 2] * e[-1, 1:nx, 3 : ny + 2])
    rows = jnp.concatenate([z_terms(masked[:, 3 : nx + 2, 2:3]), inner], axis=2)
    result = jnp.concatenate([z_terms(masked[:, 2:3, 2 : ny + 2]), rows], axis=1)
    for axis_pos in (1, 2):
        near = window(masked, axis_pos, 1) + window(masked, axis_pos, 3)
        far = window(masked, axis_pos, 0) + window(masked, axis_pos, 4)
        result = result - 4.0 / 3.0 * near + 1.0 / 12.0 * far
    return 0.25 * result


def z_terms(block):
    nz = block.shape[-1] - 4

    def part(dz):
        return block[..., 2 + dz : nz + 2 + dz]

    return 8.0 * part(0) - 4.0 / 3.0 * (part(-1) + part(1)) + 1.0 / 12.0 * (part(-2) + part(2))


def body(edge_coeffs_x, edge_coeffs_y, edge_coeffs_z, flips, flags):
    closed_map, open_map = basis_tables()
    nx, ny, nz = flags.shape
    precise = lax.Precision.HIGHEST
    inputs = [
        (edge_coeffs_x, flips[0], open_map, closed_map, closed_map),
        (edge_coeffs_y, flips[1], closed_map, open_map, closed_map),
        (edge_coeffs_z, flips[2], closed_map, closed_map, open_map),
    ]
    length = nz + 4
    up_places = [nz, nz + 1, nz + 2]
    down_places = [2, 3]
    planars = []
    depths = []
    slabs = []
    for coef, flip, table_x, table_y, table_z in inputs:
        planar = planar_part(coef, flip, table_x, table_y, table_z.shape[1])
        depth_map = depth_map_of(table_z, coef.shape[4])
        edge_map = jnp.asarray(depth_map[up_places + down_places], jnp.float32)
        planars.append(planar)
        depths.append(depth_map)
        slabs.append(
            lax.dot_general(edge_map, planar, (((1,), (1,)), ((), ())), precision=lax.Precision.HIGH)
        )
    keep_own = (1 - flags).astype(jnp.float32)
    keep = jnp.pad(keep_own, ((0, 1), (2, 2), (2, 2)))
    keep_layers = [
        lax.slice_in_dim(keep_own, nz - 2, nz, axis=2),
        jnp.zeros_like(lax.slice_in_dim(keep_own, 0, 1, axis=2)),
        lax.slice_in_dim(keep_own, 0, 2, axis=2),
    ]
    keep_layers = jnp.moveaxis(jnp.concatenate(keep_layers, axis=2), 2, 0)
    slabs.append(jnp.pad(keep_layers, ((0, 0), (0, 1), (2, 2))).reshape(5, -1))
    slabs = jnp.stack(slabs)
    up = slabs[:, :3].reshape(-1, slabs.shape[2])
    down = slabs[:, 3:].reshape(-1, slabs.shape[2])
    from_prev, from_next = both_ways(up, down, "gz")
    own_parts = [
        jnp.dot(planar, jnp.asarray(depth.T, jnp.float32), precision=lax.Precision.HIGH)
        for planar, depth in zip(planars, depths)
    ]
    arrived = jnp.concatenate(
        [from_prev.reshape(4, 3, -1), from_next.reshape(4, 2, -1)], axis=1
    )
    place = np.zeros((5, length))
    for row, col in enumerate([0, 1, 2, nz + 2, nz + 3]):
        place[row, col] = 1.0
    place = jnp.asarray(place, jnp.float32)
    nodal = []
    for comp in range(3):
        folded = lax.dot_general(arrived[comp], place, (((0,), (0,)), ((), ())), precision=lax.Precision.HIGH)
        nodal.append((own_parts[comp] + folded).reshape(nx + 1, ny + 4, length))
    keep_in = jnp.moveaxis(arrived[3].reshape(5, nx + 1, ny + 4), 0, 2)
    keep = keep + jnp.pad(keep_in[..., :3], ((0, 0), (0, 0), (0, length - 3))) + jnp.pad(
        keep_in[..., 3:], ((0, 0), (0, 0), (nz + 2, 0))
    )
    extended = jnp.stack(nodal + [keep])
    return plane_round_and_stencil(extended, nx, ny)


def solution(mesh):
    in_specs = (
        P("gx", None, "gy", None, "gz"),
        P("gx", None, "gy", None, "gz"),
        P("gx", None, "gy", None, "gz"),
        P(None, "gx", "gy", "gz"),
        P("gx", "gy", "gz"),
    )
    out_specs = P(None, "gx", "gy", "gz")
    return jax.shard_map(body, mesh=mesh, in_specs=in_specs, out_specs=out_specs, check_vma=False)
```

```python
import math

import jax
import jax.numpy as jnp
import numpy as np
from jax import lax
from jax.sharding import PartitionSpec as P


def lagrange_table(points, targets):
    table = np.ones((len(targets), len(points)))
    for row_pos in range(len(targets)):
        for col_pos in range(len(points)):
            for other in range(len(points)):
                if other != col_pos:
                    table[row_pos, col_pos] *= (targets[row_pos] - points[other]) / (
                        points[col_pos] - points[other]
                    )
    return table


def basis_tables():
    spread = math.sqrt(3.0 / 7.0)
    targets = [0.0, (1.0 - spread) / 2.0, 0.5, (1.0 + spread) / 2.0, 1.0]
    closed = [0.0, 0.25, 0.5, 0.75, 1.0]
    inner = math.sqrt(3.0 / 7.0 - 2.0 / 7.0 * math.sqrt(6.0 / 5.0))
    outer = math.sqrt(3.0 / 7.0 + 2.0 / 7.0 * math.sqrt(6.0 / 5.0))
    gauss = [(1.0 - outer) / 2.0, (1.0 - inner) / 2.0, (1.0 + inner) / 2.0, (1.0 + outer) / 2.0]
    closed_map = np.asarray(lagrange_table(closed, targets), dtype=np.float32).astype(np.float64)
    open_map = np.asarray(lagrange_table(gauss, targets), dtype=np.float32).astype(np.float64)
    return closed_map, open_map


def assembly_matrix(table, count):
    size = table.shape[1]
    matrix = np.zeros((4 * count + 1, count * size))
    for elem_pos in range(count):
        matrix[4 * elem_pos : 4 * elem_pos + 5, size * elem_pos : size * elem_pos + size] += table
    return matrix


def planar_part(coef, flip, table_x, table_y, size_z):
    ex_count, size_x, ey_count, size_y, merged = coef.shape
    orient = jnp.repeat((1 - 2 * flip).astype(jnp.float32), size_z, axis=2)
    signed = (coef * orient[:, None, :, None, :]).reshape(ex_count * size_x * ey_count * size_y, merged)
    rows_y = np.pad(assembly_matrix(table_y, ey_count), ((2, 1), (0, 0)))
    plane_map = np.kron(assembly_matrix(table_x, ex_count), rows_y)
    return jnp.dot(jnp.asarray(plane_map, jnp.float32), signed, precision=lax.Precision.HIGH)


def depth_map_of(table_z, merged):
    return np.pad(assembly_matrix(table_z, merged // table_z.shape[1]), ((2, 1), (0, 0)))


def shifted(block, axis, step=1):
    count = lax.axis_size(axis)
    if count == 1:
        return block
    return lax.ppermute(block, axis, [(i, (i + step) % count) for i in range(count)])


def both_ways(up, down, axis):
    if lax.axis_size(axis) <= 2:
        both = shifted(jnp.concatenate([up, down]), axis)
        return both[: up.shape[0]], both[up.shape[0] :]
    return shifted(up, axis), shifted(down, axis, -1)


def to_wire(slab, dim):
    layers = jnp.moveaxis(slab, dim, 0)
    return layers.reshape(layers.shape[0] * layers.shape[1], -1), layers.shape


def from_wire(rows, shape, dim):
    return jnp.moveaxis(rows.reshape(shape), 0, dim)


def fold_and_halo(extended, axis, dim):
    length = extended.shape[dim]
    n = length - 4
    up, up_shape = to_wire(lax.slice_in_dim(extended, n, n + 3, axis=dim), dim)
    down, down_shape = to_wire(lax.slice_in_dim(extended, 2, 4, axis=dim), dim)
    from_prev, from_next = both_ways(up, down, axis)
    widths_prev = [(0, 0)] * extended.ndim
    widths_prev[dim] = (0, length - 3)
    widths_next = [(0, 0)] * extended.ndim
    widths_next[dim] = (n + 2, 0)
    return (
        extended
        + jnp.pad(from_wire(from_prev, up_shape, dim), widths_prev)
        + jnp.pad(from_wire(from_next, down_shape, dim), widths_next)
    )


def cross_rows(plane, ny, nz):
    own = plane[:, 2 : ny + 2, 2 : nz + 2]
    strips_y = jnp.concatenate([plane[:, 0:2, 2 : nz + 2], plane[:, ny + 2 :, 2 : nz + 2]], axis=1)
    strips_z = jnp.concatenate([plane[:, 2 : ny + 2, 0:2], plane[:, 2 : ny + 2, nz + 2 :]], axis=2)
    strips_z = jnp.swapaxes(strips_z, 1, 2).reshape(-1)
    strips_z = jnp.pad(strips_z, (0, -strips_z.shape[0] % nz))
    return [own.reshape(-1, nz), strips_y.reshape(-1, nz), strips_z.reshape(-1, nz)]


def cross_plane(own, strips_y, strips_z):
    middle = jnp.concatenate([strips_z[..., 0:2], own, strips_z[..., 2:4]], axis=2)
    widths = ((0, 0), (0, 0), (2, 2))
    return jnp.concatenate(
        [jnp.pad(strips_y[:, 0:2], widths), middle, jnp.pad(strips_y[:, 2:4], widths)], axis=1
    )


def last_round_and_stencil(extended, axis, ny, nz):
    n = extended.shape[1] - 1
    comps = extended.shape[0] - 1
    data = extended[:comps]
    keep = extended[comps]

    def own(block):
        return block[..., 2 : ny + 2, 2 : nz + 2]

    halo_up = own(data[:, n - 2 : n] * keep[n - 2 : n])
    halo_down = own(data[:, 1] * keep[1])
    up_parts = [halo_up.reshape(-1, nz)] + cross_rows(data[:, n], ny, nz)
    down_parts = [own(data[:, 0]).reshape(-1, nz), own(keep[0]), halo_down.reshape(-1, nz)]
    up = jnp.concatenate(up_parts)
    down = jnp.concatenate(down_parts)
    from_prev, from_next = both_ways(up, down, axis)

    sizes = [part.shape[0] for part in up_parts]
    marks = np.cumsum([0] + sizes)
    prev_halo = from_prev[marks[0] : marks[1]].reshape(comps, 2, ny, nz)
    prev_own = from_prev[marks[1] : marks[2]].reshape(comps, ny, nz)
    prev_strips_y = from_prev[marks[2] : marks[3]].reshape(comps, 4, nz)
    prev_strips_z = from_prev[marks[3] : marks[4]].reshape(-1)[: comps * 4 * ny]
    prev_strips_z = jnp.swapaxes(prev_strips_z.reshape(comps, 4, ny), 1, 2)
    fold_in = cross_plane(prev_own, prev_strips_y, prev_strips_z)

    plane_rows = comps * ny
    next_fold = from_next[:plane_rows].reshape(comps, ny, nz)
    next_keep = from_next[plane_rows : plane_rows + ny]
    next_halo = from_next[plane_rows + ny :].reshape(comps, ny, nz)

    inner = data[:, 1:n] * keep[1:n]
    first = (data[:, 0] + fold_in) * keep[0]
    last = (own(data[:, n]) + next_fold) * next_keep
    across = jnp.concatenate([yz_terms(first[:, None], ny, nz), yz_terms(inner, ny, nz)], axis=1)
    column = jnp.concatenate(
        [prev_halo, own(first)[:, None], own(inner), last[:, None], next_halo[:, None]], axis=1
    )
    near = column[:, 1 : n + 1] + column[:, 3 : n + 3]
    far = column[:, 0:n] + column[:, 4 : n + 4]
    return 0.25 * (across - 4.0 / 3.0 * near + 1.0 / 12.0 * far)


def yz_terms(block, ny, nz):
    def part(dy, dz):
        return block[..., 2 + dy : ny + 2 + dy, 2 + dz : nz + 2 + dz]

    near = part(-1, 0) + part(1, 0) + part(0, -1) + part(0, 1)
    far = part(-2, 0) + part(2, 0) + part(0, -2) + part(0, 2)
    return 8.0 * part(0, 0) - 4.0 / 3.0 * near + 1.0 / 12.0 * far


def window(padded_array, axis_pos, offset):
    starts = [0, 2, 2, 2]
    limits = [
        padded_array.shape[0],
        padded_array.shape[1] - 2,
        padded_array.shape[2] - 2,
        padded_array.shape[3] - 2,
    ]
    starts[axis_pos] = offset
    limits[axis_pos] = offset + padded_array.shape[axis_pos] - 4
    return lax.slice(padded_array, tuple(starts), tuple(limits))


def stencil_apply(padded_array):
    total = 8.0 * window(padded_array, 1, 2)
    for axis_pos in (1, 2, 3):
        near = window(padded_array, axis_pos, 1) + window(padded_array, axis_pos, 3)
        far = window(padded_array, axis_pos, 0) + window(padded_array, axis_pos, 4)
        total = total - 4.0 / 3.0 * near + 1.0 / 12.0 * far
    return 0.25 * total


def exchange(payloads, axes):
    sizes = [lax.axis_size(axis) for axis in axes]
    groups = {}
    for offset in payloads:
        key = tuple(o % s for o, s in zip(offset, sizes))
        groups.setdefault(key, []).append(offset)
    arrived = {}
    previous = None
    for key, offsets in groups.items():
        parts = [part for offset in offsets for part in payloads[offset]]
        if previous is not None:
            previous, parts = lax.optimization_barrier((previous, parts))
        rows = jnp.concatenate([as_rows(part) for part in parts])
        previous = rows
        if any(key):
            pairs = []
            for source in np.ndindex(*sizes):
                target = tuple((c + k) % s for c, k, s in zip(source, key, sizes))
                pairs.append((int(np.ravel_multi_index(source, sizes)), int(np.ravel_multi_index(target, sizes))))
            rows = lax.ppermute(rows, tuple(axes), pairs)
        start = 0
        for offset in offsets:
            parts = []
            for part in payloads[offset]:
                count = -(-part.size // 128)
                parts.append(rows[start : start + count].reshape(-1)[: part.size].reshape(part.shape))
                start += count
            arrived[offset] = parts
    return arrived


def as_rows(part):
    if part.shape[-1] == 128:
        return part.reshape(-1, 128)
    flat = part.reshape(-1)
    return jnp.pad(flat, (0, -flat.shape[0] % 128)).reshape(-1, 128)


def placed(block, starts, shape):
    return jnp.pad(block, [(b, s - b - d) for b, d, s in zip(starts, block.shape, shape)])


def plane_round_and_stencil(extended, nx, ny):
    e = extended
    payloads = {
        (1, 0): (e[:, nx - 2 : nx, 2 : ny + 2, 2:-2], e[:-1, nx : nx + 1, 2 : ny + 3]),
        (-1, 0): (e[:, 0:2, 2 : ny + 2, 2:-2],),
        (0, 1): (e[:, :, ny : ny + 3],),
        (0, -1): (e[:, 0:nx, 2:4],),
        (1, 1): (e[:, nx - 2 : nx + 1, ny + 2], e[:, nx, ny : ny + 2]),
        (-1, 1): (e[:, 0:2, ny + 2],),
        (1, -1): (e[:, nx, 2:4],),
    }
    got = exchange(payloads, ("gx", "gy"))
    channels, _, _, depth = e.shape
    shape = (channels, nx + 4, ny + 4, depth)

    def at(block, layer, row, col=0):
        return placed(block, (0, layer, row, col), shape)

    halo_x, fold_x = got[(1, 0)]
    corner_x, corner_y = got[(1, 1)]
    total = (
        at(e, 2, 0)
        + at(halo_x, 0, 2, 2)
        + at(fold_x, 2, 2)
        + at(got[(-1, 0)][0], nx + 2, 2, 2)
        + at(got[(0, 1)][0], 2, 0)
        + at(got[(0, -1)][0], 2, ny + 2)
        + at(corner_x[:, :, None], 0, 2)
        + at(corner_y[:, None], 2, 0)
        + at(got[(-1, 1)][0][:, :, None], nx + 2, 2)
        + at(got[(1, -1)][0][:, None], 2, ny + 2)
    )
    masked = total[:-1] * total[-1]
    inner = z_terms(e[:-1, 1:nx, 3 : ny + 2] * e[-1, 1:nx, 3 : ny + 2])
    rows = jnp.concatenate([z_terms(masked[:, 3 : nx + 2, 2:3]), inner], axis=2)
    result = jnp.concatenate([z_terms(masked[:, 2:3, 2 : ny + 2]), rows], axis=1)
    for axis_pos in (1, 2):
        near = window(masked, axis_pos, 1) + window(masked, axis_pos, 3)
        far = window(masked, axis_pos, 0) + window(masked, axis_pos, 4)
        result = result - 4.0 / 3.0 * near + 1.0 / 12.0 * far
    return 0.25 * result


def z_terms(block):
    nz = block.shape[-1] - 4

    def part(dz):
        return block[..., 2 + dz : nz + 2 + dz]

    return 8.0 * part(0) - 4.0 / 3.0 * (part(-1) + part(1)) + 1.0 / 12.0 * (part(-2) + part(2))


def body(edge_coeffs_x, edge_coeffs_y, edge_coeffs_z, flips, flags):
    closed_map, open_map = basis_tables()
    nx, ny, nz = flags.shape
    precise = lax.Precision.HIGHEST
    inputs = [
        (edge_coeffs_x, flips[0], open_map, closed_map, closed_map),
        (edge_coeffs_y, flips[1], closed_map, open_map, closed_map),
        (edge_coeffs_z, flips[2], closed_map, closed_map, open_map),
    ]
    length = nz + 4
    up_places = [nz, nz + 1, nz + 2]
    down_places = [2, 3]
    planars = []
    depths = []
    slabs = []
    for coef, flip, table_x, table_y, table_z in inputs:
        planar = planar_part(coef, flip, table_x, table_y, table_z.shape[1])
        depth_map = depth_map_of(table_z, coef.shape[4])
        edge_map = jnp.asarray(depth_map[up_places + down_places], jnp.float32)
        planars.append(planar)
        depths.append(depth_map)
        slabs.append(
            lax.dot_general(edge_map, planar, (((1,), (1,)), ((), ())), precision=lax.Precision.HIGH)
        )
    keep_layers = [
        lax.slice_in_dim(flags, nz - 2, nz, axis=2),
        jnp.ones_like(lax.slice_in_dim(flags, 0, 1, axis=2)),
        lax.slice_in_dim(flags, 0, 2, axis=2),
    ]
    keep_layers = (1 - jnp.moveaxis(jnp.concatenate(keep_layers, axis=2), 2, 0)).astype(jnp.float32)
    slabs.append(jnp.pad(keep_layers, ((0, 0), (0, 1), (2, 2))).reshape(5, -1))
    slabs = jnp.stack(slabs)
    up = slabs[:, :3].reshape(-1, slabs.shape[2])
    down = slabs[:, 3:].reshape(-1, slabs.shape[2])
    from_prev, from_next = both_ways(up, down, "gz")
    own_parts = lax.optimization_barrier(
        [
            jnp.dot(planar, jnp.asarray(depth.T, jnp.float32), precision=lax.Precision.HIGH)
            for planar, depth in zip(planars, depths)
        ]
    )
    arrived = jnp.concatenate(
        [from_prev.reshape(4, 3, -1), from_next.reshape(4, 2, -1)], axis=1
    )
    place = np.zeros((5, length))
    for row, col in enumerate([0, 1, 2, nz + 2, nz + 3]):
        place[row, col] = 1.0
    place = jnp.asarray(place, jnp.float32)
    nodal = []
    for comp in range(3):
        folded = lax.dot_general(arrived[comp], place, (((0,), (0,)), ((), ())), precision=lax.Precision.HIGH)
        nodal.append((own_parts[comp] + folded).reshape(nx + 1, ny + 4, length))
    keep = jnp.pad((1 - flags).astype(jnp.float32), ((0, 1), (2, 2), (2, 2)))
    keep_in = jnp.moveaxis(arrived[3].reshape(5, nx + 1, ny + 4), 0, 2)
    keep = keep + jnp.pad(keep_in[..., :3], ((0, 0), (0, 0), (0, length - 3))) + jnp.pad(
        keep_in[..., 3:], ((0, 0), (0, 0), (nz + 2, 0))
    )
    extended = jnp.stack(nodal + [keep])
    return plane_round_and_stencil(extended, nx, ny)


def solution(mesh):
    in_specs = (
        P("gx", None, "gy", None, "gz"),
        P("gx", None, "gy", None, "gz"),
        P("gx", None, "gy", None, "gz"),
        P(None, "gx", "gy", "gz"),
        P("gx", "gy", "gz"),
    )
    out_specs = P(None, "gx", "gy", "gz")
    return jax.shard_map(body, mesh=mesh, in_specs=in_specs, out_specs=out_specs, check_vma=False)
```
